32 devices in a mesh: ep: 16 (over z, y, x), tp: 2 (over core).
Axes of the slice: x: 2, y: 2, z: 4, core: 2. Of those that a mesh axis runs over, the one named last changes fastest.
Arguments:
- tokens: bfloat16 [2048, 1536], P('ep', 'tp'), may hold values from -0.29882812 to 0.29882812
- queries: bfloat16 [2048, 1536], P('ep')
- kv_cache: bfloat16 [16, 2, 96, 16, 512], P('ep', 'tp')
- page_table: int32 [64, 48], P('ep'), may hold values from 0 to 95, as said below
- query_lens: int32 [16, 4], P('ep'), may hold values from 1 to 80, 128 in all within a row
- past_lens: int32 [16, 4], P('ep'), may hold values from 0 to 688
- out_weight: bfloat16 [1536, 1536], P(None, 'tp')
- norm_gain: float32 [1536], P('tp'), may hold values from 0.1 to 1.9
- route_ids: int32 [2048, 4], P('ep'), may hold values from 0 to 7, all different within a row; in each aligned block of 128 rows (0 to 127, 128 to 255, ...) at most 128 rows name the same one
- route_weights: float32 [2048, 4], P('ep'), may hold values from 0.1 to 1
- gate_w: bfloat16 [16, 1536, 768], P('ep', None, 'tp'), as said below
- up_w: bfloat16 [16, 1536, 768], P('ep', None, 'tp'), as said below
- down_w: bfloat16 [16, 768, 1536], P('ep', 'tp'), as said below
- final_gain: float32 [1536], P('tp'), may hold values from 0.1 to 1.9
Outputs:
- normed_out: bfloat16 [2048, 1536], P('ep', 'tp')
The draws below stay inside these ranges and needn't reach their ends.
Inputs may be any that keep to these rules, and one draw needn't show every extreme that they name: `page_table`: for each group and each t below 2, the entries over the group's 4 requests and all j with j mod 2 = t are distinct. `query_lens`: the 4 requests of a group have 128 rows together; in every group one request has exactly 80. `route_ids`: each row names 4 different experts; in each aligned block of 128 rows no expert is named by more than 128 rows, a bound that some block reaches. `gate_w`: slot s and slot s + 8 hold the same weights, those of expert s. `up_w`: slot s and slot s + 8 hold the same weights, those of expert s. `down_w`: slot s and slot s + 8 hold the same weights, those of expert s.
All inputs are finite; a program needn't handle non-finite values.
Results may differ from the reference program's by a relative error of at most 0.025.
Values may be sent and summed in bfloat16 or wider, within the bound.
No kernel may reach another device: no remote copies, remote signals or barrier semaphores. Data moves between devices by JAX's collectives and lax.ppermute only.
A program may use at most 64 MiB of HBM per device.

```python
import math
import jax
import jax.numpy as jnp
import numpy as np
from jax import lax

D = 1536
QUERY_HEADS = 12
KEY_VALUE_HEADS = 2
HEAD_SIZE = 128
FF = 768
TOPK = 4
TOKEN_ROWS_LOCAL = 128
REQ_DEV = 4
PAGE_POSITIONS = 16
PPT = 24
E = 8
QW = 1536
CACHED_WIDTH = 512
MAXP = 48
PAGES_DEV = 96
QMAX = 80
PASTMAX = 688
MOST = 128
TOKENS = 2048
REQUESTS = 64
N_EP = 16
N_TP = 2


def feature_scales(key):
    rough = jax.random.uniform(jax.random.fold_in(key, 41), (D,), jnp.float32, 0.7, 1.4)
    ramp = jnp.arange(D, dtype=jnp.float32) / (D - 1) - 0.5
    spread = 1.386
    return jnp.exp(spread * ramp) * rough


def draw_queries(key, part):
    base = jax.random.normal(jax.random.fold_in(key, 21), (TOKENS, QUERY_HEADS * HEAD_SIZE), jnp.float32)
    return base.astype(jnp.bfloat16)


def draw_kv_cache(key, part):
    shape = (N_EP, N_TP, PAGES_DEV, PAGE_POSITIONS, CACHED_WIDTH)
    base = jax.random.normal(jax.random.fold_in(key, 22), shape, jnp.float32)
    return base.astype(jnp.bfloat16)


def draw_page_table(key, part):
    keys = jax.random.split(jax.random.fold_in(key, 31), N_EP * N_TP)
    perms = jax.vmap(lambda one: jax.random.permutation(one, PAGES_DEV))(keys).reshape(N_EP, N_TP, PAGES_DEV)
    request = jnp.arange(REQUESTS)
    group = request // REQ_DEV
    inner = request % REQ_DEV
    logical = jnp.arange(MAXP)
    device_t = logical % N_TP
    column = logical // N_TP
    return perms[group[:, None], device_t[None, :], inner[:, None] * PPT + column[None, :]].astype(jnp.int32)


def draw_past_lens(key, part):
    values = jax.random.randint(jax.random.fold_in(key, 32), (N_EP, REQ_DEV), 0, PASTMAX + 1)
    return values.at[0, 0].set(PASTMAX).astype(jnp.int32)


def draw_out_weight(key, part):
    single = jax.random.normal(jax.random.fold_in(key, 14), (QW, D), jnp.float32) * QW ** (-0.5)
    return (single * feature_scales(key)[None, :]).astype(jnp.bfloat16)


def expert_weights(key, salt, shape, fan_in):
    single = jax.random.normal(jax.random.fold_in(key, salt), shape, jnp.float32) * fan_in ** (-0.5)
    return jnp.concatenate([single, single], axis=0).astype(jnp.bfloat16)


def draw_gate_w(key, part):
    return expert_weights(key, 11, (E, D, FF), D)


def draw_up_w(key, part):
    return expert_weights(key, 12, (E, D, FF), D)


def draw_down_w(key, part):
    single = jax.random.normal(jax.random.fold_in(key, 13), (E, FF, D), jnp.float32) * FF ** (-0.5)
    single = single * feature_scales(key)[None, None, :]
    return jnp.concatenate([single, single], axis=0).astype(jnp.bfloat16)


def block_scale(stream_key, shape, cuts, least, high):
    loudness = 1.0
    for dim, shards_of in cuts:
        steps = jax.random.uniform(jax.random.fold_in(jax.random.fold_in(stream_key, 6), dim), (shards_of,), jnp.float32, least / len(cuts), high / len(cuts))
        loudness = loudness * jnp.repeat(jnp.exp(steps), shape[dim] // shards_of).reshape((-1,) + (1,) * (len(shape) - 1 - dim))
    return loudness


def length_profile(amount, total, bound, slope):
    weights = [(1 << 20) // math.isqrt(standing ** slope) + 1 for standing in range(2, amount + 1)]
    spare, counts = total - bound - (amount - 1), [1] * (amount - 1)
    while spare > 0:
        free = [i for i in range(amount - 1) if counts[i] < bound]
        pool, remaining = sum([weights[i] for i in free]), spare
        for i in free:
            more = min(bound - counts[i], max(1, remaining * weights[i] // pool), spare)
            counts[i] = counts[i] + more
            spare = spare - more
    return np.array([bound] + counts)


def ragged(rng, number_of, total, bound, lean):
    if number_of == 2:
        one = jax.random.randint(rng, (), max(1, total - bound), min(bound, total - 1) + 1)
        return jnp.stack([one, total - one])
    lengths = jnp.asarray(length_profile(number_of, total, bound, lean), jnp.int32)
    pairs = (number_of - 1) // 2
    giver, taker = lengths[1:1 + 2 * pairs:2], lengths[2:2 + 2 * pairs:2]
    slack = jnp.minimum(giver - 1, bound - taker)
    moved = jax.random.randint(jax.random.fold_in(rng, 1), (pairs,), 0, 1 << 20) % (slack + 1)
    lengths = lengths.at[1:1 + 2 * pairs:2].set(giver - moved).at[2:2 + 2 * pairs:2].set(taker + moved)
    return lengths[jax.random.permutation(jax.random.fold_in(rng, 2), number_of)]


def shared_out(key, own, number, rows, count, top, reach, skew):
    sequence = jax.random.permutation(key, count)
    crowded, common = load_shares(count, rows * top, reach, skew, True), load_shares(count, rows * top, reach, skew, False)
    places = jnp.arange(count)

    def named(lengths, turn):
        used = int((lengths > 0).sum())
        fixed = max(1, used // 4)
        shifted = fixed + (places - fixed + turn * (used - fixed)) % max(1, count - fixed)
        return jnp.zeros((count,), jnp.int32).at[sequence[jnp.where(places < fixed, places, shifted)]].set(jnp.asarray(lengths, jnp.int32))

    lengths = jnp.where(number % 4 == 0, named(crowded, number // 4), named(common, number - number // 4 - 1))
    mixed = jax.random.permutation(jax.random.fold_in(own, 3), count)
    source_of, taker = mixed[0:count // 2 * 2:2], mixed[1:count // 2 * 2:2]
    margin = jnp.minimum(lengths[source_of] - 1, reach - lengths[taker]) // 2
    margin = jnp.where((source_of == sequence[0]) | (taker == sequence[0]) | (lengths[taker] == 0), 0, jnp.maximum(margin, 0))
    shifted = jax.random.randint(jax.random.fold_in(own, 4), (count // 2,), 0, 1 << 20) % (margin + 1)
    lengths = lengths.at[source_of].add(-shifted).at[taker].add(shifted)
    members = jnp.searchsorted(jnp.cumsum(lengths), jnp.arange(rows * top), side="right").astype(jnp.int32)
    listing = members.reshape(top, rows).T
    listing = listing[jax.random.permutation(jax.random.fold_in(own, 1), rows)]
    turn = jax.random.randint(jax.random.fold_in(own, 2), (rows, 1), 0, top)
    return jnp.take_along_axis(listing, (jnp.arange(top)[None, :] + turn) % top, axis=1)


def load_shares(count, total, reach, skew, full):
    portions = [(1 << 20) // math.isqrt(standing ** skew) + 1 for standing in range(1, count + 1)]
    largest = reach if full else min(reach, max(-(-total // count), total * portions[0] // sum(portions)))
    least = 1 if total - largest >= count - 1 else 0
    given, rest = [largest] + [least] * (count - 1), total - largest - least * (count - 1)
    while rest > 0:
        candidates = [i for i in range(1, count) if given[i] < largest] or [i for i in range(1, count) if given[i] < reach]
        whole, left = sum([portions[i] for i in candidates]), rest
        for i in candidates:
            more = min(reach - given[i], max(1, left * portions[i] // whole), rest)
            given[i] = given[i] + more
            rest = rest - more
    return np.array(given)


def scatter_about(rng, shape, width, limit, cuts=(), kind=jnp.bfloat16):
    drawn = width * jax.random.normal(rng, shape, jnp.float32)
    if cuts:
        drawn = drawn * block_scale(rng, shape, cuts, -0.22, 0.18)
    return jnp.clip(drawn, -limit, limit).astype(kind)


def setup_inputs(seed: int = 0) -> dict:
    splits = jax.random.split(jax.random.key(seed), 15)
    tokens = scatter_about(splits[0], (TOKENS, D), 0.05, 0.29882812, ((0, 16), (1, 2)))
    queries = draw_queries(jax.random.fold_in(splits[14], 71), 0)
    kv_cache = draw_kv_cache(jax.random.fold_in(splits[14], 71), 0)
    page_table = draw_page_table(jax.random.fold_in(splits[14], 71), 0)
    query_lens = jax.vmap(lambda own: ragged(own, REQ_DEV, TOKEN_ROWS_LOCAL, QMAX, 2))(jax.random.split(splits[4], N_EP)).reshape((N_EP, REQ_DEV)).astype(jnp.int32)
    past_lens = draw_past_lens(jax.random.fold_in(splits[14], 71), 0)
    out_weight = draw_out_weight(jax.random.fold_in(splits[14], 71), 0)
    norm_gain = jnp.clip(1.0 + 0.18 * jax.random.normal(splits[7], (D,), jnp.float32), 0.1, 1.9)
    route_ids_keys = jax.random.split(jax.random.fold_in(splits[8], 1), TOKENS // TOKEN_ROWS_LOCAL)
    route_ids_turns = jax.random.permutation(jax.random.fold_in(splits[8], 3), TOKENS // TOKEN_ROWS_LOCAL)
    route_ids = jax.vmap(lambda own, number: shared_out(jax.random.fold_in(splits[8], 2), own, number, TOKEN_ROWS_LOCAL, E, TOPK, MOST, 2))(route_ids_keys, route_ids_turns).reshape((TOKENS, TOPK))
    route_weights = jnp.clip(jnp.exp(math.log(1.0) - 2.3025851 * jax.random.uniform(splits[9], (TOKENS, TOPK), jnp.float32) ** block_scale(splits[9], (TOKENS, TOPK), ((0, 16),), -0.2, 0.2)), 0.1, 1.0)
    gate_w = draw_gate_w(jax.random.fold_in(splits[14], 71), 0)
    up_w = draw_up_w(jax.random.fold_in(splits[14], 71), 0)
    down_w = draw_down_w(jax.random.fold_in(splits[14], 71), 0)
    final_gain = jnp.clip(1.0 + 0.18 * jax.random.normal(splits[13], (D,), jnp.float32), 0.1, 1.9)
    return dict(tokens=tokens, queries=queries, kv_cache=kv_cache, page_table=page_table, query_lens=query_lens, past_lens=past_lens, out_weight=out_weight, norm_gain=norm_gain, route_ids=route_ids, route_weights=route_weights, gate_w=gate_w, up_w=up_w, down_w=down_w, final_gain=final_gain)


EPSILON = 1e-06

def group_attention(group, queries, kv_cache, page_table, query_lens, past_lens):
    query_count = query_lens[group]
    past_count = past_lens[group]
    row_ends = jnp.cumsum(query_count)
    row_starts = row_ends - query_count
    row_iota = jnp.arange(TOKEN_ROWS_LOCAL, dtype=jnp.int32)
    row_req = lax.optimization_barrier(jnp.sum((row_iota[:, None] >= row_ends[None, :]).astype(jnp.int32), axis=1))
    row_pos = row_iota - row_starts[row_req] + past_count[row_req]
    table_rows = lax.dynamic_slice_in_dim(page_table, (group * REQ_DEV).astype(jnp.int32), REQ_DEV, 0)
    logical = jnp.arange(MAXP, dtype=jnp.int32)
    owner = logical % N_TP
    group_pages = kv_cache[group]
    key_count_total = REQ_DEV * MAXP * PAGE_POSITIONS
    page_row_block = group_pages[owner[None, :], table_rows].reshape(key_count_total, CACHED_WIDTH)
    key_iota = jnp.arange(key_count_total, dtype=jnp.int32)
    key_req = key_iota // (MAXP * PAGE_POSITIONS)
    key_pos = key_iota % (MAXP * PAGE_POSITIONS)
    allowed = (row_req[:, None] == key_req[None, :]) & (key_pos[None, :] <= row_pos[:, None])
    gathered_keys = page_row_block[:, :KEY_VALUE_HEADS * HEAD_SIZE].reshape(key_count_total, KEY_VALUE_HEADS, HEAD_SIZE).astype(jnp.float32)
    gathered_values = page_row_block[:, KEY_VALUE_HEADS * HEAD_SIZE:].reshape(key_count_total, KEY_VALUE_HEADS, HEAD_SIZE).astype(jnp.float32)
    query_row_block = lax.dynamic_slice_in_dim(queries, (group * TOKEN_ROWS_LOCAL).astype(jnp.int32), TOKEN_ROWS_LOCAL, 0)
    query_head_rows = query_row_block.reshape(TOKEN_ROWS_LOCAL, KEY_VALUE_HEADS, QUERY_HEADS // KEY_VALUE_HEADS, HEAD_SIZE).astype(jnp.float32)
    scores = jnp.einsum('rkgd,lkd->rkgl', query_head_rows, gathered_keys) * HEAD_SIZE ** (-0.5)
    score_mask = allowed[:, None, None, :]
    row_max = lax.optimization_barrier(jnp.max(jnp.where(score_mask, scores, -1e+30), axis=-1))
    soft = jnp.where(score_mask, jnp.exp(scores - row_max[..., None]), 0.0)
    row_sum = lax.optimization_barrier(jnp.sum(soft, axis=-1))
    soft_round = lax.optimization_barrier(soft.astype(jnp.bfloat16))
    weighted = jnp.einsum('rkgl,lkd->rkgd', soft_round.astype(jnp.float32), gathered_values)
    return (weighted / row_sum[..., None]).reshape(TOKEN_ROWS_LOCAL, QUERY_HEADS * HEAD_SIZE).astype(jnp.bfloat16)

def reference(tokens, queries, kv_cache, page_table, query_lens, past_lens, out_weight, norm_gain, route_ids, route_weights, gate_w, up_w, down_w, final_gain):
    attended = lax.map(lambda group: group_attention(group, queries, kv_cache, page_table, query_lens, past_lens), jnp.arange(N_EP, dtype=jnp.int32))
    attended = attended.reshape(TOKENS, QUERY_HEADS * HEAD_SIZE)
    resid = tokens.astype(jnp.float32) + jnp.dot(attended, out_weight, preferred_element_type=jnp.float32)
    mid_scale = lax.rsqrt(lax.optimization_barrier(jnp.mean(resid * resid, axis=1)) + EPSILON)
    normed = (resid * mid_scale[:, None] * norm_gain).astype(jnp.bfloat16)
    flat_ids = route_ids.reshape(-1)
    assign_count = TOKENS * TOPK
    order = jnp.argsort(flat_ids, stable=True).astype(jnp.int32)
    expert_load = lax.optimization_barrier(jnp.sum((flat_ids[:, None] == jnp.arange(E, dtype=jnp.int32)[None, :]).astype(jnp.int32), axis=0))
    expert_start = (jnp.cumsum(expert_load) - expert_load).astype(jnp.int32)
    group_size = N_EP * MOST
    order_pad = jnp.concatenate([order, jnp.zeros((group_size,), jnp.int32)])
    block_width = FF // N_TP

    def expert_step(expert, results):
        picked = lax.dynamic_slice_in_dim(order_pad, expert_start[expert], group_size)
        live = jnp.arange(group_size, dtype=jnp.int32) < expert_load[expert]
        inputs = normed[picked // TOPK]
        gate_val = jnp.dot(inputs, gate_w[expert], preferred_element_type=jnp.float32)
        up_val = jnp.dot(inputs, up_w[expert], preferred_element_type=jnp.float32)
        hidden = (jnp.maximum(gate_val, 0.0) * up_val).astype(jnp.bfloat16)
        blocks = jnp.einsum('nbf,bfd->nbd', hidden.reshape(group_size, N_TP, block_width).astype(jnp.float32), down_w[expert].reshape(N_TP, block_width, D).astype(jnp.float32))
        blocks = lax.optimization_barrier(blocks.astype(jnp.bfloat16))
        expert_out = lax.optimization_barrier(jnp.sum(blocks.astype(jnp.float32), axis=1))
        target = jnp.where(live, picked, assign_count)
        return results.at[target].set(expert_out, mode='drop')
    results = lax.fori_loop(0, E, expert_step, jnp.zeros((assign_count, D), jnp.float32))
    branch = lax.optimization_barrier(jnp.sum(route_weights[:, :, None] * results.reshape(TOKENS, TOPK, D), axis=1))
    mixed = resid + branch
    out_scale = lax.rsqrt(lax.optimization_barrier(jnp.mean(mixed * mixed, axis=1)) + EPSILON)
    return (mixed * out_scale[:, None] * final_gain).astype(jnp.bfloat16)
```

```python
import jax
import jax.numpy as jnp
from jax import lax
from jax.sharding import Mesh, NamedSharding, PartitionSpec as P

QUERY_HEADS = 12
KEY_VALUE_HEADS = 2
HEAD_SIZE = 128
PAGE_POSITIONS = 16


EPSILON = 1e-06


def merged(shard, axis, join):
    gathered = jax.tree.map(
        lambda a, kind: lax.all_gather(a.astype(kind), axis),
        shard,
        (jnp.bfloat16, jnp.bfloat16, jnp.bfloat16),
    )

    def take(source):
        return jax.tree.map(
            lambda a, own: lax.dynamic_index_in_dim(a, source, 0, False).astype(own.dtype),
            gathered,
            shard,
        )

    return lax.fori_loop(
        1, lax.axis_size(axis), lambda source, state: join(state, take(source)), take(0)
    )


def merge_parts(first, second):
    joint_max = jnp.maximum(first[0], second[0])
    scale_first = jnp.exp(first[0] - joint_max)
    scale_second = jnp.exp(second[0] - joint_max)
    return (
        joint_max,
        first[1] * scale_first + second[1] * scale_second,
        first[2] * scale_first[..., None] + second[2] * scale_second[..., None],
    )


def shards(
    tokens,
    queries,
    kv_cache,
    page_table,
    query_lens,
    past_lens,
    out_weight,
    norm_gain,
    route_ids,
    route_weights,
    gate_w,
    up_w,
    down_w,
    final_gain,
):
    tp_index = lax.axis_index("tp")
    tp_count = lax.axis_size("tp")
    count_of_rows, feat_part = tokens.shape
    full_width = feat_part * tp_count
    local_groups = query_lens.shape[0]
    req_count = query_lens.shape[1]
    group_rows = count_of_rows // local_groups
    head_groups = QUERY_HEADS // KEY_VALUE_HEADS
    per_device = page_table.shape[1] // tp_count

    def one_group(local):
        query_count = lax.dynamic_index_in_dim(query_lens, local, 0, keepdims=False)
        past_count = lax.dynamic_index_in_dim(past_lens, local, 0, keepdims=False)
        row_ends = jnp.cumsum(query_count)
        row_starts = row_ends - query_count
        row_iota = jnp.arange(group_rows, dtype=jnp.int32)
        row_req = jnp.sum((row_iota[:, None] >= row_ends[None, :]).astype(jnp.int32), axis=1)
        req_onehot = (row_req[:, None] == jnp.arange(req_count, dtype=jnp.int32)[None, :]).astype(
            jnp.int32
        )
        row_pos = row_iota + jnp.sum(req_onehot * (past_count - row_starts)[None, :], axis=1)
        local_table = lax.dynamic_index_in_dim(
            page_table.reshape(req_count, per_device, tp_count), tp_index, axis=2, keepdims=False
        )
        group_pages = lax.dynamic_index_in_dim(kv_cache, local, 0, keepdims=False)[0]
        page_row_block = group_pages[local_table.reshape(-1)]
        key_count_total = page_row_block.shape[0] * PAGE_POSITIONS
        flattened_cache = page_row_block.reshape(key_count_total, 2 * KEY_VALUE_HEADS * HEAD_SIZE)
        gathered_keys = flattened_cache[:, : KEY_VALUE_HEADS * HEAD_SIZE].reshape(
            key_count_total, KEY_VALUE_HEADS, HEAD_SIZE
        )
        gathered_values = flattened_cache[:, KEY_VALUE_HEADS * HEAD_SIZE :].reshape(
            key_count_total, KEY_VALUE_HEADS, HEAD_SIZE
        )
        key_iota = jnp.arange(key_count_total, dtype=jnp.int32)
        key_req = key_iota // (per_device * PAGE_POSITIONS)
        within = key_iota % (per_device * PAGE_POSITIONS)
        key_pos = (
            within // PAGE_POSITIONS * tp_count + tp_index
        ) * PAGE_POSITIONS + within % PAGE_POSITIONS
        allowed = (row_req[:, None] == key_req[None, :]) & (key_pos[None, :] <= row_pos[:, None])
        query_head_rows = queries.reshape(group_rows, KEY_VALUE_HEADS, head_groups, HEAD_SIZE)
        scores = jnp.einsum(
            "rkgd,lkd->rkgl", query_head_rows, gathered_keys, preferred_element_type=jnp.float32
        ) * HEAD_SIZE ** (-0.5)
        score_mask = allowed[:, None, None, :]
        part_max = jnp.max(jnp.where(score_mask, scores, -1e30), axis=-1)
        soft = jnp.where(score_mask, jnp.exp(scores - part_max[..., None]), 0.0)
        part_sum = jnp.sum(soft, axis=-1)
        part_weighted = jnp.einsum(
            "rkgl,lkd->rkgd",
            soft.astype(jnp.bfloat16),
            gathered_values,
            preferred_element_type=jnp.float32,
        )
        return (part_max, part_sum, part_weighted)

    row_max, row_sum, weighted = lax.map(one_group, jnp.arange(local_groups, dtype=jnp.int32))
    row_max = row_max.reshape(count_of_rows, KEY_VALUE_HEADS, head_groups)
    row_sum = row_sum.reshape(count_of_rows, KEY_VALUE_HEADS, head_groups)
    weighted = weighted.reshape(count_of_rows, KEY_VALUE_HEADS, head_groups, HEAD_SIZE)
    row_max, row_sum, weighted = merged((row_max, row_sum, weighted), "tp", merge_parts)
    attended = (
        (weighted / row_sum[..., None])
        .reshape(count_of_rows, QUERY_HEADS * HEAD_SIZE)
        .astype(jnp.bfloat16)
    )
    resid = tokens.astype(jnp.float32) + jnp.dot(
        attended, out_weight, preferred_element_type=jnp.float32
    )
    mid_squares = lax.psum(jnp.sum(resid * resid, axis=1), "tp")
    normed = (resid * lax.rsqrt(mid_squares / full_width + EPSILON)[:, None] * norm_gain).astype(
        jnp.bfloat16
    )
    top_count = route_ids.shape[1]
    half_count = lax.axis_size("el")
    experts = half_count
    capacity = count_of_rows * top_count * 2 // experts
    buffer_len = experts * capacity
    flat_ids = route_ids.reshape(-1)
    expert_onehot = (flat_ids[:, None] == jnp.arange(experts, dtype=jnp.int32)[None, :]).astype(
        jnp.int32
    )
    expert_rank = jnp.sum(
        (jnp.cumsum(expert_onehot, axis=0) - expert_onehot) * expert_onehot, axis=1
    )
    target = (flat_ids * capacity + expert_rank).reshape(count_of_rows, top_count)
    slot_iota = jnp.arange(buffer_len, dtype=jnp.int32)
    hits = target[None, :, :] == slot_iota[:, None, None]
    dispatch = jnp.any(hits, axis=2).astype(jnp.bfloat16)
    outgoing = jnp.dot(dispatch, normed, preferred_element_type=jnp.float32).astype(jnp.bfloat16)
    arrived = lax.all_to_all(
        outgoing.reshape(experts, capacity, feat_part),
        "el",
        split_axis=0,
        concat_axis=0,
        tiled=True,
    )
    inputs = lax.all_gather(arrived, "tp", axis=2, tiled=True).reshape(buffer_len, full_width)
    gate_value = jnp.dot(inputs, gate_w[0], preferred_element_type=jnp.float32)
    up_value = jnp.dot(inputs, up_w[0], preferred_element_type=jnp.float32)
    hidden = (jnp.maximum(gate_value, 0.0) * up_value).astype(jnp.bfloat16)
    partial_value = jnp.dot(hidden, down_w[0], preferred_element_type=jnp.float32).astype(
        jnp.bfloat16
    )
    summed = lax.psum_scatter(partial_value, "tp", scatter_dimension=1, tiled=True)
    returned = lax.all_to_all(
        summed.reshape(experts, capacity, feat_part),
        "el",
        split_axis=0,
        concat_axis=0,
        tiled=True,
    ).reshape(buffer_len, feat_part)
    combine = jnp.sum(
        jnp.where(
            target[:, :, None] == slot_iota[None, None, :],
            route_weights[:, :, None],
            0.0,
        ),
        axis=1,
    )
    branch = jnp.dot(
        combine,
        returned.astype(jnp.float32),
        precision=lax.Precision.HIGHEST,
        preferred_element_type=jnp.float32,
    )
    mixed_rows = resid + branch
    out_squares = lax.psum(jnp.sum(mixed_rows * mixed_rows, axis=1), "tp")
    return (
        mixed_rows * lax.rsqrt(out_squares / full_width + EPSILON)[:, None] * final_gain
    ).astype(jnp.bfloat16)


def solution(mesh):
    ep_count, tp_count = mesh.devices.shape
    halves = Mesh(mesh.devices.reshape(2, ep_count // 2, tp_count), ("eh", "el", "tp"))
    ep = ("eh", "el")
    placed = (
        P(ep, "tp"),
        P(ep, None),
        P(ep, "tp", None, None, None),
        P(ep, None),
        P(ep, None),
        P(ep, None),
        P(None, "tp"),
        P("tp"),
        P(ep, None),
        P(ep, None),
        P(ep, None, "tp"),
        P(ep, None, "tp"),
        P(ep, "tp", None),
        P("tp"),
    )
    inner = jax.shard_map(
        shards, mesh=halves, in_specs=placed, out_specs=P(ep, "tp"), check_vma=False
    )
    result_sharding = NamedSharding(mesh, P("ep", "tp"))

    def run(*args):
        return lax.with_sharding_constraint(inner(*args), result_sharding)

    return run
```

```python
import jax
import jax.numpy as jnp
from jax import lax
from jax.sharding import Mesh, NamedSharding, PartitionSpec as P

QUERY_HEADS = 12
KEY_VALUE_HEADS = 2
HEAD_SIZE = 128
PAGE_POSITIONS = 16


EPSILON = 1e-06


def merged(shard, axis, join):
    gathered = jax.tree.map(
        lambda a, kind: lax.all_gather(a.astype(kind), axis),
        shard,
        (jnp.bfloat16, jnp.bfloat16, jnp.bfloat16),
    )

    def take(source):
        return jax.tree.map(
            lambda a, own: lax.dynamic_index_in_dim(a, source, 0, False).astype(own.dtype),
            gathered,
            shard,
        )

    return lax.fori_loop(
        1, lax.axis_size(axis), lambda source, state: join(state, take(source)), take(0)
    )


def tp_gather(part, axis):
    if lax.axis_size("tp") != 2:
        return lax.all_gather(part, "tp", axis=axis, tiled=True)
    other = lax.ppermute(part, "tp", perm=[(0, 1), (1, 0)])
    first = lax.axis_index("tp") == 0
    low = jnp.where(first, part, other)
    high = jnp.where(first, other, part)
    return jnp.concatenate([low, high], axis=axis)


def tp_scatter_sum(full, axis):
    if lax.axis_size("tp") != 2:
        return lax.psum_scatter(full, "tp", scatter_dimension=axis, tiled=True)
    low, high = jnp.split(full, 2, axis=axis)
    first = lax.axis_index("tp") == 0
    keep = jnp.where(first, low, high)
    send = jnp.where(first, high, low)
    other = lax.ppermute(send, "tp", perm=[(0, 1), (1, 0)])
    return (keep.astype(jnp.float32) + other.astype(jnp.float32)).astype(full.dtype)


def merge_parts(first, second):
    joint_max = jnp.maximum(first[0], second[0])
    scale_first = jnp.exp(first[0] - joint_max)
    scale_second = jnp.exp(second[0] - joint_max)
    return (
        joint_max,
        first[1] * scale_first + second[1] * scale_second,
        first[2] * scale_first[..., None] + second[2] * scale_second[..., None],
    )


def shards(
    tokens,
    queries,
    kv_cache,
    page_table,
    query_lens,
    past_lens,
    out_weight,
    norm_gain,
    route_ids,
    route_weights,
    gate_w,
    up_w,
    down_w,
    final_gain,
):
    tp_index = lax.axis_index("tp")
    tp_count = lax.axis_size("tp")
    count_of_rows, feat_part = tokens.shape
    full_width = feat_part * tp_count
    local_groups = query_lens.shape[0]
    req_count = query_lens.shape[1]
    group_rows = count_of_rows // local_groups
    head_groups = QUERY_HEADS // KEY_VALUE_HEADS
    per_device = page_table.shape[1] // tp_count

    def one_group(local):
        query_count = lax.dynamic_index_in_dim(query_lens, local, 0, keepdims=False)
        past_count = lax.dynamic_index_in_dim(past_lens, local, 0, keepdims=False)
        row_ends = jnp.cumsum(query_count)
        row_starts = row_ends - query_count
        row_iota = jnp.arange(group_rows, dtype=jnp.int32)
        row_req = jnp.sum((row_iota[:, None] >= row_ends[None, :]).astype(jnp.int32), axis=1)
        req_onehot = (row_req[:, None] == jnp.arange(req_count, dtype=jnp.int32)[None, :]).astype(
            jnp.int32
        )
        row_pos = row_iota + jnp.sum(req_onehot * (past_count - row_starts)[None, :], axis=1)
        local_table = lax.dynamic_index_in_dim(
            page_table.reshape(req_count, per_device, tp_count), tp_index, axis=2, keepdims=False
        )
        group_pages = lax.dynamic_index_in_dim(kv_cache, local, 0, keepdims=False)[0]
        page_row_block = group_pages[local_table.reshape(-1)]
        key_count_total = page_row_block.shape[0] * PAGE_POSITIONS
        flattened_cache = page_row_block.reshape(key_count_total, 2 * KEY_VALUE_HEADS * HEAD_SIZE)
        gathered_keys = flattened_cache[:, : KEY_VALUE_HEADS * HEAD_SIZE].reshape(
            key_count_total, KEY_VALUE_HEADS, HEAD_SIZE
        )
        gathered_values = flattened_cache[:, KEY_VALUE_HEADS * HEAD_SIZE :].reshape(
            key_count_total, KEY_VALUE_HEADS, HEAD_SIZE
        )
        key_iota = jnp.arange(key_count_total, dtype=jnp.int32)
        key_req = key_iota // (per_device * PAGE_POSITIONS)
        within = key_iota % (per_device * PAGE_POSITIONS)
        key_pos = (
            within // PAGE_POSITIONS * tp_count + tp_index
        ) * PAGE_POSITIONS + within % PAGE_POSITIONS
        allowed = (row_req[:, None] == key_req[None, :]) & (key_pos[None, :] <= row_pos[:, None])
        query_head_rows = queries.reshape(group_rows, KEY_VALUE_HEADS, head_groups, HEAD_SIZE)
        scores = jnp.einsum(
            "rkgd,lkd->rkgl", query_head_rows, gathered_keys, preferred_element_type=jnp.float32
        ) * HEAD_SIZE ** (-0.5)
        score_mask = allowed[:, None, None, :]
        part_max = jnp.max(jnp.where(score_mask, scores, -1e30), axis=-1)
        soft = jnp.where(score_mask, jnp.exp(scores - part_max[..., None]), 0.0)
        part_sum = jnp.sum(soft, axis=-1)
        part_weighted = jnp.einsum(
            "rkgl,lkd->rkgd",
            soft.astype(jnp.bfloat16),
            gathered_values,
            preferred_element_type=jnp.float32,
        )
        return (part_max, part_sum, part_weighted)

    row_max, row_sum, weighted = lax.map(one_group, jnp.arange(local_groups, dtype=jnp.int32))
    row_max = row_max.reshape(count_of_rows, KEY_VALUE_HEADS, head_groups)
    row_sum = row_sum.reshape(count_of_rows, KEY_VALUE_HEADS, head_groups)
    weighted = weighted.reshape(count_of_rows, KEY_VALUE_HEADS, head_groups, HEAD_SIZE)
    row_max, row_sum, weighted = merged((row_max, row_sum, weighted), "tp", merge_parts)
    attended = (
        (weighted / row_sum[..., None])
        .reshape(count_of_rows, QUERY_HEADS * HEAD_SIZE)
        .astype(jnp.bfloat16)
    )
    resid = tokens.astype(jnp.float32) + jnp.dot(
        attended, out_weight, preferred_element_type=jnp.float32
    )
    mid_squares = lax.psum(jnp.sum(resid * resid, axis=1), "tp")
    normed = (resid * lax.rsqrt(mid_squares / full_width + EPSILON)[:, None] * norm_gain).astype(
        jnp.bfloat16
    )
    top_count = route_ids.shape[1]
    half_count = lax.axis_size("el")
    experts = half_count
    capacity = count_of_rows * top_count * 2 // experts
    buffer_len = experts * capacity
    flat_ids = route_ids.reshape(-1)
    expert_onehot = (flat_ids[:, None] == jnp.arange(experts, dtype=jnp.int32)[None, :]).astype(
        jnp.int32
    )
    expert_rank = jnp.sum(
        (jnp.cumsum(expert_onehot, axis=0) - expert_onehot) * expert_onehot, axis=1
    )
    target = (flat_ids * capacity + expert_rank).reshape(count_of_rows, top_count)
    slot_iota = jnp.arange(buffer_len, dtype=jnp.int32)
    hits = target[None, :, :] == slot_iota[:, None, None]
    dispatch = jnp.any(hits, axis=2).astype(jnp.bfloat16)
    outgoing = jnp.dot(dispatch, normed, preferred_element_type=jnp.float32).astype(jnp.bfloat16)
    arrived = lax.all_to_all(
        outgoing.reshape(experts, capacity, feat_part),
        "el",
        split_axis=0,
        concat_axis=0,
        tiled=True,
    )
    inputs = tp_gather(arrived, 2).reshape(buffer_len, full_width)
    gate_value = jnp.dot(inputs, gate_w[0], preferred_element_type=jnp.float32)
    up_value = jnp.dot(inputs, up_w[0], preferred_element_type=jnp.float32)
    hidden = (jnp.maximum(gate_value, 0.0) * up_value).astype(jnp.bfloat16)
    partial_value = jnp.dot(hidden, down_w[0], preferred_element_type=jnp.float32).astype(
        jnp.bfloat16
    )
    summed = tp_scatter_sum(partial_value, 1)
    returned = lax.all_to_all(
        summed.reshape(experts, capacity, feat_part),
        "el",
        split_axis=0,
        concat_axis=0,
        tiled=True,
    ).reshape(buffer_len, feat_part)
    combine = jnp.sum(
        jnp.where(
            target[:, :, None] == slot_iota[None, None, :],
            route_weights[:, :, None],
            0.0,
        ),
        axis=1,
    )
    branch = jnp.dot(
        combine,
        returned.astype(jnp.float32),
        precision=lax.Precision.HIGHEST,
        preferred_element_type=jnp.float32,
    )
    mixed_rows = resid + branch
    out_squares = lax.psum(jnp.sum(mixed_rows * mixed_rows, axis=1), "tp")
    return (
        mixed_rows * lax.rsqrt(out_squares / full_width + EPSILON)[:, None] * final_gain
    ).astype(jnp.bfloat16)


def solution(mesh):
    ep_count, tp_count = mesh.devices.shape
    halves = Mesh(mesh.devices.reshape(2, ep_count // 2, tp_count), ("eh", "el", "tp"))
    ep = ("eh", "el")
    placed = (
        P(ep, "tp"),
        P(ep, None),
        P(ep, "tp", None, None, None),
        P(ep, None),
        P(ep, None),
        P(ep, None),
        P(None, "tp"),
        P("tp"),
        P(ep, None),
        P(ep, None),
        P(ep, None, "tp"),
        P(ep, None, "tp"),
        P(ep, "tp", None),
        P("tp"),
    )
    inner = jax.shard_map(
        shards, mesh=halves, in_specs=placed, out_specs=P(ep, "tp"), check_vma=False
    )
    result_sharding = NamedSharding(mesh, P("ep", "tp"))

    def run(*args):
        return lax.with_sharding_constraint(inner(*args), result_sharding)

    return run
```

```python
import jax
import jax.numpy as jnp
from jax import lax
from jax.sharding import Mesh, NamedSharding, PartitionSpec as P

QUERY_HEADS = 12
KEY_VALUE_HEADS = 2
HEAD_SIZE = 128
PAGE_POSITIONS = 16


EPSILON = 1e-06


def merged(shard, axis, join):
    gathered = jax.tree.map(
        lambda a, kind: lax.all_gather(a.astype(kind), axis),
        shard,
        (jnp.bfloat16, jnp.bfloat16, jnp.bfloat16),
    )

    def take(source):
        return jax.tree.map(
            lambda a, own: lax.dynamic_index_in_dim(a, source, 0, False).astype(own.dtype),
            gathered,
            shard,
        )

    return lax.fori_loop(
        1, lax.axis_size(axis), lambda source, state: join(state, take(source)), take(0)
    )


def relative(expert, me, count):
    if count & (count - 1) == 0:
        return jnp.bitwise_xor(expert, me)
    return (expert - me) % count


def exchange(chunks, count):
    pieces = [chunks[0]]
    for step in range(1, count):
        if count & (count - 1) == 0:
            pairs = [(i, i ^ step) for i in range(count)]
        else:
            pairs = [(i, (i + step) % count) for i in range(count)]
        pieces.append(lax.ppermute(chunks[step], "el", perm=pairs))
    return jnp.stack(pieces)


def tp_gather(part, axis):
    if lax.axis_size("tp") != 2:
        return lax.all_gather(part, "tp", axis=axis, tiled=True)
    other = lax.ppermute(part, "tp", perm=[(0, 1), (1, 0)])
    first = lax.axis_index("tp") == 0
    low = jnp.where(first, part, other)
    high = jnp.where(first, other, part)
    return jnp.concatenate([low, high], axis=axis)


def tp_scatter_sum(full, axis):
    if lax.axis_size("tp") != 2:
        return lax.psum_scatter(full, "tp", scatter_dimension=axis, tiled=True)
    low, high = jnp.split(full, 2, axis=axis)
    first = lax.axis_index("tp") == 0
    keep = jnp.where(first, low, high)
    send = jnp.where(first, high, low)
    other = lax.ppermute(send, "tp", perm=[(0, 1), (1, 0)])
    return (keep.astype(jnp.float32) + other.astype(jnp.float32)).astype(full.dtype)


def merge_parts(first, second):
    joint_max = jnp.maximum(first[0], second[0])
    scale_first = jnp.exp(first[0] - joint_max)
    scale_second = jnp.exp(second[0] - joint_max)
    return (
        joint_max,
        first[1] * scale_first + second[1] * scale_second,
        first[2] * scale_first[..., None] + second[2] * scale_second[..., None],
    )


def shards(
    tokens,
    queries,
    kv_cache,
    page_table,
    query_lens,
    past_lens,
    out_weight,
    norm_gain,
    route_ids,
    route_weights,
    gate_w,
    up_w,
    down_w,
    final_gain,
):
    tp_index = lax.axis_index("tp")
    tp_count = lax.axis_size("tp")
    count_of_rows, feat_part = tokens.shape
    full_width = feat_part * tp_count
    local_groups = query_lens.shape[0]
    req_count = query_lens.shape[1]
    group_rows = count_of_rows // local_groups
    head_groups = QUERY_HEADS // KEY_VALUE_HEADS
    per_device = page_table.shape[1] // tp_count

    def one_group(local):
        query_count = lax.dynamic_index_in_dim(query_lens, local, 0, keepdims=False)
        past_count = lax.dynamic_index_in_dim(past_lens, local, 0, keepdims=False)
        row_ends = jnp.cumsum(query_count)
        row_starts = row_ends - query_count
        row_iota = jnp.arange(group_rows, dtype=jnp.int32)
        row_req = jnp.sum((row_iota[:, None] >= row_ends[None, :]).astype(jnp.int32), axis=1)
        req_onehot = (row_req[:, None] == jnp.arange(req_count, dtype=jnp.int32)[None, :]).astype(
            jnp.int32
        )
        row_pos = row_iota + jnp.sum(req_onehot * (past_count - row_starts)[None, :], axis=1)
        local_table = lax.dynamic_index_in_dim(
            page_table.reshape(req_count, per_device, tp_count), tp_index, axis=2, keepdims=False
        )
        group_pages = lax.dynamic_index_in_dim(kv_cache, local, 0, keepdims=False)[0]
        page_row_block = group_pages[local_table.reshape(-1)]
        key_count_total = page_row_block.shape[0] * PAGE_POSITIONS
        flattened_cache = page_row_block.reshape(key_count_total, 2 * KEY_VALUE_HEADS * HEAD_SIZE)
        gathered_keys = flattened_cache[:, : KEY_VALUE_HEADS * HEAD_SIZE].reshape(
            key_count_total, KEY_VALUE_HEADS, HEAD_SIZE
        )
        gathered_values = flattened_cache[:, KEY_VALUE_HEADS * HEAD_SIZE :].reshape(
            key_count_total, KEY_VALUE_HEADS, HEAD_SIZE
        )
        key_iota = jnp.arange(key_count_total, dtype=jnp.int32)
        key_req = key_iota // (per_device * PAGE_POSITIONS)
        within = key_iota % (per_device * PAGE_POSITIONS)
        key_pos = (
            within // PAGE_POSITIONS * tp_count + tp_index
        ) * PAGE_POSITIONS + within % PAGE_POSITIONS
        allowed = (row_req[:, None] == key_req[None, :]) & (key_pos[None, :] <= row_pos[:, None])
        query_head_rows = queries.reshape(group_rows, KEY_VALUE_HEADS, head_groups, HEAD_SIZE)
        scores = jnp.einsum(
            "rkgd,lkd->rkgl", query_head_rows, gathered_keys, preferred_element_type=jnp.float32
        ) * HEAD_SIZE ** (-0.5)
        score_mask = allowed[:, None, None, :]
        part_max = jnp.max(jnp.where(score_mask, scores, -1e30), axis=-1)
        soft = jnp.where(score_mask, jnp.exp(scores - part_max[..., None]), 0.0)
        part_sum = jnp.sum(soft, axis=-1)
        part_weighted = jnp.einsum(
            "rkgl,lkd->rkgd",
            soft.astype(jnp.bfloat16),
            gathered_values,
            preferred_element_type=jnp.float32,
        )
        return (part_max, part_sum, part_weighted)

    row_max, row_sum, weighted = lax.map(one_group, jnp.arange(local_groups, dtype=jnp.int32))
    row_max = row_max.reshape(count_of_rows, KEY_VALUE_HEADS, head_groups)
    row_sum = row_sum.reshape(count_of_rows, KEY_VALUE_HEADS, head_groups)
    weighted = weighted.reshape(count_of_rows, KEY_VALUE_HEADS, head_groups, HEAD_SIZE)
    row_max, row_sum, weighted = merged((row_max, row_sum, weighted), "tp", merge_parts)
    attended = (
        (weighted / row_sum[..., None])
        .reshape(count_of_rows, QUERY_HEADS * HEAD_SIZE)
        .astype(jnp.bfloat16)
    )
    resid = tokens.astype(jnp.float32) + jnp.dot(
        attended, out_weight, preferred_element_type=jnp.float32
    )
    mid_squares = lax.psum(jnp.sum(resid * resid, axis=1), "tp")
    normed = (resid * lax.rsqrt(mid_squares / full_width + EPSILON)[:, None] * norm_gain).astype(
        jnp.bfloat16
    )
    top_count = route_ids.shape[1]
    half_count = lax.axis_size("el")
    experts = half_count
    capacity = count_of_rows * top_count * 2 // experts
    buffer_len = experts * capacity
    flat_ids = route_ids.reshape(-1)
    expert_onehot = (flat_ids[:, None] == jnp.arange(experts, dtype=jnp.int32)[None, :]).astype(
        jnp.int32
    )
    expert_rank = jnp.sum(
        (jnp.cumsum(expert_onehot, axis=0) - expert_onehot) * expert_onehot, axis=1
    )
    my_half = lax.axis_index("el")
    target = (relative(flat_ids, my_half, half_count) * capacity + expert_rank).reshape(
        count_of_rows, top_count
    )
    slot_iota = jnp.arange(buffer_len, dtype=jnp.int32)
    hits = target[None, :, :] == slot_iota[:, None, None]
    dispatch = jnp.any(hits, axis=2).astype(jnp.bfloat16)
    outgoing = jnp.dot(dispatch, normed, preferred_element_type=jnp.float32).astype(jnp.bfloat16)
    arrived = exchange(outgoing.reshape(experts, capacity, feat_part), half_count)
    inputs = tp_gather(arrived, 2).reshape(buffer_len, full_width)
    gate_value = jnp.dot(inputs, gate_w[0], preferred_element_type=jnp.float32)
    up_value = jnp.dot(inputs, up_w[0], preferred_element_type=jnp.float32)
    hidden = (jnp.maximum(gate_value, 0.0) * up_value).astype(jnp.bfloat16)
    partial_value = jnp.dot(hidden, down_w[0], preferred_element_type=jnp.float32).astype(
        jnp.bfloat16
    )
    summed = tp_scatter_sum(partial_value, 1)
    returned = exchange(summed.reshape(experts, capacity, feat_part), half_count).reshape(
        buffer_len, feat_part
    )
    combine = jnp.sum(
        jnp.where(
            target[:, :, None] == slot_iota[None, None, :],
            route_weights[:, :, None],
            0.0,
        ),
        axis=1,
    )
    branch = jnp.dot(
        combine,
        returned.astype(jnp.float32),
        precision=lax.Precision.HIGHEST,
        preferred_element_type=jnp.float32,
    )
    mixed_rows = resid + branch
    out_squares = lax.psum(jnp.sum(mixed_rows * mixed_rows, axis=1), "tp")
    return (
        mixed_rows * lax.rsqrt(out_squares / full_width + EPSILON)[:, None] * final_gain
    ).astype(jnp.bfloat16)


def solution(mesh):
    ep_count, tp_count = mesh.devices.shape
    halves = Mesh(mesh.devices.reshape(2, ep_count // 2, tp_count), ("eh", "el", "tp"))
    ep = ("eh", "el")
    placed = (
        P(ep, "tp"),
        P(ep, None),
        P(ep, "tp", None, None, None),
        P(ep, None),
        P(ep, None),
        P(ep, None),
        P(None, "tp"),
        P("tp"),
        P(ep, None),
        P(ep, None),
        P(ep, None, "tp"),
        P(ep, None, "tp"),
        P(ep, "tp", None),
        P("tp"),
    )
    inner = jax.shard_map(
        shards, mesh=halves, in_specs=placed, out_specs=P(ep, "tp"), check_vma=False
    )
    result_sharding = NamedSharding(mesh, P("ep", "tp"))

    def run(*args):
        return lax.with_sharding_constraint(inner(*args), result_sharding)

    return run
```

```python
import jax
import jax.numpy as jnp
from jax import lax
from jax.sharding import Mesh, NamedSharding, PartitionSpec as P

QUERY_HEADS = 12
KEY_VALUE_HEADS = 2
HEAD_SIZE = 128
PAGE_POSITIONS = 16


EPSILON = 1e-06


def merged(shard, axis, join):
    gathered = jax.tree.map(
        lambda a, kind: lax.all_gather(a.astype(kind), axis),
        shard,
        (jnp.bfloat16, jnp.bfloat16, jnp.bfloat16),
    )

    def take(source):
        return jax.tree.map(
            lambda a, own: lax.dynamic_index_in_dim(a, source, 0, False).astype(own.dtype),
            gathered,
            shard,
        )

    return lax.fori_loop(
        1, lax.axis_size(axis), lambda source, state: join(state, take(source)), take(0)
    )


def relative(expert, me, count):
    if count & (count - 1) == 0:
        return jnp.bitwise_xor(expert, me)
    return (expert - me) % count


def exchange(chunks, count):
    pieces = [chunks[0]]
    for step in range(1, count):
        if count & (count - 1) == 0:
            pairs = [(i, i ^ step) for i in range(count)]
        else:
            pairs = [(i, (i + step) % count) for i in range(count)]
        pieces.append(lax.ppermute(chunks[step], "el", perm=pairs))
    return jnp.stack(pieces)


def expert_block(rows, gate_w, up_w, down_w):
    feat_part = rows.shape[1]
    if lax.axis_size("tp") != 2:
        inputs = lax.all_gather(rows, "tp", axis=1, tiled=True)
        gate_value = jnp.dot(inputs, gate_w, preferred_element_type=jnp.float32)
        up_value = jnp.dot(inputs, up_w, preferred_element_type=jnp.float32)
        hidden = (jnp.maximum(gate_value, 0.0) * up_value).astype(jnp.bfloat16)
        partial_value = jnp.dot(hidden, down_w, preferred_element_type=jnp.float32)
        return lax.psum_scatter(
            partial_value.astype(jnp.bfloat16), "tp", scatter_dimension=1, tiled=True
        )
    swap = [(0, 1), (1, 0)]
    mine = lax.axis_index("tp")
    other = 1 - mine
    rows_other = lax.ppermute(rows, "tp", perm=swap)
    gate_parts = gate_w.reshape(2, feat_part, gate_w.shape[1])
    up_parts = up_w.reshape(2, feat_part, up_w.shape[1])

    def half_product(parts, x, which):
        weight = lax.dynamic_index_in_dim(parts, which, 0, keepdims=False)
        return jnp.dot(x, weight, preferred_element_type=jnp.float32)

    gate_value = half_product(gate_parts, rows, mine) + half_product(gate_parts, rows_other, other)
    up_value = half_product(up_parts, rows, mine) + half_product(up_parts, rows_other, other)
    hidden = (jnp.maximum(gate_value, 0.0) * up_value).astype(jnp.bfloat16)

    def down_product(which):
        weight = lax.dynamic_slice_in_dim(down_w, which * feat_part, feat_part, axis=1)
        return jnp.dot(hidden, weight, preferred_element_type=jnp.float32).astype(jnp.bfloat16)

    sent = lax.ppermute(down_product(other), "tp", perm=swap)
    kept = down_product(mine)
    return (kept.astype(jnp.float32) + sent.astype(jnp.float32)).astype(jnp.bfloat16)


def tp_gather(part, axis):
    if lax.axis_size("tp") != 2:
        return lax.all_gather(part, "tp", axis=axis, tiled=True)
    other = lax.ppermute(part, "tp", perm=[(0, 1), (1, 0)])
    first = lax.axis_index("tp") == 0
    low = jnp.where(first, part, other)
    high = jnp.where(first, other, part)
    return jnp.concatenate([low, high], axis=axis)


def tp_scatter_sum(full, axis):
    if lax.axis_size("tp") != 2:
        return lax.psum_scatter(full, "tp", scatter_dimension=axis, tiled=True)
    low, high = jnp.split(full, 2, axis=axis)
    first = lax.axis_index("tp") == 0
    keep = jnp.where(first, low, high)
    send = jnp.where(first, high, low)
    other = lax.ppermute(send, "tp", perm=[(0, 1), (1, 0)])
    return (keep.astype(jnp.float32) + other.astype(jnp.float32)).astype(full.dtype)


def merge_parts(first, second):
    joint_max = jnp.maximum(first[0], second[0])
    scale_first = jnp.exp(first[0] - joint_max)
    scale_second = jnp.exp(second[0] - joint_max)
    return (
        joint_max,
        first[1] * scale_first + second[1] * scale_second,
        first[2] * scale_first[..., None] + second[2] * scale_second[..., None],
    )


def shards(
    tokens,
    queries,
    kv_cache,
    page_table,
    query_lens,
    past_lens,
    out_weight,
    norm_gain,
    route_ids,
    route_weights,
    gate_w,
    up_w,
    down_w,
    final_gain,
):
    tp_index = lax.axis_index("tp")
    tp_count = lax.axis_size("tp")
    count_of_rows, feat_part = tokens.shape
    full_width = feat_part * tp_count
    local_groups = query_lens.shape[0]
    req_count = query_lens.shape[1]
    group_rows = count_of_rows // local_groups
    head_groups = QUERY_HEADS // KEY_VALUE_HEADS
    per_device = page_table.shape[1] // tp_count

    def one_group(local):
        query_count = lax.dynamic_index_in_dim(query_lens, local, 0, keepdims=False)
        past_count = lax.dynamic_index_in_dim(past_lens, local, 0, keepdims=False)
        row_ends = jnp.cumsum(query_count)
        row_starts = row_ends - query_count
        row_iota = jnp.arange(group_rows, dtype=jnp.int32)
        row_req = jnp.sum((row_iota[:, None] >= row_ends[None, :]).astype(jnp.int32), axis=1)
        req_onehot = (row_req[:, None] == jnp.arange(req_count, dtype=jnp.int32)[None, :]).astype(
            jnp.int32
        )
        row_pos = row_iota + jnp.sum(req_onehot * (past_count - row_starts)[None, :], axis=1)
        local_table = lax.dynamic_index_in_dim(
            page_table.reshape(req_count, per_device, tp_count), tp_index, axis=2, keepdims=False
        )
        group_pages = lax.dynamic_index_in_dim(kv_cache, local, 0, keepdims=False)[0]
        page_row_block = group_pages[local_table.reshape(-1)]
        key_count_total = page_row_block.shape[0] * PAGE_POSITIONS
        flattened_cache = page_row_block.reshape(key_count_total, 2 * KEY_VALUE_HEADS * HEAD_SIZE)
        gathered_keys = flattened_cache[:, : KEY_VALUE_HEADS * HEAD_SIZE].reshape(
            key_count_total, KEY_VALUE_HEADS, HEAD_SIZE
        )
        gathered_values = flattened_cache[:, KEY_VALUE_HEADS * HEAD_SIZE :].reshape(
            key_count_total, KEY_VALUE_HEADS, HEAD_SIZE
        )
        key_iota = jnp.arange(key_count_total, dtype=jnp.int32)
        key_req = key_iota // (per_device * PAGE_POSITIONS)
        within = key_iota % (per_device * PAGE_POSITIONS)
        key_pos = (
            within // PAGE_POSITIONS * tp_count + tp_index
        ) * PAGE_POSITIONS + within % PAGE_POSITIONS
        allowed = (row_req[:, None] == key_req[None, :]) & (key_pos[None, :] <= row_pos[:, None])
        query_head_rows = queries.reshape(group_rows, KEY_VALUE_HEADS, head_groups, HEAD_SIZE)
        scores = jnp.einsum(
            "rkgd,lkd->rkgl", query_head_rows, gathered_keys, preferred_element_type=jnp.float32
        ) * HEAD_SIZE ** (-0.5)
        score_mask = allowed[:, None, None, :]
        part_max = jnp.max(jnp.where(score_mask, scores, -1e30), axis=-1)
        soft = jnp.where(score_mask, jnp.exp(scores - part_max[..., None]), 0.0)
        part_sum = jnp.sum(soft, axis=-1)
        part_weighted = jnp.einsum(
            "rkgl,lkd->rkgd",
            soft.astype(jnp.bfloat16),
            gathered_values,
            preferred_element_type=jnp.float32,
        )
        return (part_max, part_sum, part_weighted)

    row_max, row_sum, weighted = lax.map(one_group, jnp.arange(local_groups, dtype=jnp.int32))
    row_max = row_max.reshape(count_of_rows, KEY_VALUE_HEADS, head_groups)
    row_sum = row_sum.reshape(count_of_rows, KEY_VALUE_HEADS, head_groups)
    weighted = weighted.reshape(count_of_rows, KEY_VALUE_HEADS, head_groups, HEAD_SIZE)
    row_max, row_sum, weighted = merged((row_max, row_sum, weighted), "tp", merge_parts)
    attended = (
        (weighted / row_sum[..., None])
        .reshape(count_of_rows, QUERY_HEADS * HEAD_SIZE)
        .astype(jnp.bfloat16)
    )
    resid = tokens.astype(jnp.float32) + jnp.dot(
        attended, out_weight, preferred_element_type=jnp.float32
    )
    mid_squares = lax.psum(jnp.sum(resid * resid, axis=1), "tp")
    normed = (resid * lax.rsqrt(mid_squares / full_width + EPSILON)[:, None] * norm_gain).astype(
        jnp.bfloat16
    )
    top_count = route_ids.shape[1]
    half_count = lax.axis_size("el")
    experts = half_count
    capacity = count_of_rows * top_count * 2 // experts
    buffer_len = experts * capacity
    flat_ids = route_ids.reshape(-1)
    expert_onehot = (flat_ids[:, None] == jnp.arange(experts, dtype=jnp.int32)[None, :]).astype(
        jnp.int32
    )
    expert_rank = jnp.sum(
        (jnp.cumsum(expert_onehot, axis=0) - expert_onehot) * expert_onehot, axis=1
    )
    my_half = lax.axis_index("el")
    target = (relative(flat_ids, my_half, half_count) * capacity + expert_rank).reshape(
        count_of_rows, top_count
    )
    slot_iota = jnp.arange(buffer_len, dtype=jnp.int32)
    hits = target[None, :, :] == slot_iota[:, None, None]
    dispatch = jnp.any(hits, axis=2).astype(jnp.bfloat16)
    outgoing = jnp.dot(dispatch, normed, preferred_element_type=jnp.float32).astype(jnp.bfloat16)
    arrived = exchange(outgoing.reshape(experts, capacity, feat_part), half_count)
    summed = expert_block(arrived.reshape(buffer_len, feat_part), gate_w[0], up_w[0], down_w[0])
    returned = exchange(summed.reshape(experts, capacity, feat_part), half_count).reshape(
        buffer_len, feat_part
    )
    combine = jnp.sum(
        jnp.where(
            target[:, :, None] == slot_iota[None, None, :],
            route_weights[:, :, None],
            0.0,
        ),
        axis=1,
    )
    branch = jnp.dot(
        combine,
        returned.astype(jnp.float32),
        precision=lax.Precision.HIGHEST,
        preferred_element_type=jnp.float32,
    )
    mixed_rows = resid + branch
    out_squares = lax.psum(jnp.sum(mixed_rows * mixed_rows, axis=1), "tp")
    return (
        mixed_rows * lax.rsqrt(out_squares / full_width + EPSILON)[:, None] * final_gain
    ).astype(jnp.bfloat16)


def solution(mesh):
    ep_count, tp_count = mesh.devices.shape
    halves = Mesh(mesh.devices.reshape(2, ep_count // 2, tp_count), ("eh", "el", "tp"))
    ep = ("eh", "el")
    placed = (
        P(ep, "tp"),
        P(ep, None),
        P(ep, "tp", None, None, None),
        P(ep, None),
        P(ep, None),
        P(ep, None),
        P(None, "tp"),
        P("tp"),
        P(ep, None),
        P(ep, None),
        P(ep, None, "tp"),
        P(ep, None, "tp"),
        P(ep, "tp", None),
        P("tp"),
    )
    inner = jax.shard_map(
        shards, mesh=halves, in_specs=placed, out_specs=P(ep, "tp"), check_vma=False
    )
    result_sharding = NamedSharding(mesh, P("ep", "tp"))

    def run(*args):
        return lax.with_sharding_constraint(inner(*args), result_sharding)

    return run
```

```python
import jax
import jax.numpy as jnp
from jax import lax
from jax.experimental import pallas as pl
from jax.experimental.pallas import tpu as pltpu
from jax.sharding import Mesh, NamedSharding, PartitionSpec as P

QUERY_HEADS = 12
KEY_VALUE_HEADS = 2
HEAD_SIZE = 128
PAGE_POSITIONS = 16


EPSILON = 1e-06


def merged(shard, axis, join):
    if lax.axis_size(axis) == 2:
        rounded = jax.tree.map(lambda a: a.astype(jnp.bfloat16), shard)
        other = jax.tree.map(lambda a: lax.ppermute(a, axis, perm=[(0, 1), (1, 0)]), rounded)
        widen = lambda tree: jax.tree.map(lambda a, own: a.astype(own.dtype), tree, shard)
        return join(widen(rounded), widen(other))
    gathered = jax.tree.map(
        lambda a, kind: lax.all_gather(a.astype(kind), axis),
        shard,
        (jnp.bfloat16, jnp.bfloat16, jnp.bfloat16),
    )

    def take(source):
        return jax.tree.map(
            lambda a, own: lax.dynamic_index_in_dim(a, source, 0, False).astype(own.dtype),
            gathered,
            shard,
        )

    return lax.fori_loop(
        1, lax.axis_size(axis), lambda source, state: join(state, take(source)), take(0)
    )


def relative(expert, me, count):
    if count & (count - 1) == 0:
        return jnp.bitwise_xor(expert, me)
    return (expert - me) % count


def exchange(chunks, count):
    pieces = [chunks[0]]
    for step in range(1, count):
        if count & (count - 1) == 0:
            pairs = [(i, i ^ step) for i in range(count)]
        else:
            pairs = [(i, (i + step) % count) for i in range(count)]
        pieces.append(lax.ppermute(chunks[step], "el", perm=pairs))
    return jnp.stack(pieces)


def expert_block(rows, gate_w, up_w, down_w):
    feat_part = rows.shape[1]
    if lax.axis_size("tp") != 2:
        inputs = lax.all_gather(rows, "tp", axis=1, tiled=True)
        gate_value = jnp.dot(inputs, gate_w, preferred_element_type=jnp.float32)
        up_value = jnp.dot(inputs, up_w, preferred_element_type=jnp.float32)
        hidden = (jnp.maximum(gate_value, 0.0) * up_value).astype(jnp.bfloat16)
        partial_value = jnp.dot(hidden, down_w, preferred_element_type=jnp.float32)
        return lax.psum_scatter(
            partial_value.astype(jnp.bfloat16), "tp", scatter_dimension=1, tiled=True
        )
    swap = [(0, 1), (1, 0)]
    mine = lax.axis_index("tp")
    other = 1 - mine
    rows_other = lax.ppermute(rows, "tp", perm=swap)
    gate_parts = gate_w.reshape(2, feat_part, gate_w.shape[1])
    up_parts = up_w.reshape(2, feat_part, up_w.shape[1])

    def half_product(parts, x, which):
        weight = lax.dynamic_index_in_dim(parts, which, 0, keepdims=False)
        return jnp.dot(x, weight, preferred_element_type=jnp.float32)

    gate_value = half_product(gate_parts, rows, mine) + half_product(gate_parts, rows_other, other)
    up_value = half_product(up_parts, rows, mine) + half_product(up_parts, rows_other, other)
    hidden = (jnp.maximum(gate_value, 0.0) * up_value).astype(jnp.bfloat16)

    def down_product(which):
        weight = lax.dynamic_slice_in_dim(down_w, which * feat_part, feat_part, axis=1)
        return jnp.dot(hidden, weight, preferred_element_type=jnp.float32).astype(jnp.bfloat16)

    sent = lax.ppermute(down_product(other), "tp", perm=swap)
    kept = lax.optimization_barrier(down_product(mine))
    return (kept.astype(jnp.float32) + sent.astype(jnp.float32)).astype(jnp.bfloat16)


def tp_sum(value):
    if lax.axis_size("tp") != 2:
        return lax.psum(value, "tp")
    return value + lax.ppermute(value, "tp", perm=[(0, 1), (1, 0)])


def tp_gather(part, axis):
    if lax.axis_size("tp") != 2:
        return lax.all_gather(part, "tp", axis=axis, tiled=True)
    other = lax.ppermute(part, "tp", perm=[(0, 1), (1, 0)])
    first = lax.axis_index("tp") == 0
    low = jnp.where(first, part, other)
    high = jnp.where(first, other, part)
    return jnp.concatenate([low, high], axis=axis)


def tp_scatter_sum(full, axis):
    if lax.axis_size("tp") != 2:
        return lax.psum_scatter(full, "tp", scatter_dimension=axis, tiled=True)
    low, high = jnp.split(full, 2, axis=axis)
    first = lax.axis_index("tp") == 0
    keep = jnp.where(first, low, high)
    send = jnp.where(first, high, low)
    other = lax.ppermute(send, "tp", perm=[(0, 1), (1, 0)])
    return (keep.astype(jnp.float32) + other.astype(jnp.float32)).astype(full.dtype)


def merge_parts(first, second):
    joint_max = jnp.maximum(first[0], second[0])
    scale_first = jnp.exp(first[0] - joint_max)
    scale_second = jnp.exp(second[0] - joint_max)
    return (
        joint_max,
        first[1] * scale_first + second[1] * scale_second,
        first[2] * scale_first[..., None] + second[2] * scale_second[..., None],
    )


ATTN_BLOCK = 32


def attention_kernel(bounds_ref, q_ref, kv_ref, rreq_ref, rpos_ref, kpos_ref, w_ref, m_ref, l_ref):
    head_groups = QUERY_HEADS // KEY_VALUE_HEADS
    keys = kpos_ref.shape[1]
    scale = HEAD_SIZE ** (-0.5)
    w_ref[...] = jnp.zeros(w_ref.shape, jnp.float32)
    m_ref[...] = jnp.zeros(m_ref.shape, jnp.float32)
    l_ref[...] = jnp.zeros(l_ref.shape, jnp.float32)
    for block in range(q_ref.shape[0] // ATTN_BLOCK):
        rows = pl.ds(block * ATTN_BLOCK, ATTN_BLOCK)
        row_req = rreq_ref[rows, :]
        allowed = kpos_ref[...] <= rpos_ref[rows, :]
        allowed_heads = jnp.concatenate([allowed] * head_groups, axis=0)

        def body(request, carry, rows=rows, row_req=row_req, allowed_heads=allowed_heads):
            picked = row_req == request
            first_key = pl.multiple_of(request * keys, 128)
            for kv_head in range(KEY_VALUE_HEADS):
                stacked = jnp.concatenate(
                    [
                        q_ref[rows, pl.ds((kv_head * head_groups + g) * HEAD_SIZE, HEAD_SIZE)]
                        for g in range(head_groups)
                    ],
                    axis=0,
                )
                key_block = kv_ref[pl.ds(first_key, keys), pl.ds(kv_head * HEAD_SIZE, HEAD_SIZE)]
                value_block = kv_ref[
                    pl.ds(first_key, keys),
                    pl.ds((KEY_VALUE_HEADS + kv_head) * HEAD_SIZE, HEAD_SIZE),
                ]
                scores = lax.dot_general(
                    stacked,
                    key_block,
                    (((1,), (1,)), ((), ())),
                    preferred_element_type=jnp.float32,
                ) * scale
                scores = jnp.where(allowed_heads, scores, -1e30)
                top = jnp.max(scores, axis=1, keepdims=True)
                soft = jnp.where(allowed_heads, jnp.exp(scores - top), 0.0)
                total = jnp.sum(soft, axis=1, keepdims=True)
                weighted = jnp.dot(
                    soft.astype(jnp.bfloat16), value_block, preferred_element_type=jnp.float32
                )
                for g in range(head_groups):
                    head = kv_head * head_groups + g
                    part = slice(g * ATTN_BLOCK, (g + 1) * ATTN_BLOCK)
                    cols = pl.ds(head * HEAD_SIZE, HEAD_SIZE)
                    w_ref[rows, cols] = jnp.where(picked, weighted[part], w_ref[rows, cols])
                    one = pl.ds(head, 1)
                    m_ref[rows, one] = jnp.where(picked, top[part], m_ref[rows, one])
                    l_ref[rows, one] = jnp.where(picked, total[part], l_ref[rows, one])
            return carry

        lax.fori_loop(bounds_ref[2 * block], bounds_ref[2 * block + 1] + 1, body, 0)


def paged_attention(queries, cache_rows, row_req, row_pos, key_pos):
    rows = queries.shape[0]
    blocks = rows // ATTN_BLOCK
    bounds = jnp.stack(
        [row_req[0::ATTN_BLOCK], row_req[ATTN_BLOCK - 1 :: ATTN_BLOCK]], axis=1
    ).reshape(2 * blocks)
    vmem = pl.BlockSpec(memory_space=pltpu.VMEM)
    weighted, top, total = pl.pallas_call(
        attention_kernel,
        out_shape=(
            jax.ShapeDtypeStruct((rows, QUERY_HEADS * HEAD_SIZE), jnp.float32),
            jax.ShapeDtypeStruct((rows, QUERY_HEADS), jnp.float32),
            jax.ShapeDtypeStruct((rows, QUERY_HEADS), jnp.float32),
        ),
        in_specs=[pl.BlockSpec(memory_space=pltpu.SMEM)] + [vmem] * 5,
        out_specs=(vmem, vmem, vmem),
        cost_estimate=pl.CostEstimate(
            flops=4 * rows * QUERY_HEADS * HEAD_SIZE * key_pos.shape[1] * 2,
            transcendentals=rows * QUERY_HEADS * key_pos.shape[1] * 2,
            bytes_accessed=queries.size * 2 + cache_rows.size * 2 + rows * QUERY_HEADS * HEAD_SIZE * 4,
        ),
    )(bounds, queries, cache_rows, row_req[:, None], row_pos[:, None], key_pos)
    head_groups = QUERY_HEADS // KEY_VALUE_HEADS
    return (
        top.reshape(rows, KEY_VALUE_HEADS, head_groups),
        total.reshape(rows, KEY_VALUE_HEADS, head_groups),
        weighted.reshape(rows, KEY_VALUE_HEADS, head_groups, HEAD_SIZE),
    )


def shards(
    tokens,
    queries,
    kv_cache,
    page_table,
    query_lens,
    past_lens,
    out_weight,
    norm_gain,
    route_ids,
    route_weights,
    gate_w,
    up_w,
    down_w,
    final_gain,
):
    tp_index = lax.axis_index("tp")
    tp_count = lax.axis_size("tp")
    count_of_rows, feat_part = tokens.shape
    full_width = feat_part * tp_count
    local_groups = query_lens.shape[0]
    req_count = query_lens.shape[1]
    group_rows = count_of_rows // local_groups
    head_groups = QUERY_HEADS // KEY_VALUE_HEADS
    per_device = page_table.shape[1] // tp_count

    def one_group(local):
        query_count = lax.dynamic_index_in_dim(query_lens, local, 0, keepdims=False)
        past_count = lax.dynamic_index_in_dim(past_lens, local, 0, keepdims=False)
        row_ends = jnp.cumsum(query_count)
        row_starts = row_ends - query_count
        row_iota = jnp.arange(group_rows, dtype=jnp.int32)
        row_req = jnp.sum((row_iota[:, None] >= row_ends[None, :]).astype(jnp.int32), axis=1)
        req_onehot = (row_req[:, None] == jnp.arange(req_count, dtype=jnp.int32)[None, :]).astype(
            jnp.int32
        )
        row_pos = row_iota + jnp.sum(req_onehot * (past_count - row_starts)[None, :], axis=1)
        local_table = lax.dynamic_index_in_dim(
            page_table.reshape(req_count, per_device, tp_count), tp_index, axis=2, keepdims=False
        )
        group_pages = lax.dynamic_index_in_dim(kv_cache, local, 0, keepdims=False)[0]
        page_row_block = group_pages[local_table.reshape(-1)]
        key_count_total = page_row_block.shape[0] * PAGE_POSITIONS
        flattened_cache = page_row_block.reshape(key_count_total, 2 * KEY_VALUE_HEADS * HEAD_SIZE)
        gathered_keys = flattened_cache[:, : KEY_VALUE_HEADS * HEAD_SIZE].reshape(
            key_count_total, KEY_VALUE_HEADS, HEAD_SIZE
        )
        gathered_values = flattened_cache[:, KEY_VALUE_HEADS * HEAD_SIZE :].reshape(
            key_count_total, KEY_VALUE_HEADS, HEAD_SIZE
        )
        key_iota = jnp.arange(key_count_total, dtype=jnp.int32)
        key_req = key_iota // (per_device * PAGE_POSITIONS)
        within = key_iota % (per_device * PAGE_POSITIONS)
        key_pos = (
            within // PAGE_POSITIONS * tp_count + tp_index
        ) * PAGE_POSITIONS + within % PAGE_POSITIONS
        keys_per_req = per_device * PAGE_POSITIONS
        if keys_per_req % 128 == 0 and group_rows % ATTN_BLOCK == 0:
            return paged_attention(
                queries, flattened_cache, row_req, row_pos, key_pos[None, :keys_per_req]
            )
        allowed = (row_req[:, None] == key_req[None, :]) & (key_pos[None, :] <= row_pos[:, None])
        query_head_rows = queries.reshape(group_rows, KEY_VALUE_HEADS, head_groups, HEAD_SIZE)
        scores = jnp.einsum(
            "rkgd,lkd->rkgl", query_head_rows, gathered_keys, preferred_element_type=jnp.float32
        ) * HEAD_SIZE ** (-0.5)
        score_mask = allowed[:, None, None, :]
        part_max = jnp.max(jnp.where(score_mask, scores, -1e30), axis=-1)
        soft = jnp.where(score_mask, jnp.exp(scores - part_max[..., None]), 0.0)
        part_sum = jnp.sum(soft, axis=-1)
        part_weighted = jnp.einsum(
            "rkgl,lkd->rkgd",
            soft.astype(jnp.bfloat16),
            gathered_values,
            preferred_element_type=jnp.float32,
        )
        return (part_max, part_sum, part_weighted)

    row_max, row_sum, weighted = lax.map(one_group, jnp.arange(local_groups, dtype=jnp.int32))
    row_max = row_max.reshape(count_of_rows, KEY_VALUE_HEADS, head_groups)
    row_sum = row_sum.reshape(count_of_rows, KEY_VALUE_HEADS, head_groups)
    weighted = weighted.reshape(count_of_rows, KEY_VALUE_HEADS, head_groups, HEAD_SIZE)
    row_max, row_sum, weighted = merged((row_max, row_sum, weighted), "tp", merge_parts)
    attended = (
        (weighted / row_sum[..., None])
        .reshape(count_of_rows, QUERY_HEADS * HEAD_SIZE)
        .astype(jnp.bfloat16)
    )
    resid = tokens.astype(jnp.float32) + jnp.dot(
        attended, out_weight, preferred_element_type=jnp.float32
    )
    mid_squares = tp_sum(jnp.sum(resid * resid, axis=1))
    normed = (resid * lax.rsqrt(mid_squares / full_width + EPSILON)[:, None] * norm_gain).astype(
        jnp.bfloat16
    )
    top_count = route_ids.shape[1]
    half_count = lax.axis_size("el")
    experts = half_count
    capacity = count_of_rows * top_count * 2 // experts
    buffer_len = experts * capacity
    flat_ids = route_ids.reshape(-1)
    expert_onehot = (flat_ids[:, None] == jnp.arange(experts, dtype=jnp.int32)[None, :]).astype(
        jnp.int32
    )
    assign_iota = jnp.arange(flat_ids.shape[0], dtype=jnp.int32)
    earlier = (assign_iota[None, :] < assign_iota[:, None]).astype(jnp.bfloat16)
    before = jnp.dot(
        earlier, expert_onehot.astype(jnp.bfloat16), preferred_element_type=jnp.float32
    ).astype(jnp.int32)
    expert_rank = jnp.sum(before * expert_onehot, axis=1)
    my_half = lax.axis_index("el")
    target = (relative(flat_ids, my_half, half_count) * capacity + expert_rank).reshape(
        count_of_rows, top_count
    )
    slot_iota = jnp.arange(buffer_len, dtype=jnp.int32)
    hits = target[None, :, :] == slot_iota[:, None, None]
    dispatch = jnp.any(hits, axis=2).astype(jnp.bfloat16)
    outgoing = jnp.dot(dispatch, normed, preferred_element_type=jnp.float32).astype(jnp.bfloat16)
    arrived = exchange(outgoing.reshape(experts, capacity, feat_part), half_count)
    flat_rows = lax.optimization_barrier(arrived.reshape(buffer_len, feat_part))
    group_rows = buffer_len // 2
    summed = jnp.concatenate(
        [
            expert_block(
                flat_rows[start : start + group_rows], gate_w[0], up_w[0], down_w[0]
            )
            for start in (0, group_rows)
        ],
        axis=0,
    )
    returned = exchange(summed.reshape(experts, capacity, feat_part), half_count).reshape(
        buffer_len, feat_part
    )
    combine = jnp.sum(
        jnp.where(
            target[:, :, None] == slot_iota[None, None, :],
            route_weights[:, :, None],
            0.0,
        ),
        axis=1,
    )
    branch = jnp.dot(
        combine,
        returned.astype(jnp.float32),
        precision=lax.Precision.HIGHEST,
        preferred_element_type=jnp.float32,
    )
    mixed_rows = resid + branch
    out_squares = tp_sum(jnp.sum(mixed_rows * mixed_rows, axis=1))
    return (
        mixed_rows * lax.rsqrt(out_squares / full_width + EPSILON)[:, None] * final_gain
    ).astype(jnp.bfloat16)


def solution(mesh):
    ep_count, tp_count = mesh.devices.shape
    halves = Mesh(mesh.devices.reshape(2, ep_count // 2, tp_count), ("eh", "el", "tp"))
    ep = ("eh", "el")
    placed = (
        P(ep, "tp"),
        P(ep, None),
        P(ep, "tp", None, None, None),
        P(ep, None),
        P(ep, None),
        P(ep, None),
        P(None, "tp"),
        P("tp"),
        P(ep, None),
        P(ep, None),
        P(ep, None, "tp"),
        P(ep, None, "tp"),
        P(ep, "tp", None),
        P("tp"),
    )
    inner = jax.shard_map(
        shards, mesh=halves, in_specs=placed, out_specs=P(ep, "tp"), check_vma=False
    )
    result_sharding = NamedSharding(mesh, P("ep", "tp"))

    def run(*args):
        return lax.with_sharding_constraint(inner(*args), result_sharding)

    return run
```

```python
import jax
import jax.numpy as jnp
from jax import lax
from jax.experimental import pallas as pl
from jax.experimental.pallas import tpu as pltpu
from jax.sharding import Mesh, NamedSharding, PartitionSpec as P

QUERY_HEADS = 12
KEY_VALUE_HEADS = 2
HEAD_SIZE = 128
PAGE_POSITIONS = 16


EPSILON = 1e-06


def merged(shard, axis, join):
    if lax.axis_size(axis) == 2:
        rounded = jax.tree.map(lambda a: a.astype(jnp.bfloat16), shard)
        other = jax.tree.map(lambda a: lax.ppermute(a, axis, perm=[(0, 1), (1, 0)]), rounded)
        widen = lambda tree: jax.tree.map(lambda a, own: a.astype(own.dtype), tree, shard)
        return join(widen(rounded), widen(other))
    gathered = jax.tree.map(
        lambda a, kind: lax.all_gather(a.astype(kind), axis),
        shard,
        (jnp.bfloat16, jnp.bfloat16, jnp.bfloat16),
    )

    def take(source):
        return jax.tree.map(
            lambda a, own: lax.dynamic_index_in_dim(a, source, 0, False).astype(own.dtype),
            gathered,
            shard,
        )

    return lax.fori_loop(
        1, lax.axis_size(axis), lambda source, state: join(state, take(source)), take(0)
    )


def relative(expert, me, count):
    if count & (count - 1) == 0:
        return jnp.bitwise_xor(expert, me)
    return (expert - me) % count


def exchange(chunks, count):
    pieces = [chunks[0]]
    for step in range(1, count):
        if count & (count - 1) == 0:
            pairs = [(i, i ^ step) for i in range(count)]
        else:
            pairs = [(i, (i + step) % count) for i in range(count)]
        pieces.append(lax.ppermute(chunks[step], "el", perm=pairs))
    return jnp.stack(pieces)


def expert_block(rows, gate_w, up_w, down_w):
    feat_part = rows.shape[1]
    if lax.axis_size("tp") != 2:
        inputs = lax.all_gather(rows, "tp", axis=1, tiled=True)
        gate_value = jnp.dot(inputs, gate_w, preferred_element_type=jnp.float32)
        up_value = jnp.dot(inputs, up_w, preferred_element_type=jnp.float32)
        hidden = (jnp.maximum(gate_value, 0.0) * up_value).astype(jnp.bfloat16)
        partial_value = jnp.dot(hidden, down_w, preferred_element_type=jnp.float32)
        return lax.psum_scatter(
            partial_value.astype(jnp.bfloat16), "tp", scatter_dimension=1, tiled=True
        )
    swap = [(0, 1), (1, 0)]
    mine = lax.axis_index("tp")
    other = 1 - mine
    rows_other = lax.ppermute(rows, "tp", perm=swap)
    gate_parts = gate_w.reshape(2, feat_part, gate_w.shape[1])
    up_parts = up_w.reshape(2, feat_part, up_w.shape[1])

    def half_product(parts, x, which):
        weight = lax.dynamic_index_in_dim(parts, which, 0, keepdims=False)
        return jnp.dot(x, weight, preferred_element_type=jnp.float32)

    gate_value = half_product(gate_parts, rows, mine) + half_product(gate_parts, rows_other, other)
    up_value = half_product(up_parts, rows, mine) + half_product(up_parts, rows_other, other)
    hidden = (jnp.maximum(gate_value, 0.0) * up_value).astype(jnp.bfloat16)

    def down_product(which):
        weight = lax.dynamic_slice_in_dim(down_w, which * feat_part, feat_part, axis=1)
        return jnp.dot(hidden, weight, preferred_element_type=jnp.float32).astype(jnp.bfloat16)

    sent = lax.ppermute(down_product(other), "tp", perm=swap)
    kept = lax.optimization_barrier(down_product(mine))
    return (kept.astype(jnp.float32) + sent.astype(jnp.float32)).astype(jnp.bfloat16)


def tp_sum(value):
    if lax.axis_size("tp") != 2:
        return lax.psum(value, "tp")
    return value + lax.ppermute(value, "tp", perm=[(0, 1), (1, 0)])


def tp_gather(part, axis):
    if lax.axis_size("tp") != 2:
        return lax.all_gather(part, "tp", axis=axis, tiled=True)
    other = lax.ppermute(part, "tp", perm=[(0, 1), (1, 0)])
    first = lax.axis_index("tp") == 0
    low = jnp.where(first, part, other)
    high = jnp.where(first, other, part)
    return jnp.concatenate([low, high], axis=axis)


def tp_scatter_sum(full, axis):
    if lax.axis_size("tp") != 2:
        return lax.psum_scatter(full, "tp", scatter_dimension=axis, tiled=True)
    low, high = jnp.split(full, 2, axis=axis)
    first = lax.axis_index("tp") == 0
    keep = jnp.where(first, low, high)
    send = jnp.where(first, high, low)
    other = lax.ppermute(send, "tp", perm=[(0, 1), (1, 0)])
    return (keep.astype(jnp.float32) + other.astype(jnp.float32)).astype(full.dtype)


def merge_parts(first, second):
    joint_max = jnp.maximum(first[0], second[0])
    scale_first = jnp.exp(first[0] - joint_max)
    scale_second = jnp.exp(second[0] - joint_max)
    return (
        joint_max,
        first[1] * scale_first + second[1] * scale_second,
        first[2] * scale_first[..., None] + second[2] * scale_second[..., None],
    )


ATTN_BLOCK = 32


def attention_kernel(bounds_ref, q_ref, kv_ref, rreq_ref, rpos_ref, kpos_ref, w_ref, m_ref, l_ref):
    keys = kpos_ref.shape[1]
    scale = HEAD_SIZE ** (-0.5)
    w_ref[...] = jnp.zeros(w_ref.shape, jnp.float32)
    m_ref[...] = jnp.zeros(m_ref.shape, jnp.float32)
    l_ref[...] = jnp.zeros(l_ref.shape, jnp.float32)
    for block in range(q_ref.shape[1]):
        row_req = rreq_ref[block]
        allowed = kpos_ref[...] <= rpos_ref[block]

        def body(request, carry, block=block, row_req=row_req, allowed=allowed):
            picked = row_req == request
            first_key = pl.multiple_of(request * keys, 128)
            for kv_head in range(KEY_VALUE_HEADS):
                key_block = kv_ref[pl.ds(first_key, keys), pl.ds(kv_head * HEAD_SIZE, HEAD_SIZE)]
                value_block = kv_ref[
                    pl.ds(first_key, keys),
                    pl.ds((KEY_VALUE_HEADS + kv_head) * HEAD_SIZE, HEAD_SIZE),
                ]
                scores = lax.dot_general(
                    q_ref[kv_head, block],
                    key_block,
                    (((1,), (1,)), ((), ())),
                    preferred_element_type=jnp.float32,
                ) * scale
                scores = jnp.where(allowed, scores, -1e30)
                top = jnp.max(scores, axis=1, keepdims=True)
                soft = jnp.where(allowed, jnp.exp(scores - top), 0.0)
                total = jnp.sum(soft, axis=1, keepdims=True)
                weighted = jnp.dot(
                    soft.astype(jnp.bfloat16), value_block, preferred_element_type=jnp.float32
                )
                w_ref[kv_head, block] = jnp.where(picked, weighted, w_ref[kv_head, block])
                m_ref[kv_head, block] = jnp.where(picked, top, m_ref[kv_head, block])
                l_ref[kv_head, block] = jnp.where(picked, total, l_ref[kv_head, block])
            return carry

        lax.fori_loop(bounds_ref[2 * block], bounds_ref[2 * block + 1] + 1, body, 0)


def paged_attention(queries, cache_rows, row_req, row_pos, key_pos):
    rows = queries.shape[0]
    blocks = rows // ATTN_BLOCK
    head_groups = QUERY_HEADS // KEY_VALUE_HEADS
    stack = head_groups * ATTN_BLOCK
    bounds = jnp.stack(
        [row_req[0::ATTN_BLOCK], row_req[ATTN_BLOCK - 1 :: ATTN_BLOCK]], axis=1
    ).reshape(2 * blocks)
    stacked_q = (
        queries.reshape(blocks, ATTN_BLOCK, KEY_VALUE_HEADS, head_groups, HEAD_SIZE)
        .transpose(2, 0, 3, 1, 4)
        .reshape(KEY_VALUE_HEADS, blocks, stack, HEAD_SIZE)
    )

    def per_row(values):
        return jnp.broadcast_to(
            values.reshape(blocks, 1, ATTN_BLOCK), (blocks, head_groups, ATTN_BLOCK)
        ).reshape(blocks, stack, 1)

    vmem = pl.BlockSpec(memory_space=pltpu.VMEM)
    weighted, top, total = pl.pallas_call(
        attention_kernel,
        out_shape=(
            jax.ShapeDtypeStruct((KEY_VALUE_HEADS, blocks, stack, HEAD_SIZE), jnp.float32),
            jax.ShapeDtypeStruct((KEY_VALUE_HEADS, blocks, stack, 1), jnp.float32),
            jax.ShapeDtypeStruct((KEY_VALUE_HEADS, blocks, stack, 1), jnp.float32),
        ),
        in_specs=[pl.BlockSpec(memory_space=pltpu.SMEM)] + [vmem] * 5,
        out_specs=(vmem, vmem, vmem),
        cost_estimate=pl.CostEstimate(
            flops=4 * rows * QUERY_HEADS * HEAD_SIZE * key_pos.shape[1] * 2,
            transcendentals=rows * QUERY_HEADS * key_pos.shape[1] * 2,
            bytes_accessed=queries.size * 2 + cache_rows.size * 2 + rows * QUERY_HEADS * HEAD_SIZE * 4,
        ),
    )(bounds, stacked_q, cache_rows, per_row(row_req), per_row(row_pos), key_pos)

    def unstack(values):
        return (
            values.reshape(KEY_VALUE_HEADS, blocks, head_groups, ATTN_BLOCK, -1)
            .transpose(1, 3, 0, 2, 4)
            .reshape(rows, KEY_VALUE_HEADS, head_groups, -1)
        )

    return (unstack(top)[..., 0], unstack(total)[..., 0], unstack(weighted))


def shards(
    tokens,
    queries,
    kv_cache,
    page_table,
    query_lens,
    past_lens,
    out_weight,
    norm_gain,
    route_ids,
    route_weights,
    gate_w,
    up_w,
    down_w,
    final_gain,
):
    tp_index = lax.axis_index("tp")
    tp_count = lax.axis_size("tp")
    count_of_rows, feat_part = tokens.shape
    full_width = feat_part * tp_count
    local_groups = query_lens.shape[0]
    req_count = query_lens.shape[1]
    group_rows = count_of_rows // local_groups
    head_groups = QUERY_HEADS // KEY_VALUE_HEADS
    per_device = page_table.shape[1] // tp_count

    def one_group(local):
        query_count = lax.dynamic_index_in_dim(query_lens, local, 0, keepdims=False)
        past_count = lax.dynamic_index_in_dim(past_lens, local, 0, keepdims=False)
        row_ends = jnp.cumsum(query_count)
        row_starts = row_ends - query_count
        row_iota = jnp.arange(group_rows, dtype=jnp.int32)
        row_req = jnp.sum((row_iota[:, None] >= row_ends[None, :]).astype(jnp.int32), axis=1)
        req_onehot = (row_req[:, None] == jnp.arange(req_count, dtype=jnp.int32)[None, :]).astype(
            jnp.int32
        )
        row_pos = row_iota + jnp.sum(req_onehot * (past_count - row_starts)[None, :], axis=1)
        local_table = lax.dynamic_index_in_dim(
            page_table.reshape(req_count, per_device, tp_count), tp_index, axis=2, keepdims=False
        )
        group_pages = lax.dynamic_index_in_dim(kv_cache, local, 0, keepdims=False)[0]
        page_row_block = group_pages[local_table.reshape(-1)]
        key_count_total = page_row_block.shape[0] * PAGE_POSITIONS
        flattened_cache = page_row_block.reshape(key_count_total, 2 * KEY_VALUE_HEADS * HEAD_SIZE)
        gathered_keys = flattened_cache[:, : KEY_VALUE_HEADS * HEAD_SIZE].reshape(
            key_count_total, KEY_VALUE_HEADS, HEAD_SIZE
        )
        gathered_values = flattened_cache[:, KEY_VALUE_HEADS * HEAD_SIZE :].reshape(
            key_count_total, KEY_VALUE_HEADS, HEAD_SIZE
        )
        key_iota = jnp.arange(key_count_total, dtype=jnp.int32)
        key_req = key_iota // (per_device * PAGE_POSITIONS)
        within = key_iota % (per_device * PAGE_POSITIONS)
        key_pos = (
            within // PAGE_POSITIONS * tp_count + tp_index
        ) * PAGE_POSITIONS + within % PAGE_POSITIONS
        keys_per_req = per_device * PAGE_POSITIONS
        if keys_per_req % 128 == 0 and group_rows % ATTN_BLOCK == 0:
            return paged_attention(
                queries, flattened_cache, row_req, row_pos, key_pos[None, :keys_per_req]
            )
        allowed = (row_req[:, None] == key_req[None, :]) & (key_pos[None, :] <= row_pos[:, None])
        query_head_rows = queries.reshape(group_rows, KEY_VALUE_HEADS, head_groups, HEAD_SIZE)
        scores = jnp.einsum(
            "rkgd,lkd->rkgl", query_head_rows, gathered_keys, preferred_element_type=jnp.float32
        ) * HEAD_SIZE ** (-0.5)
        score_mask = allowed[:, None, None, :]
        part_max = jnp.max(jnp.where(score_mask, scores, -1e30), axis=-1)
        soft = jnp.where(score_mask, jnp.exp(scores - part_max[..., None]), 0.0)
        part_sum = jnp.sum(soft, axis=-1)
        part_weighted = jnp.einsum(
            "rkgl,lkd->rkgd",
            soft.astype(jnp.bfloat16),
            gathered_values,
            preferred_element_type=jnp.float32,
        )
        return (part_max, part_sum, part_weighted)

    row_max, row_sum, weighted = lax.map(one_group, jnp.arange(local_groups, dtype=jnp.int32))
    row_max = row_max.reshape(count_of_rows, KEY_VALUE_HEADS, head_groups)
    row_sum = row_sum.reshape(count_of_rows, KEY_VALUE_HEADS, head_groups)
    weighted = weighted.reshape(count_of_rows, KEY_VALUE_HEADS, head_groups, HEAD_SIZE)
    row_max, row_sum, weighted = merged((row_max, row_sum, weighted), "tp", merge_parts)
    attended = (
        (weighted / row_sum[..., None])
        .reshape(count_of_rows, QUERY_HEADS * HEAD_SIZE)
        .astype(jnp.bfloat16)
    )
    resid = tokens.astype(jnp.float32) + jnp.dot(
        attended, out_weight, preferred_element_type=jnp.float32
    )
    mid_squares = tp_sum(jnp.sum(resid * resid, axis=1))
    normed = (resid * lax.rsqrt(mid_squares / full_width + EPSILON)[:, None] * norm_gain).astype(
        jnp.bfloat16
    )
    top_count = route_ids.shape[1]
    half_count = lax.axis_size("el")
    experts = half_count
    capacity = count_of_rows * top_count * 2 // experts
    buffer_len = experts * capacity
    flat_ids = route_ids.reshape(-1)
    expert_onehot = (flat_ids[:, None] == jnp.arange(experts, dtype=jnp.int32)[None, :]).astype(
        jnp.int32
    )
    assign_iota = jnp.arange(flat_ids.shape[0], dtype=jnp.int32)
    earlier = (assign_iota[None, :] < assign_iota[:, None]).astype(jnp.bfloat16)
    before = jnp.dot(
        earlier, expert_onehot.astype(jnp.bfloat16), preferred_element_type=jnp.float32
    ).astype(jnp.int32)
    expert_rank = jnp.sum(before * expert_onehot, axis=1)
    my_half = lax.axis_index("el")
    target = (relative(flat_ids, my_half, half_count) * capacity + expert_rank).reshape(
        count_of_rows, top_count
    )
    slot_iota = jnp.arange(buffer_len, dtype=jnp.int32)
    hits = target[None, :, :] == slot_iota[:, None, None]
    dispatch = jnp.any(hits, axis=2).astype(jnp.bfloat16)
    outgoing = jnp.dot(dispatch, normed, preferred_element_type=jnp.float32).astype(jnp.bfloat16)
    arrived = exchange(outgoing.reshape(experts, capacity, feat_part), half_count)
    flat_rows = lax.optimization_barrier(arrived.reshape(buffer_len, feat_part))
    group_rows = buffer_len // 2
    summed = jnp.concatenate(
        [
            expert_block(
                flat_rows[start : start + group_rows], gate_w[0], up_w[0], down_w[0]
            )
            for start in (0, group_rows)
        ],
        axis=0,
    )
    returned = exchange(summed.reshape(experts, capacity, feat_part), half_count).reshape(
        buffer_len, feat_part
    )
    combine = jnp.sum(
        jnp.where(
            target[:, :, None] == slot_iota[None, None, :],
            route_weights[:, :, None],
            0.0,
        ),
        axis=1,
    )
    branch = jnp.dot(
        combine,
        returned.astype(jnp.float32),
        precision=lax.Precision.HIGHEST,
        preferred_element_type=jnp.float32,
    )
    mixed_rows = resid + branch
    out_squares = tp_sum(jnp.sum(mixed_rows * mixed_rows, axis=1))
    return (
        mixed_rows * lax.rsqrt(out_squares / full_width + EPSILON)[:, None] * final_gain
    ).astype(jnp.bfloat16)


def solution(mesh):
    ep_count, tp_count = mesh.devices.shape
    halves = Mesh(mesh.devices.reshape(2, ep_count // 2, tp_count), ("eh", "el", "tp"))
    ep = ("eh", "el")
    placed = (
        P(ep, "tp"),
        P(ep, None),
        P(ep, "tp", None, None, None),
        P(ep, None),
        P(ep, None),
        P(ep, None),
        P(None, "tp"),
        P("tp"),
        P(ep, None),
        P(ep, None),
        P(ep, None, "tp"),
        P(ep, None, "tp"),
        P(ep, "tp", None),
        P("tp"),
    )
    inner = jax.shard_map(
        shards, mesh=halves, in_specs=placed, out_specs=P(ep, "tp"), check_vma=False
    )
    result_sharding = NamedSharding(mesh, P("ep", "tp"))

    def run(*args):
        return lax.with_sharding_constraint(inner(*args), result_sharding)

    return run
```

```python
import jax
import jax.numpy as jnp
from jax import lax
from jax.sharding import Mesh, NamedSharding, PartitionSpec as P

QUERY_HEADS = 12
KEY_VALUE_HEADS = 2
HEAD_SIZE = 128
PAGE_POSITIONS = 16


EPSILON = 1e-06


def merged(shard, axis, join):
    if lax.axis_size(axis) == 2:
        rounded = jax.tree.map(lambda a: a.astype(jnp.bfloat16), shard)
        other = jax.tree.map(lambda a: lax.ppermute(a, axis, perm=[(0, 1), (1, 0)]), rounded)
        widen = lambda tree: jax.tree.map(lambda a, own: a.astype(own.dtype), tree, shard)
        return join(widen(rounded), widen(other))
    gathered = jax.tree.map(
        lambda a, kind: lax.all_gather(a.astype(kind), axis),
        shard,
        (jnp.bfloat16, jnp.bfloat16, jnp.bfloat16),
    )

    def take(source):
        return jax.tree.map(
            lambda a, own: lax.dynamic_index_in_dim(a, source, 0, False).astype(own.dtype),
            gathered,
            shard,
        )

    return lax.fori_loop(
        1, lax.axis_size(axis), lambda source, state: join(state, take(source)), take(0)
    )


def relative(expert, me, count):
    if count & (count - 1) == 0:
        return jnp.bitwise_xor(expert, me)
    return (expert - me) % count


def exchange(chunks, count):
    pieces = [chunks[0]]
    for step in range(1, count):
        if count & (count - 1) == 0:
            pairs = [(i, i ^ step) for i in range(count)]
        else:
            pairs = [(i, (i + step) % count) for i in range(count)]
        pieces.append(lax.ppermute(chunks[step], "el", perm=pairs))
    return jnp.stack(pieces)


def expert_block(rows, gate_w, up_w, down_w):
    feat_part = rows.shape[1]
    if lax.axis_size("tp") != 2:
        inputs = lax.all_gather(rows, "tp", axis=1, tiled=True)
        gate_value = jnp.dot(inputs, gate_w, preferred_element_type=jnp.float32)
        up_value = jnp.dot(inputs, up_w, preferred_element_type=jnp.float32)
        hidden = (jnp.maximum(gate_value, 0.0) * up_value).astype(jnp.bfloat16)
        partial_value = jnp.dot(hidden, down_w, preferred_element_type=jnp.float32)
        return lax.psum_scatter(
            partial_value.astype(jnp.bfloat16), "tp", scatter_dimension=1, tiled=True
        )
    swap = [(0, 1), (1, 0)]
    mine = lax.axis_index("tp")
    other = 1 - mine
    rows_other = lax.ppermute(rows, "tp", perm=swap)
    gate_parts = gate_w.reshape(2, feat_part, gate_w.shape[1])
    up_parts = up_w.reshape(2, feat_part, up_w.shape[1])

    def half_product(parts, x, which):
        weight = lax.dynamic_index_in_dim(parts, which, 0, keepdims=False)
        return jnp.dot(x, weight, preferred_element_type=jnp.float32)

    gate_value = half_product(gate_parts, rows, mine) + half_product(gate_parts, rows_other, other)
    up_value = half_product(up_parts, rows, mine) + half_product(up_parts, rows_other, other)
    hidden = (jnp.maximum(gate_value, 0.0) * up_value).astype(jnp.bfloat16)

    def down_product(which):
        weight = lax.dynamic_slice_in_dim(down_w, which * feat_part, feat_part, axis=1)
        return jnp.dot(hidden, weight, preferred_element_type=jnp.float32).astype(jnp.bfloat16)

    sent = lax.ppermute(down_product(other), "tp", perm=swap)
    kept = lax.optimization_barrier(down_product(mine))
    return (kept.astype(jnp.float32) + sent.astype(jnp.float32)).astype(jnp.bfloat16)


def tp_sum(value):
    if lax.axis_size("tp") != 2:
        return lax.psum(value, "tp")
    return value + lax.ppermute(value, "tp", perm=[(0, 1), (1, 0)])


def tp_gather(part, axis):
    if lax.axis_size("tp") != 2:
        return lax.all_gather(part, "tp", axis=axis, tiled=True)
    other = lax.ppermute(part, "tp", perm=[(0, 1), (1, 0)])
    first = lax.axis_index("tp") == 0
    low = jnp.where(first, part, other)
    high = jnp.where(first, other, part)
    return jnp.concatenate([low, high], axis=axis)


def tp_scatter_sum(full, axis):
    if lax.axis_size("tp") != 2:
        return lax.psum_scatter(full, "tp", scatter_dimension=axis, tiled=True)
    low, high = jnp.split(full, 2, axis=axis)
    first = lax.axis_index("tp") == 0
    keep = jnp.where(first, low, high)
    send = jnp.where(first, high, low)
    other = lax.ppermute(send, "tp", perm=[(0, 1), (1, 0)])
    return (keep.astype(jnp.float32) + other.astype(jnp.float32)).astype(full.dtype)


def merge_parts(first, second):
    joint_max = jnp.maximum(first[0], second[0])
    scale_first = jnp.exp(first[0] - joint_max)
    scale_second = jnp.exp(second[0] - joint_max)
    return (
        joint_max,
        first[1] * scale_first + second[1] * scale_second,
        first[2] * scale_first[..., None] + second[2] * scale_second[..., None],
    )


def shards(
    tokens,
    queries,
    kv_cache,
    page_table,
    query_lens,
    past_lens,
    out_weight,
    norm_gain,
    route_ids,
    route_weights,
    gate_w,
    up_w,
    down_w,
    final_gain,
):
    tp_index = lax.axis_index("tp")
    tp_count = lax.axis_size("tp")
    count_of_rows, feat_part = tokens.shape
    full_width = feat_part * tp_count
    local_groups = query_lens.shape[0]
    req_count = query_lens.shape[1]
    group_rows = count_of_rows // local_groups
    head_groups = QUERY_HEADS // KEY_VALUE_HEADS
    per_device = page_table.shape[1] // tp_count

    def one_group(local):
        query_count = lax.dynamic_index_in_dim(query_lens, local, 0, keepdims=False)
        past_count = lax.dynamic_index_in_dim(past_lens, local, 0, keepdims=False)
        row_ends = jnp.cumsum(query_count)
        row_starts = row_ends - query_count
        row_iota = jnp.arange(group_rows, dtype=jnp.int32)
        row_req = jnp.sum((row_iota[:, None] >= row_ends[None, :]).astype(jnp.int32), axis=1)
        req_onehot = (row_req[:, None] == jnp.arange(req_count, dtype=jnp.int32)[None, :]).astype(
            jnp.int32
        )
        row_pos = row_iota + jnp.sum(req_onehot * (past_count - row_starts)[None, :], axis=1)
        local_table = lax.dynamic_index_in_dim(
            page_table.reshape(req_count, per_device, tp_count), tp_index, axis=2, keepdims=False
        )
        group_pages = lax.dynamic_index_in_dim(kv_cache, local, 0, keepdims=False)[0]
        page_row_block = group_pages[local_table.reshape(-1)]
        key_count_total = page_row_block.shape[0] * PAGE_POSITIONS
        flattened_cache = page_row_block.reshape(key_count_total, 2 * KEY_VALUE_HEADS * HEAD_SIZE)
        gathered_keys = flattened_cache[:, : KEY_VALUE_HEADS * HEAD_SIZE].reshape(
            key_count_total, KEY_VALUE_HEADS, HEAD_SIZE
        )
        gathered_values = flattened_cache[:, KEY_VALUE_HEADS * HEAD_SIZE :].reshape(
            key_count_total, KEY_VALUE_HEADS, HEAD_SIZE
        )
        key_iota = jnp.arange(key_count_total, dtype=jnp.int32)
        key_req = key_iota // (per_device * PAGE_POSITIONS)
        within = key_iota % (per_device * PAGE_POSITIONS)
        key_pos = (
            within // PAGE_POSITIONS * tp_count + tp_index
        ) * PAGE_POSITIONS + within % PAGE_POSITIONS
        allowed = (row_req[:, None] == key_req[None, :]) & (key_pos[None, :] <= row_pos[:, None])
        score_mask = allowed[:, None, :]
        outs = []
        for kv_head in range(KEY_VALUE_HEADS):
            head_rows = queries[:, kv_head * head_groups * HEAD_SIZE : (kv_head + 1) * head_groups * HEAD_SIZE]
            head_rows = head_rows.reshape(group_rows, head_groups, HEAD_SIZE)
            head_keys = flattened_cache[:, kv_head * HEAD_SIZE : (kv_head + 1) * HEAD_SIZE]
            head_values = flattened_cache[
                :, (KEY_VALUE_HEADS + kv_head) * HEAD_SIZE : (KEY_VALUE_HEADS + kv_head + 1) * HEAD_SIZE
            ]
            scores = jnp.einsum(
                "rgd,ld->rgl", head_rows, head_keys, preferred_element_type=jnp.float32
            ) * HEAD_SIZE ** (-0.5)
            top = jnp.max(jnp.where(score_mask, scores, -1e30), axis=-1)
            soft = jnp.where(score_mask, jnp.exp(scores - top[..., None]), 0.0)
            total = jnp.sum(soft, axis=-1)
            weighted_part = jnp.einsum(
                "rgl,ld->rgd",
                soft.astype(jnp.bfloat16),
                head_values,
                preferred_element_type=jnp.float32,
            )
            outs.append((top, total, weighted_part))
        part_max = jnp.stack([o[0] for o in outs], axis=1)
        part_sum = jnp.stack([o[1] for o in outs], axis=1)
        part_weighted = jnp.stack([o[2] for o in outs], axis=1)
        return (part_max, part_sum, part_weighted)

    row_max, row_sum, weighted = lax.map(one_group, jnp.arange(local_groups, dtype=jnp.int32))
    row_max = row_max.reshape(count_of_rows, KEY_VALUE_HEADS, head_groups)
    row_sum = row_sum.reshape(count_of_rows, KEY_VALUE_HEADS, head_groups)
    weighted = weighted.reshape(count_of_rows, KEY_VALUE_HEADS, head_groups, HEAD_SIZE)
    row_max, row_sum, weighted = merged((row_max, row_sum, weighted), "tp", merge_parts)
    attended = (
        (weighted / row_sum[..., None])
        .reshape(count_of_rows, QUERY_HEADS * HEAD_SIZE)
        .astype(jnp.bfloat16)
    )
    resid = tokens.astype(jnp.float32) + jnp.dot(
        attended, out_weight, preferred_element_type=jnp.float32
    )
    mid_squares = tp_sum(jnp.sum(resid * resid, axis=1))
    normed = (resid * lax.rsqrt(mid_squares / full_width + EPSILON)[:, None] * norm_gain).astype(
        jnp.bfloat16
    )
    top_count = route_ids.shape[1]
    half_count = lax.axis_size("el")
    experts = half_count
    capacity = count_of_rows * top_count * 2 // experts
    buffer_len = experts * capacity
    flat_ids = route_ids.reshape(-1)
    expert_onehot = (flat_ids[:, None] == jnp.arange(experts, dtype=jnp.int32)[None, :]).astype(
        jnp.int32
    )
    assign_iota = jnp.arange(flat_ids.shape[0], dtype=jnp.int32)
    earlier = (assign_iota[None, :] < assign_iota[:, None]).astype(jnp.bfloat16)
    before = jnp.dot(
        earlier, expert_onehot.astype(jnp.bfloat16), preferred_element_type=jnp.float32
    ).astype(jnp.int32)
    expert_rank = jnp.sum(before * expert_onehot, axis=1)
    my_half = lax.axis_index("el")
    target = (relative(flat_ids, my_half, half_count) * capacity + expert_rank).reshape(
        count_of_rows, top_count
    )
    slot_iota = jnp.arange(buffer_len, dtype=jnp.int32)
    hits = target[None, :, :] == slot_iota[:, None, None]
    dispatch = jnp.any(hits, axis=2).astype(jnp.bfloat16)
    outgoing = jnp.dot(dispatch, normed, preferred_element_type=jnp.float32).astype(jnp.bfloat16)
    arrived = exchange(outgoing.reshape(experts, capacity, feat_part), half_count)
    flat_rows = lax.optimization_barrier(arrived.reshape(buffer_len, feat_part))
    group_rows = buffer_len // 2
    summed = jnp.concatenate(
        [
            expert_block(
                flat_rows[start : start + group_rows], gate_w[0], up_w[0], down_w[0]
            )
            for start in (0, group_rows)
        ],
        axis=0,
    )
    returned = exchange(summed.reshape(experts, capacity, feat_part), half_count).reshape(
        buffer_len, feat_part
    )
    combine = jnp.sum(
        jnp.where(
            target[:, :, None] == slot_iota[None, None, :],
            route_weights[:, :, None],
            0.0,
        ),
        axis=1,
    )
    branch = jnp.dot(
        combine,
        returned.astype(jnp.float32),
        precision=lax.Precision.HIGHEST,
        preferred_element_type=jnp.float32,
    )
    mixed_rows = resid + branch
    out_squares = tp_sum(jnp.sum(mixed_rows * mixed_rows, axis=1))
    return (
        mixed_rows * lax.rsqrt(out_squares / full_width + EPSILON)[:, None] * final_gain
    ).astype(jnp.bfloat16)


def solution(mesh):
    ep_count, tp_count = mesh.devices.shape
    halves = Mesh(mesh.devices.reshape(2, ep_count // 2, tp_count), ("eh", "el", "tp"))
    ep = ("eh", "el")
    placed = (
        P(ep, "tp"),
        P(ep, None),
        P(ep, "tp", None, None, None),
        P(ep, None),
        P(ep, None),
        P(ep, None),
        P(None, "tp"),
        P("tp"),
        P(ep, None),
        P(ep, None),
        P(ep, None, "tp"),
        P(ep, None, "tp"),
        P(ep, "tp", None),
        P("tp"),
    )
    inner = jax.shard_map(
        shards, mesh=halves, in_specs=placed, out_specs=P(ep, "tp"), check_vma=False
    )
    result_sharding = NamedSharding(mesh, P("ep", "tp"))

    def run(*args):
        return lax.with_sharding_constraint(inner(*args), result_sharding)

    return run
```

```python
import jax
import jax.numpy as jnp
from jax import lax
from jax.sharding import Mesh, NamedSharding, PartitionSpec as P

QUERY_HEADS = 12
KEY_VALUE_HEADS = 2
HEAD_SIZE = 128
PAGE_POSITIONS = 16


EPSILON = 1e-06


def merged(shard, axis, join):
    if lax.axis_size(axis) == 2:
        rounded = jax.tree.map(lambda a: a.astype(jnp.bfloat16), shard)
        other = jax.tree.map(lambda a: lax.ppermute(a, axis, perm=[(0, 1), (1, 0)]), rounded)
        widen = lambda tree: jax.tree.map(lambda a, own: a.astype(own.dtype), tree, shard)
        return join(widen(rounded), widen(other))
    gathered = jax.tree.map(
        lambda a, kind: lax.all_gather(a.astype(kind), axis),
        shard,
        (jnp.bfloat16, jnp.bfloat16, jnp.bfloat16),
    )

    def take(source):
        return jax.tree.map(
            lambda a, own: lax.dynamic_index_in_dim(a, source, 0, False).astype(own.dtype),
            gathered,
            shard,
        )

    return lax.fori_loop(
        1, lax.axis_size(axis), lambda source, state: join(state, take(source)), take(0)
    )


def relative(expert, me, count):
    if count & (count - 1) == 0:
        return jnp.bitwise_xor(expert, me)
    return (expert - me) % count


def exchange(chunks, count):
    pieces = [chunks[0]]
    for step in range(1, count):
        if count & (count - 1) == 0:
            pairs = [(i, i ^ step) for i in range(count)]
        else:
            pairs = [(i, (i + step) % count) for i in range(count)]
        pieces.append(lax.ppermute(chunks[step], "el", perm=pairs))
    return jnp.stack(pieces)


def expert_block(rows, gate_w, up_w, down_w):
    feat_part = rows.shape[1]
    if lax.axis_size("tp") != 2:
        inputs = lax.all_gather(rows, "tp", axis=1, tiled=True)
        gate_value = jnp.dot(inputs, gate_w, preferred_element_type=jnp.float32)
        up_value = jnp.dot(inputs, up_w, preferred_element_type=jnp.float32)
        hidden = (jnp.maximum(gate_value, 0.0) * up_value).astype(jnp.bfloat16)
        partial_value = jnp.dot(hidden, down_w, preferred_element_type=jnp.float32)
        return lax.psum_scatter(
            partial_value.astype(jnp.bfloat16), "tp", scatter_dimension=1, tiled=True
        )
    swap = [(0, 1), (1, 0)]
    mine = lax.axis_index("tp")
    other = 1 - mine
    rows_other = lax.ppermute(rows, "tp", perm=swap)
    gate_parts = gate_w.reshape(2, feat_part, gate_w.shape[1])
    up_parts = up_w.reshape(2, feat_part, up_w.shape[1])

    def half_product(parts, x, which):
        weight = lax.dynamic_index_in_dim(parts, which, 0, keepdims=False)
        return jnp.dot(x, weight, preferred_element_type=jnp.float32)

    gate_value = half_product(gate_parts, rows, mine) + half_product(gate_parts, rows_other, other)
    up_value = half_product(up_parts, rows, mine) + half_product(up_parts, rows_other, other)
    hidden = (jnp.maximum(gate_value, 0.0) * up_value).astype(jnp.bfloat16)

    def down_product(which):
        weight = lax.dynamic_slice_in_dim(down_w, which * feat_part, feat_part, axis=1)
        return jnp.dot(hidden, weight, preferred_element_type=jnp.float32).astype(jnp.bfloat16)

    sent = lax.ppermute(down_product(other), "tp", perm=swap)
    kept = lax.optimization_barrier(down_product(mine))
    return (kept.astype(jnp.float32) + sent.astype(jnp.float32)).astype(jnp.bfloat16)


def tp_sum(value):
    if lax.axis_size("tp") != 2:
        return lax.psum(value, "tp")
    return value + lax.ppermute(value, "tp", perm=[(0, 1), (1, 0)])


def tp_gather(part, axis):
    if lax.axis_size("tp") != 2:
        return lax.all_gather(part, "tp", axis=axis, tiled=True)
    other = lax.ppermute(part, "tp", perm=[(0, 1), (1, 0)])
    first = lax.axis_index("tp") == 0
    low = jnp.where(first, part, other)
    high = jnp.where(first, other, part)
    return jnp.concatenate([low, high], axis=axis)


def tp_scatter_sum(full, axis):
    if lax.axis_size("tp") != 2:
        return lax.psum_scatter(full, "tp", scatter_dimension=axis, tiled=True)
    low, high = jnp.split(full, 2, axis=axis)
    first = lax.axis_index("tp") == 0
    keep = jnp.where(first, low, high)
    send = jnp.where(first, high, low)
    other = lax.ppermute(send, "tp", perm=[(0, 1), (1, 0)])
    return (keep.astype(jnp.float32) + other.astype(jnp.float32)).astype(full.dtype)


def merge_parts(first, second):
    joint_max = jnp.maximum(first[0], second[0])
    scale_first = jnp.exp(first[0] - joint_max)
    scale_second = jnp.exp(second[0] - joint_max)
    return (
        joint_max,
        first[1] * scale_first + second[1] * scale_second,
        first[2] * scale_first[..., None] + second[2] * scale_second[..., None],
    )


def shards(
    tokens,
    queries,
    kv_cache,
    page_table,
    query_lens,
    past_lens,
    out_weight,
    norm_gain,
    route_ids,
    route_weights,
    gate_w,
    up_w,
    down_w,
    final_gain,
):
    tp_index = lax.axis_index("tp")
    tp_count = lax.axis_size("tp")
    count_of_rows, feat_part = tokens.shape
    full_width = feat_part * tp_count
    local_groups = query_lens.shape[0]
    req_count = query_lens.shape[1]
    group_rows = count_of_rows // local_groups
    head_groups = QUERY_HEADS // KEY_VALUE_HEADS
    per_device = page_table.shape[1] // tp_count

    def one_group(local):
        query_count = lax.dynamic_index_in_dim(query_lens, local, 0, keepdims=False)
        past_count = lax.dynamic_index_in_dim(past_lens, local, 0, keepdims=False)
        req_iota = jnp.arange(req_count, dtype=jnp.int32)
        row_ends = jnp.sum(
            jnp.where(req_iota[None, :] <= req_iota[:, None], query_count[None, :], 0), axis=1
        )
        row_starts = row_ends - query_count
        row_iota = jnp.arange(group_rows, dtype=jnp.int32)
        row_req = jnp.sum((row_iota[:, None] >= row_ends[None, :]).astype(jnp.int32), axis=1)
        req_onehot = (row_req[:, None] == jnp.arange(req_count, dtype=jnp.int32)[None, :]).astype(
            jnp.int32
        )
        row_pos = row_iota + jnp.sum(req_onehot * (past_count - row_starts)[None, :], axis=1)
        local_table = lax.dynamic_index_in_dim(
            page_table.reshape(req_count, per_device, tp_count), tp_index, axis=2, keepdims=False
        )
        group_pages = lax.dynamic_index_in_dim(kv_cache, local, 0, keepdims=False)[0]
        page_row_block = group_pages[local_table.reshape(-1)]
        key_count_total = page_row_block.shape[0] * PAGE_POSITIONS
        flattened_cache = page_row_block.reshape(key_count_total, 2 * KEY_VALUE_HEADS * HEAD_SIZE)
        gathered_keys = flattened_cache[:, : KEY_VALUE_HEADS * HEAD_SIZE].reshape(
            key_count_total, KEY_VALUE_HEADS, HEAD_SIZE
        )
        gathered_values = flattened_cache[:, KEY_VALUE_HEADS * HEAD_SIZE :].reshape(
            key_count_total, KEY_VALUE_HEADS, HEAD_SIZE
        )
        key_iota = jnp.arange(key_count_total, dtype=jnp.int32)
        key_req = key_iota // (per_device * PAGE_POSITIONS)
        within = key_iota % (per_device * PAGE_POSITIONS)
        key_pos = (
            within // PAGE_POSITIONS * tp_count + tp_index
        ) * PAGE_POSITIONS + within % PAGE_POSITIONS
        allowed = (row_req[:, None] == key_req[None, :]) & (key_pos[None, :] <= row_pos[:, None])
        score_mask = allowed[:, None, :]
        outs = []
        for kv_head in range(KEY_VALUE_HEADS):
            head_rows = queries[:, kv_head * head_groups * HEAD_SIZE : (kv_head + 1) * head_groups * HEAD_SIZE]
            head_rows = head_rows.reshape(group_rows, head_groups, HEAD_SIZE)
            head_keys = flattened_cache[:, kv_head * HEAD_SIZE : (kv_head + 1) * HEAD_SIZE]
            head_values = flattened_cache[
                :, (KEY_VALUE_HEADS + kv_head) * HEAD_SIZE : (KEY_VALUE_HEADS + kv_head + 1) * HEAD_SIZE
            ]
            scores = jnp.einsum(
                "rgd,ld->rgl", head_rows, head_keys, preferred_element_type=jnp.float32
            ) * HEAD_SIZE ** (-0.5)
            top = jnp.max(jnp.where(score_mask, scores, -1e30), axis=-1)
            soft = jnp.where(score_mask, jnp.exp(scores - top[..., None]), 0.0)
            total = jnp.sum(soft, axis=-1)
            weighted_part = jnp.einsum(
                "rgl,ld->rgd",
                soft.astype(jnp.bfloat16),
                head_values,
                preferred_element_type=jnp.float32,
            )
            outs.append((top, total, weighted_part))
        part_max = jnp.stack([o[0] for o in outs], axis=1)
        part_sum = jnp.stack([o[1] for o in outs], axis=1)
        part_weighted = jnp.stack([o[2] for o in outs], axis=1)
        return (part_max, part_sum, part_weighted)

    row_max, row_sum, weighted = lax.map(one_group, jnp.arange(local_groups, dtype=jnp.int32))
    row_max = row_max.reshape(count_of_rows, KEY_VALUE_HEADS, head_groups)
    row_sum = row_sum.reshape(count_of_rows, KEY_VALUE_HEADS, head_groups)
    weighted = weighted.reshape(count_of_rows, KEY_VALUE_HEADS, head_groups, HEAD_SIZE)
    row_max, row_sum, weighted = merged((row_max, row_sum, weighted), "tp", merge_parts)
    attended = (
        (weighted / row_sum[..., None])
        .reshape(count_of_rows, QUERY_HEADS * HEAD_SIZE)
        .astype(jnp.bfloat16)
    )
    resid = tokens.astype(jnp.float32) + jnp.dot(
        attended, out_weight, preferred_element_type=jnp.float32
    )
    mid_squares = tp_sum(jnp.sum(resid * resid, axis=1))
    normed = (resid * lax.rsqrt(mid_squares / full_width + EPSILON)[:, None] * norm_gain).astype(
        jnp.bfloat16
    )
    top_count = route_ids.shape[1]
    half_count = lax.axis_size("el")
    experts = half_count
    capacity = count_of_rows * top_count * 2 // experts
    buffer_len = experts * capacity
    flat_ids = route_ids.reshape(-1)
    expert_onehot = (flat_ids[:, None] == jnp.arange(experts, dtype=jnp.int32)[None, :]).astype(
        jnp.int32
    )
    assign_iota = jnp.arange(flat_ids.shape[0], dtype=jnp.int32)
    earlier = (assign_iota[None, :] < assign_iota[:, None]).astype(jnp.bfloat16)
    before = jnp.dot(
        earlier, expert_onehot.astype(jnp.bfloat16), preferred_element_type=jnp.float32
    ).astype(jnp.int32)
    expert_rank = jnp.sum(before * expert_onehot, axis=1)
    my_half = lax.axis_index("el")
    target = (relative(flat_ids, my_half, half_count) * capacity + expert_rank).reshape(
        count_of_rows, top_count
    )
    slot_iota = jnp.arange(buffer_len, dtype=jnp.int32)
    hits = target[None, :, :] == slot_iota[:, None, None]
    dispatch = jnp.any(hits, axis=2).astype(jnp.bfloat16)
    outgoing = jnp.dot(dispatch, normed, preferred_element_type=jnp.float32).astype(jnp.bfloat16)
    arrived = exchange(outgoing.reshape(experts, capacity, feat_part), half_count)
    flat_rows = lax.optimization_barrier(arrived.reshape(buffer_len, feat_part))
    group_rows = buffer_len // 2
    first_done = expert_block(flat_rows[:group_rows], gate_w[0], up_w[0], down_w[0])
    first_done, second_rows = lax.optimization_barrier((first_done, flat_rows[group_rows:]))
    second_done = expert_block(second_rows, gate_w[0], up_w[0], down_w[0])
    per_group = group_rows // capacity
    result_chunks = [
        done[index * capacity : (index + 1) * capacity]
        for done in (first_done, second_done)
        for index in range(per_group)
    ]
    returned = exchange(result_chunks, half_count).reshape(buffer_len, feat_part)
    combine = jnp.sum(
        jnp.where(
            target[:, :, None] == slot_iota[None, None, :],
            route_weights[:, :, None],
            0.0,
        ),
        axis=1,
    )
    branch = jnp.dot(
        combine,
        returned.astype(jnp.float32),
        precision=lax.Precision.HIGHEST,
        preferred_element_type=jnp.float32,
    )
    mixed_rows = resid + branch
    out_squares = tp_sum(jnp.sum(mixed_rows * mixed_rows, axis=1))
    return (
        mixed_rows * lax.rsqrt(out_squares / full_width + EPSILON)[:, None] * final_gain
    ).astype(jnp.bfloat16)


def solution(mesh):
    ep_count, tp_count = mesh.devices.shape
    halves = Mesh(mesh.devices.reshape(2, ep_count // 2, tp_count), ("eh", "el", "tp"))
    ep = ("eh", "el")
    placed = (
        P(ep, "tp"),
        P(ep, None),
        P(ep, "tp", None, None, None),
        P(ep, None),
        P(ep, None),
        P(ep, None),
        P(None, "tp"),
        P("tp"),
        P(ep, None),
        P(ep, None),
        P(ep, None, "tp"),
        P(ep, None, "tp"),
        P(ep, "tp", None),
        P("tp"),
    )
    inner = jax.shard_map(
        shards, mesh=halves, in_specs=placed, out_specs=P(ep, "tp"), check_vma=False
    )
    result_sharding = NamedSharding(mesh, P("ep", "tp"))

    def run(*args):
        return lax.with_sharding_constraint(inner(*args), result_sharding)

    return run
```

```python
import jax
import jax.numpy as jnp
from jax import lax
from jax.sharding import Mesh, NamedSharding, PartitionSpec as P

QUERY_HEADS = 12
KEY_VALUE_HEADS = 2
HEAD_SIZE = 128
PAGE_POSITIONS = 16


EPSILON = 1e-06


def merged(shard, axis, join):
    if lax.axis_size(axis) == 2:
        rounded = jax.tree.map(lambda a: a.astype(jnp.bfloat16), shard)
        other = jax.tree.map(lambda a: lax.ppermute(a, axis, perm=[(0, 1), (1, 0)]), rounded)
        widen = lambda tree: jax.tree.map(lambda a, own: a.astype(own.dtype), tree, shard)
        return join(widen(rounded), widen(other))
    gathered = jax.tree.map(
        lambda a, kind: lax.all_gather(a.astype(kind), axis),
        shard,
        (jnp.bfloat16, jnp.bfloat16, jnp.bfloat16),
    )

    def take(source):
        return jax.tree.map(
            lambda a, own: lax.dynamic_index_in_dim(a, source, 0, False).astype(own.dtype),
            gathered,
            shard,
        )

    return lax.fori_loop(
        1, lax.axis_size(axis), lambda source, state: join(state, take(source)), take(0)
    )


def relative(expert, me, count):
    if count & (count - 1) == 0:
        return jnp.bitwise_xor(expert, me)
    return (expert - me) % count


def exchange(chunks, count):
    pieces = [chunks[0]]
    for step in range(1, count):
        if count & (count - 1) == 0:
            pairs = [(i, i ^ step) for i in range(count)]
        else:
            pairs = [(i, (i + step) % count) for i in range(count)]
        pieces.append(lax.ppermute(chunks[step], "el", perm=pairs))
    return jnp.stack(pieces)


def expert_block(rows, gate_w, up_w, down_w):
    feat_part = rows.shape[1]
    if lax.axis_size("tp") != 2:
        inputs = lax.all_gather(rows, "tp", axis=1, tiled=True)
        gate_value = jnp.dot(inputs, gate_w, preferred_element_type=jnp.float32)
        up_value = jnp.dot(inputs, up_w, preferred_element_type=jnp.float32)
        hidden = (jnp.maximum(gate_value, 0.0) * up_value).astype(jnp.bfloat16)
        partial_value = jnp.dot(hidden, down_w, preferred_element_type=jnp.float32)
        return lax.psum_scatter(
            partial_value.astype(jnp.bfloat16), "tp", scatter_dimension=1, tiled=True
        )
    swap = [(0, 1), (1, 0)]
    mine = lax.axis_index("tp")
    other = 1 - mine
    rows_other = lax.ppermute(rows, "tp", perm=swap)
    gate_parts = gate_w.reshape(2, feat_part, gate_w.shape[1])
    up_parts = up_w.reshape(2, feat_part, up_w.shape[1])

    def half_product(parts, x, which):
        weight = lax.dynamic_index_in_dim(parts, which, 0, keepdims=False)
        return jnp.dot(x, weight, preferred_element_type=jnp.float32)

    gate_value = half_product(gate_parts, rows, mine) + half_product(gate_parts, rows_other, other)
    up_value = half_product(up_parts, rows, mine) + half_product(up_parts, rows_other, other)
    hidden = (jnp.maximum(gate_value, 0.0) * up_value).astype(jnp.bfloat16)

    def down_product(which):
        weight = lax.dynamic_slice_in_dim(down_w, which * feat_part, feat_part, axis=1)
        return jnp.dot(hidden, weight, preferred_element_type=jnp.float32).astype(jnp.bfloat16)

    sent = lax.ppermute(down_product(other), "tp", perm=swap)
    kept = lax.optimization_barrier(down_product(mine))
    return (kept.astype(jnp.float32) + sent.astype(jnp.float32)).astype(jnp.bfloat16)


def tp_sum(value):
    if lax.axis_size("tp") != 2:
        return lax.psum(value, "tp")
    return value + lax.ppermute(value, "tp", perm=[(0, 1), (1, 0)])


def tp_gather(part, axis):
    if lax.axis_size("tp") != 2:
        return lax.all_gather(part, "tp", axis=axis, tiled=True)
    other = lax.ppermute(part, "tp", perm=[(0, 1), (1, 0)])
    first = lax.axis_index("tp") == 0
    low = jnp.where(first, part, other)
    high = jnp.where(first, other, part)
    return jnp.concatenate([low, high], axis=axis)


def tp_scatter_sum(full, axis):
    if lax.axis_size("tp") != 2:
        return lax.psum_scatter(full, "tp", scatter_dimension=axis, tiled=True)
    low, high = jnp.split(full, 2, axis=axis)
    first = lax.axis_index("tp") == 0
    keep = jnp.where(first, low, high)
    send = jnp.where(first, high, low)
    other = lax.ppermute(send, "tp", perm=[(0, 1), (1, 0)])
    return (keep.astype(jnp.float32) + other.astype(jnp.float32)).astype(full.dtype)


def merge_parts(first, second):
    joint_max = jnp.maximum(first[0], second[0])
    scale_first = jnp.exp(first[0] - joint_max)
    scale_second = jnp.exp(second[0] - joint_max)
    return (
        joint_max,
        first[1] * scale_first + second[1] * scale_second,
        first[2] * scale_first[..., None] + second[2] * scale_second[..., None],
    )


def shards(
    tokens,
    queries,
    kv_cache,
    page_table,
    query_lens,
    past_lens,
    out_weight,
    norm_gain,
    route_ids,
    route_weights,
    gate_w,
    up_w,
    down_w,
    final_gain,
):
    tp_index = lax.axis_index("tp")
    tp_count = lax.axis_size("tp")
    count_of_rows, feat_part = tokens.shape
    full_width = feat_part * tp_count
    local_groups = query_lens.shape[0]
    req_count = query_lens.shape[1]
    group_rows = count_of_rows // local_groups
    head_groups = QUERY_HEADS // KEY_VALUE_HEADS
    per_device = page_table.shape[1] // tp_count

    def one_group(local):
        query_count = lax.dynamic_index_in_dim(query_lens, local, 0, keepdims=False)
        past_count = lax.dynamic_index_in_dim(past_lens, local, 0, keepdims=False)
        req_iota = jnp.arange(req_count, dtype=jnp.int32)
        row_ends = jnp.sum(
            jnp.where(req_iota[None, :] <= req_iota[:, None], query_count[None, :], 0), axis=1
        )
        row_starts = row_ends - query_count
        row_iota = jnp.arange(group_rows, dtype=jnp.int32)
        row_req = jnp.sum((row_iota[:, None] >= row_ends[None, :]).astype(jnp.int32), axis=1)
        req_onehot = (row_req[:, None] == jnp.arange(req_count, dtype=jnp.int32)[None, :]).astype(
            jnp.int32
        )
        row_pos = row_iota + jnp.sum(req_onehot * (past_count - row_starts)[None, :], axis=1)
        local_table = page_table[:, 0::tp_count]
        for other in range(1, tp_count):
            local_table = jnp.where(tp_index == other, page_table[:, other::tp_count], local_table)
        group_pages = lax.dynamic_index_in_dim(kv_cache, local, 0, keepdims=False)[0]
        page_row_block = group_pages[local_table.reshape(-1)]
        key_count_total = page_row_block.shape[0] * PAGE_POSITIONS
        flattened_cache = page_row_block.reshape(key_count_total, 2 * KEY_VALUE_HEADS * HEAD_SIZE)
        gathered_keys = flattened_cache[:, : KEY_VALUE_HEADS * HEAD_SIZE].reshape(
            key_count_total, KEY_VALUE_HEADS, HEAD_SIZE
        )
        gathered_values = flattened_cache[:, KEY_VALUE_HEADS * HEAD_SIZE :].reshape(
            key_count_total, KEY_VALUE_HEADS, HEAD_SIZE
        )
        key_iota = jnp.arange(key_count_total, dtype=jnp.int32)
        key_req = key_iota // (per_device * PAGE_POSITIONS)
        within = key_iota % (per_device * PAGE_POSITIONS)
        key_pos = (
            within // PAGE_POSITIONS * tp_count + tp_index
        ) * PAGE_POSITIONS + within % PAGE_POSITIONS
        allowed = (row_req[:, None] == key_req[None, :]) & (key_pos[None, :] <= row_pos[:, None])
        score_mask = allowed[:, None, :]
        outs = []
        for kv_head in range(KEY_VALUE_HEADS):
            head_rows = queries[:, kv_head * head_groups * HEAD_SIZE : (kv_head + 1) * head_groups * HEAD_SIZE]
            head_rows = head_rows.reshape(group_rows, head_groups, HEAD_SIZE)
            head_keys = flattened_cache[:, kv_head * HEAD_SIZE : (kv_head + 1) * HEAD_SIZE]
            head_values = flattened_cache[
                :, (KEY_VALUE_HEADS + kv_head) * HEAD_SIZE : (KEY_VALUE_HEADS + kv_head + 1) * HEAD_SIZE
            ]
            scores = jnp.einsum(
                "rgd,ld->rgl", head_rows, head_keys, preferred_element_type=jnp.float32
            ) * HEAD_SIZE ** (-0.5)
            top = jnp.max(jnp.where(score_mask, scores, -1e30), axis=-1)
            soft = jnp.where(score_mask, jnp.exp(scores - top[..., None]), 0.0)
            total = jnp.sum(soft, axis=-1)
            weighted_part = jnp.einsum(
                "rgl,ld->rgd",
                soft.astype(jnp.bfloat16),
                head_values,
                preferred_element_type=jnp.float32,
            )
            outs.append((top, total, weighted_part))
        part_max = jnp.stack([o[0] for o in outs], axis=1)
        part_sum = jnp.stack([o[1] for o in outs], axis=1)
        part_weighted = jnp.stack([o[2] for o in outs], axis=1)
        return (part_max, part_sum, part_weighted)

    row_max, row_sum, weighted = lax.map(one_group, jnp.arange(local_groups, dtype=jnp.int32))
    row_max = row_max.reshape(count_of_rows, KEY_VALUE_HEADS, head_groups)
    row_sum = row_sum.reshape(count_of_rows, KEY_VALUE_HEADS, head_groups)
    weighted = weighted.reshape(count_of_rows, KEY_VALUE_HEADS, head_groups, HEAD_SIZE)
    row_max, row_sum, weighted = merged((row_max, row_sum, weighted), "tp", merge_parts)
    attended = (
        (weighted / row_sum[..., None])
        .reshape(count_of_rows, QUERY_HEADS * HEAD_SIZE)
        .astype(jnp.bfloat16)
    )
    resid = tokens.astype(jnp.float32) + jnp.dot(
        attended, out_weight, preferred_element_type=jnp.float32
    )
    mid_squares = tp_sum(jnp.sum(resid * resid, axis=1))
    normed = (resid * lax.rsqrt(mid_squares / full_width + EPSILON)[:, None] * norm_gain).astype(
        jnp.bfloat16
    )
    top_count = route_ids.shape[1]
    half_count = lax.axis_size("el")
    experts = half_count
    capacity = count_of_rows * top_count * 2 // experts
    buffer_len = experts * capacity
    flat_ids = route_ids.reshape(-1)
    expert_onehot = (flat_ids[:, None] == jnp.arange(experts, dtype=jnp.int32)[None, :]).astype(
        jnp.int32
    )
    assign_iota = jnp.arange(flat_ids.shape[0], dtype=jnp.int32)
    earlier = (assign_iota[None, :] < assign_iota[:, None]).astype(jnp.bfloat16)
    before = jnp.dot(
        earlier, expert_onehot.astype(jnp.bfloat16), preferred_element_type=jnp.float32
    ).astype(jnp.int32)
    expert_rank = jnp.sum(before * expert_onehot, axis=1)
    my_half = lax.axis_index("el")
    target = (relative(flat_ids, my_half, half_count) * capacity + expert_rank).reshape(
        count_of_rows, top_count
    )
    slot_iota = jnp.arange(buffer_len, dtype=jnp.int32)
    hits = target[None, :, :] == slot_iota[:, None, None]
    dispatch = jnp.any(hits, axis=2).astype(jnp.bfloat16)
    outgoing = jnp.dot(dispatch, normed, preferred_element_type=jnp.float32).astype(jnp.bfloat16)
    arrived = exchange(outgoing.reshape(experts, capacity, feat_part), half_count)
    flat_rows = lax.optimization_barrier(arrived.reshape(buffer_len, feat_part))
    group_rows = buffer_len // 2
    summed = jnp.concatenate(
        [
            expert_block(
                flat_rows[start : start + group_rows], gate_w[0], up_w[0], down_w[0]
            )
            for start in (0, group_rows)
        ],
        axis=0,
    )
    returned = exchange(summed.reshape(experts, capacity, feat_part), half_count).reshape(
        buffer_len, feat_part
    )
    combine = jnp.sum(
        jnp.where(
            target[:, :, None] == slot_iota[None, None, :],
            route_weights[:, :, None],
            0.0,
        ),
        axis=1,
    )
    branch = jnp.dot(
        combine,
        returned.astype(jnp.float32),
        precision=lax.Precision.HIGHEST,
        preferred_element_type=jnp.float32,
    )
    mixed_rows = resid + branch
    out_squares = tp_sum(jnp.sum(mixed_rows * mixed_rows, axis=1))
    return (
        mixed_rows * lax.rsqrt(out_squares / full_width + EPSILON)[:, None] * final_gain
    ).astype(jnp.bfloat16)


def solution(mesh):
    ep_count, tp_count = mesh.devices.shape
    halves = Mesh(mesh.devices.reshape(2, ep_count // 2, tp_count), ("eh", "el", "tp"))
    ep = ("eh", "el")
    placed = (
        P(ep, "tp"),
        P(ep, None),
        P(ep, "tp", None, None, None),
        P(ep, None),
        P(ep, None),
        P(ep, None),
        P(None, "tp"),
        P("tp"),
        P(ep, None),
        P(ep, None),
        P(ep, None, "tp"),
        P(ep, None, "tp"),
        P(ep, "tp", None),
        P("tp"),
    )
    inner = jax.shard_map(
        shards, mesh=halves, in_specs=placed, out_specs=P(ep, "tp"), check_vma=False
    )
    result_sharding = NamedSharding(mesh, P("ep", "tp"))

    def run(*args):
        return lax.with_sharding_constraint(inner(*args), result_sharding)

    return run
```

```python
import jax
import jax.numpy as jnp
from jax import lax
from jax.sharding import Mesh, NamedSharding, PartitionSpec as P

QUERY_HEADS = 12
KEY_VALUE_HEADS = 2
HEAD_SIZE = 128
PAGE_POSITIONS = 16


EPSILON = 1e-06


def merged(shard, axis, join):
    if lax.axis_size(axis) == 2:
        rounded = jax.tree.map(lambda a: a.astype(jnp.bfloat16), shard)
        other = jax.tree.map(lambda a: lax.ppermute(a, axis, perm=[(0, 1), (1, 0)]), rounded)
        widen = lambda tree: jax.tree.map(lambda a, own: a.astype(own.dtype), tree, shard)
        return join(widen(rounded), widen(other))
    gathered = jax.tree.map(
        lambda a, kind: lax.all_gather(a.astype(kind), axis),
        shard,
        (jnp.bfloat16, jnp.bfloat16, jnp.bfloat16),
    )

    def take(source):
        return jax.tree.map(
            lambda a, own: lax.dynamic_index_in_dim(a, source, 0, False).astype(own.dtype),
            gathered,
            shard,
        )

    return lax.fori_loop(
        1, lax.axis_size(axis), lambda source, state: join(state, take(source)), take(0)
    )


def relative(expert, me, count):
    if count & (count - 1) == 0:
        return jnp.bitwise_xor(expert, me)
    return (expert - me) % count


def exchange(chunks, count):
    pieces = [chunks[0]]
    for step in range(1, count):
        if count & (count - 1) == 0:
            pairs = [(i, i ^ step) for i in range(count)]
        else:
            pairs = [(i, (i + step) % count) for i in range(count)]
        pieces.append(lax.ppermute(chunks[step], "el", perm=pairs))
    return jnp.stack(pieces)


def expert_block(rows, gate_w, up_w, down_w):
    feat_part = rows.shape[1]
    if lax.axis_size("tp") != 2:
        inputs = lax.all_gather(rows, "tp", axis=1, tiled=True)
        gate_value = jnp.dot(inputs, gate_w, preferred_element_type=jnp.float32)
        up_value = jnp.dot(inputs, up_w, preferred_element_type=jnp.float32)
        hidden = (jnp.maximum(gate_value, 0.0) * up_value).astype(jnp.bfloat16)
        partial_value = jnp.dot(hidden, down_w, preferred_element_type=jnp.float32)
        return lax.psum_scatter(
            partial_value.astype(jnp.bfloat16), "tp", scatter_dimension=1, tiled=True
        )
    swap = [(0, 1), (1, 0)]
    mine = lax.axis_index("tp")
    other = 1 - mine
    rows_other = lax.ppermute(rows, "tp", perm=swap)
    gate_parts = gate_w.reshape(2, feat_part, gate_w.shape[1])
    up_parts = up_w.reshape(2, feat_part, up_w.shape[1])

    def half_product(parts, x, which):
        weight = lax.dynamic_index_in_dim(parts, which, 0, keepdims=False)
        return jnp.dot(x, weight, preferred_element_type=jnp.float32)

    gate_value = half_product(gate_parts, rows, mine) + half_product(gate_parts, rows_other, other)
    up_value = half_product(up_parts, rows, mine) + half_product(up_parts, rows_other, other)
    hidden = (jnp.maximum(gate_value, 0.0) * up_value).astype(jnp.bfloat16)

    def down_product(which):
        weight = lax.dynamic_slice_in_dim(down_w, which * feat_part, feat_part, axis=1)
        return jnp.dot(hidden, weight, preferred_element_type=jnp.float32).astype(jnp.bfloat16)

    sent = lax.ppermute(down_product(other), "tp", perm=swap)
    kept = lax.optimization_barrier(down_product(mine))
    return (kept.astype(jnp.float32) + sent.astype(jnp.float32)).astype(jnp.bfloat16)


def tp_sum(value):
    if lax.axis_size("tp") != 2:
        return lax.psum(value, "tp")
    return value + lax.ppermute(value, "tp", perm=[(0, 1), (1, 0)])


def tp_gather(part, axis):
    if lax.axis_size("tp") != 2:
        return lax.all_gather(part, "tp", axis=axis, tiled=True)
    other = lax.ppermute(part, "tp", perm=[(0, 1), (1, 0)])
    first = lax.axis_index("tp") == 0
    low = jnp.where(first, part, other)
    high = jnp.where(first, other, part)
    return jnp.concatenate([low, high], axis=axis)


def tp_scatter_sum(full, axis):
    if lax.axis_size("tp") != 2:
        return lax.psum_scatter(full, "tp", scatter_dimension=axis, tiled=True)
    low, high = jnp.split(full, 2, axis=axis)
    first = lax.axis_index("tp") == 0
    keep = jnp.where(first, low, high)
    send = jnp.where(first, high, low)
    other = lax.ppermute(send, "tp", perm=[(0, 1), (1, 0)])
    return (keep.astype(jnp.float32) + other.astype(jnp.float32)).astype(full.dtype)


def merge_parts(first, second):
    joint_max = jnp.maximum(first[0], second[0])
    scale_first = jnp.exp(first[0] - joint_max)
    scale_second = jnp.exp(second[0] - joint_max)
    return (
        joint_max,
        first[1] * scale_first + second[1] * scale_second,
        first[2] * scale_first[..., None] + second[2] * scale_second[..., None],
    )


def shards(
    tokens,
    queries,
    kv_cache,
    page_table,
    query_lens,
    past_lens,
    out_weight,
    norm_gain,
    route_ids,
    route_weights,
    gate_w,
    up_w,
    down_w,
    final_gain,
):
    tp_index = lax.axis_index("tp")
    tp_count = lax.axis_size("tp")
    count_of_rows, feat_part = tokens.shape
    full_width = feat_part * tp_count
    req_count = query_lens.shape[1]
    head_groups = QUERY_HEADS // KEY_VALUE_HEADS
    per_device = page_table.shape[1] // tp_count

    query_count = query_lens[0]
    past_count = past_lens[0]
    req_iota = jnp.arange(req_count, dtype=jnp.int32)
    row_ends = jnp.sum(
        jnp.where(req_iota[None, :] <= req_iota[:, None], query_count[None, :], 0), axis=1
    )
    row_starts = row_ends - query_count
    row_iota = jnp.arange(count_of_rows, dtype=jnp.int32)
    row_req = jnp.sum((row_iota[:, None] >= row_ends[None, :]).astype(jnp.int32), axis=1)
    req_onehot = (row_req[:, None] == req_iota[None, :]).astype(jnp.int32)
    row_pos = row_iota + jnp.sum(req_onehot * (past_count - row_starts)[None, :], axis=1)
    local_table = page_table[:, 0::tp_count]
    for other in range(1, tp_count):
        local_table = jnp.where(tp_index == other, page_table[:, other::tp_count], local_table)
    page_row_block = kv_cache[0, 0][local_table.reshape(-1)]
    key_count_total = page_row_block.shape[0] * PAGE_POSITIONS
    flattened_cache = page_row_block.reshape(key_count_total, 2 * KEY_VALUE_HEADS * HEAD_SIZE)
    key_iota = jnp.arange(key_count_total, dtype=jnp.int32)
    key_req = key_iota // (per_device * PAGE_POSITIONS)
    within = key_iota % (per_device * PAGE_POSITIONS)
    key_pos = (
        within // PAGE_POSITIONS * tp_count + tp_index
    ) * PAGE_POSITIONS + within % PAGE_POSITIONS
    allowed = (row_req[:, None] == key_req[None, :]) & (key_pos[None, :] <= row_pos[:, None])

    top_count = route_ids.shape[1]
    half_count = lax.axis_size("el")
    experts = half_count
    most = count_of_rows * top_count * 2 // experts
    chunk_count = 2 if count_of_rows % 16 == 0 else 1
    chunk_rows = count_of_rows // chunk_count
    capacity = min(most, chunk_rows)
    buffer_len = experts * capacity
    my_half = lax.axis_index("el")

    def attend(rows):
        score_mask = allowed[rows][:, None, :]
        chunk_queries = queries[rows]
        outs = []
        for kv_head in range(KEY_VALUE_HEADS):
            head_rows = chunk_queries[
                :, kv_head * head_groups * HEAD_SIZE : (kv_head + 1) * head_groups * HEAD_SIZE
            ].reshape(chunk_rows, head_groups, HEAD_SIZE)
            head_keys = flattened_cache[:, kv_head * HEAD_SIZE : (kv_head + 1) * HEAD_SIZE]
            head_values = flattened_cache[
                :, (KEY_VALUE_HEADS + kv_head) * HEAD_SIZE : (KEY_VALUE_HEADS + kv_head + 1) * HEAD_SIZE
            ]
            scores = jnp.einsum(
                "rgd,ld->rgl", head_rows, head_keys, preferred_element_type=jnp.float32
            ) * HEAD_SIZE ** (-0.5)
            top = jnp.max(jnp.where(score_mask, scores, -1e30), axis=-1)
            soft = jnp.where(score_mask, jnp.exp(scores - top[..., None]), 0.0)
            total = jnp.sum(soft, axis=-1)
            weighted_part = jnp.einsum(
                "rgl,ld->rgd",
                soft.astype(jnp.bfloat16),
                head_values,
                preferred_element_type=jnp.float32,
            )
            outs.append((top, total, weighted_part))
        row_max = jnp.stack([o[0] for o in outs], axis=1)
        row_sum = jnp.stack([o[1] for o in outs], axis=1)
        weighted = jnp.stack([o[2] for o in outs], axis=1)
        row_max, row_sum, weighted = merged((row_max, row_sum, weighted), "tp", merge_parts)
        attended = (
            (weighted / row_sum[..., None])
            .reshape(chunk_rows, QUERY_HEADS * HEAD_SIZE)
            .astype(jnp.bfloat16)
        )
        resid = tokens[rows].astype(jnp.float32) + jnp.dot(
            attended, out_weight, preferred_element_type=jnp.float32
        )
        mid_squares = tp_sum(jnp.sum(resid * resid, axis=1))
        normed = (
            resid * lax.rsqrt(mid_squares / full_width + EPSILON)[:, None] * norm_gain
        ).astype(jnp.bfloat16)
        return resid, normed

    def send_rows(rows, normed):
        flat_ids = route_ids[rows].reshape(-1)
        expert_onehot = (
            flat_ids[:, None] == jnp.arange(experts, dtype=jnp.int32)[None, :]
        ).astype(jnp.int32)
        assign_iota = jnp.arange(flat_ids.shape[0], dtype=jnp.int32)
        earlier = (assign_iota[None, :] < assign_iota[:, None]).astype(jnp.bfloat16)
        before = jnp.dot(
            earlier, expert_onehot.astype(jnp.bfloat16), preferred_element_type=jnp.float32
        ).astype(jnp.int32)
        expert_rank = jnp.sum(before * expert_onehot, axis=1)
        target = (relative(flat_ids, my_half, half_count) * capacity + expert_rank).reshape(
            chunk_rows, top_count
        )
        slot_iota = jnp.arange(buffer_len, dtype=jnp.int32)
        hits = target[None, :, :] == slot_iota[:, None, None]
        dispatch = jnp.any(hits, axis=2).astype(jnp.bfloat16)
        outgoing = jnp.dot(dispatch, normed, preferred_element_type=jnp.float32).astype(
            jnp.bfloat16
        )
        arrived = exchange(outgoing.reshape(experts, capacity, feat_part), half_count)
        return target, outgoing, arrived

    def expert_rows(arrived):
        flat_rows = lax.optimization_barrier(arrived.reshape(buffer_len, feat_part))
        return expert_block(flat_rows, gate_w[0], up_w[0], down_w[0])

    def finish(rows, resid, target, summed):
        slot_iota = jnp.arange(buffer_len, dtype=jnp.int32)
        returned = exchange(summed.reshape(experts, capacity, feat_part), half_count).reshape(
            buffer_len, feat_part
        )
        combine = jnp.sum(
            jnp.where(
                target[:, :, None] == slot_iota[None, None, :],
                route_weights[rows][:, :, None],
                0.0,
            ),
            axis=1,
        )
        branch = jnp.dot(
            combine,
            returned.astype(jnp.float32),
            precision=lax.Precision.HIGHEST,
            preferred_element_type=jnp.float32,
        )
        mixed_rows = resid + branch
        out_squares = tp_sum(jnp.sum(mixed_rows * mixed_rows, axis=1))
        return (
            mixed_rows * lax.rsqrt(out_squares / full_width + EPSILON)[:, None] * final_gain
        ).astype(jnp.bfloat16)

    if chunk_count == 1:
        rows = slice(0, count_of_rows)
        resid, normed = attend(rows)
        target, _, arrived = send_rows(rows, normed)
        return finish(rows, resid, target, expert_rows(arrived))
    first = slice(0, chunk_rows)
    second = slice(chunk_rows, count_of_rows)
    resid_a, normed_a = attend(first)
    target_a, outgoing_a, arrived_a = send_rows(first, normed_a)
    outgoing_a, queries = lax.optimization_barrier((outgoing_a, queries))
    resid_b, normed_b = attend(second)
    arrived_a, normed_b = lax.optimization_barrier((arrived_a, normed_b))
    summed_a = expert_rows(arrived_a)
    summed_a, normed_b = lax.optimization_barrier((summed_a, normed_b))
    target_b, _, arrived_b = send_rows(second, normed_b)
    summed_b = expert_rows(arrived_b)
    summed_a, summed_b = lax.optimization_barrier((summed_a, summed_b))
    return jnp.concatenate(
        [finish(first, resid_a, target_a, summed_a), finish(second, resid_b, target_b, summed_b)],
        axis=0,
    )


def solution(mesh):
    ep_count, tp_count = mesh.devices.shape
    halves = Mesh(mesh.devices.reshape(2, ep_count // 2, tp_count), ("eh", "el", "tp"))
    ep = ("eh", "el")
    placed = (
        P(ep, "tp"),
        P(ep, None),
        P(ep, "tp", None, None, None),
        P(ep, None),
        P(ep, None),
        P(ep, None),
        P(None, "tp"),
        P("tp"),
        P(ep, None),
        P(ep, None),
        P(ep, None, "tp"),
        P(ep, None, "tp"),
        P(ep, "tp", None),
        P("tp"),
    )
    inner = jax.shard_map(
        shards, mesh=halves, in_specs=placed, out_specs=P(ep, "tp"), check_vma=False
    )
    result_sharding = NamedSharding(mesh, P("ep", "tp"))

    def run(*args):
        return lax.with_sharding_constraint(inner(*args), result_sharding)

    return run
```

```python
import jax
import jax.numpy as jnp
from jax import lax
from jax.sharding import Mesh, NamedSharding, PartitionSpec as P

QUERY_HEADS = 12
KEY_VALUE_HEADS = 2
HEAD_SIZE = 128
PAGE_POSITIONS = 16


EPSILON = 1e-06


def merged(shard, axis, join):
    if lax.axis_size(axis) == 2:
        rounded = jax.tree.map(lambda a: a.astype(jnp.bfloat16), shard)
        other = jax.tree.map(lambda a: lax.ppermute(a, axis, perm=[(0, 1), (1, 0)]), rounded)
        widen = lambda tree: jax.tree.map(lambda a, own: a.astype(own.dtype), tree, shard)
        return join(widen(rounded), widen(other))
    gathered = jax.tree.map(
        lambda a, kind: lax.all_gather(a.astype(kind), axis),
        shard,
        (jnp.bfloat16, jnp.bfloat16, jnp.bfloat16),
    )

    def take(source):
        return jax.tree.map(
            lambda a, own: lax.dynamic_index_in_dim(a, source, 0, False).astype(own.dtype),
            gathered,
            shard,
        )

    return lax.fori_loop(
        1, lax.axis_size(axis), lambda source, state: join(state, take(source)), take(0)
    )


def relative(expert, me, count):
    if count & (count - 1) == 0:
        return jnp.bitwise_xor(expert, me)
    return (expert - me) % count


def exchange(chunks, count):
    pieces = [chunks[0]]
    for step in range(1, count):
        if count & (count - 1) == 0:
            pairs = [(i, i ^ step) for i in range(count)]
        else:
            pairs = [(i, (i + step) % count) for i in range(count)]
        pieces.append(lax.ppermute(chunks[step], "el", perm=pairs))
    return jnp.stack(pieces)


def expert_block(rows, gate_w, up_w, down_w):
    feat_part = rows.shape[1]
    if lax.axis_size("tp") != 2:
        inputs = lax.all_gather(rows, "tp", axis=1, tiled=True)
        gate_value = jnp.dot(inputs, gate_w, preferred_element_type=jnp.float32)
        up_value = jnp.dot(inputs, up_w, preferred_element_type=jnp.float32)
        hidden = (jnp.maximum(gate_value, 0.0) * up_value).astype(jnp.bfloat16)
        partial_value = jnp.dot(hidden, down_w, preferred_element_type=jnp.float32)
        return lax.psum_scatter(
            partial_value.astype(jnp.bfloat16), "tp", scatter_dimension=1, tiled=True
        )
    swap = [(0, 1), (1, 0)]
    mine = lax.axis_index("tp")
    other = 1 - mine
    rows_other = lax.ppermute(rows, "tp", perm=swap)
    gate_parts = gate_w.reshape(2, feat_part, gate_w.shape[1])
    up_parts = up_w.reshape(2, feat_part, up_w.shape[1])

    def half_product(parts, x, which):
        weight = lax.dynamic_index_in_dim(parts, which, 0, keepdims=False)
        return jnp.dot(x, weight, preferred_element_type=jnp.float32)

    gate_value = half_product(gate_parts, rows, mine) + half_product(gate_parts, rows_other, other)
    up_value = half_product(up_parts, rows, mine) + half_product(up_parts, rows_other, other)
    hidden = (jnp.maximum(gate_value, 0.0) * up_value).astype(jnp.bfloat16)

    def down_product(which):
        weight = lax.dynamic_slice_in_dim(down_w, which * feat_part, feat_part, axis=1)
        return jnp.dot(hidden, weight, preferred_element_type=jnp.float32).astype(jnp.bfloat16)

    sent = lax.ppermute(down_product(other), "tp", perm=swap)
    kept = lax.optimization_barrier(down_product(mine))
    return (kept.astype(jnp.float32) + sent.astype(jnp.float32)).astype(jnp.bfloat16)


def tp_sum(value):
    if lax.axis_size("tp") != 2:
        return lax.psum(value, "tp")
    return value + lax.ppermute(value, "tp", perm=[(0, 1), (1, 0)])


def tp_gather(part, axis):
    if lax.axis_size("tp") != 2:
        return lax.all_gather(part, "tp", axis=axis, tiled=True)
    other = lax.ppermute(part, "tp", perm=[(0, 1), (1, 0)])
    first = lax.axis_index("tp") == 0
    low = jnp.where(first, part, other)
    high = jnp.where(first, other, part)
    return jnp.concatenate([low, high], axis=axis)


def tp_scatter_sum(full, axis):
    if lax.axis_size("tp") != 2:
        return lax.psum_scatter(full, "tp", scatter_dimension=axis, tiled=True)
    low, high = jnp.split(full, 2, axis=axis)
    first = lax.axis_index("tp") == 0
    keep = jnp.where(first, low, high)
    send = jnp.where(first, high, low)
    other = lax.ppermute(send, "tp", perm=[(0, 1), (1, 0)])
    return (keep.astype(jnp.float32) + other.astype(jnp.float32)).astype(full.dtype)


def merge_parts(first, second):
    joint_max = jnp.maximum(first[0], second[0])
    scale_first = jnp.exp(first[0] - joint_max)
    scale_second = jnp.exp(second[0] - joint_max)
    return (
        joint_max,
        first[1] * scale_first + second[1] * scale_second,
        first[2] * scale_first[..., None] + second[2] * scale_second[..., None],
    )


def shards(
    tokens,
    queries,
    kv_cache,
    page_table,
    query_lens,
    past_lens,
    out_weight,
    norm_gain,
    route_ids,
    route_weights,
    gate_w,
    up_w,
    down_w,
    final_gain,
):
    tp_index = lax.axis_index("tp")
    tp_count = lax.axis_size("tp")
    count_of_rows, feat_part = tokens.shape
    full_width = feat_part * tp_count
    local_groups = query_lens.shape[0]
    req_count = query_lens.shape[1]
    group_rows = count_of_rows // local_groups
    head_groups = QUERY_HEADS // KEY_VALUE_HEADS
    per_device = page_table.shape[1] // tp_count

    def one_group(local):
        query_count = lax.dynamic_index_in_dim(query_lens, local, 0, keepdims=False)
        past_count = lax.dynamic_index_in_dim(past_lens, local, 0, keepdims=False)
        row_ends = jnp.cumsum(query_count)
        row_starts = row_ends - query_count
        row_iota = jnp.arange(group_rows, dtype=jnp.int32)
        row_req = jnp.sum((row_iota[:, None] >= row_ends[None, :]).astype(jnp.int32), axis=1)
        req_onehot = (row_req[:, None] == jnp.arange(req_count, dtype=jnp.int32)[None, :]).astype(
            jnp.int32
        )
        row_pos = row_iota + jnp.sum(req_onehot * (past_count - row_starts)[None, :], axis=1)
        local_table = lax.dynamic_index_in_dim(
            page_table.reshape(req_count, per_device, tp_count), tp_index, axis=2, keepdims=False
        )
        group_pages = lax.dynamic_index_in_dim(kv_cache, local, 0, keepdims=False)[0]
        page_row_block = group_pages[local_table.reshape(-1)]
        key_count_total = page_row_block.shape[0] * PAGE_POSITIONS
        flattened_cache = page_row_block.reshape(key_count_total, 2 * KEY_VALUE_HEADS * HEAD_SIZE)
        gathered_keys = flattened_cache[:, : KEY_VALUE_HEADS * HEAD_SIZE].reshape(
            key_count_total, KEY_VALUE_HEADS, HEAD_SIZE
        )
        gathered_values = flattened_cache[:, KEY_VALUE_HEADS * HEAD_SIZE :].reshape(
            key_count_total, KEY_VALUE_HEADS, HEAD_SIZE
        )
        key_iota = jnp.arange(key_count_total, dtype=jnp.int32)
        key_req = key_iota // (per_device * PAGE_POSITIONS)
        within = key_iota % (per_device * PAGE_POSITIONS)
        key_pos = (
            within // PAGE_POSITIONS * tp_count + tp_index
        ) * PAGE_POSITIONS + within % PAGE_POSITIONS
        allowed = (row_req[:, None] == key_req[None, :]) & (key_pos[None, :] <= row_pos[:, None])
        score_mask = allowed[:, None, :]
        outs = []
        for kv_head in range(KEY_VALUE_HEADS):
            head_rows = queries[:, kv_head * head_groups * HEAD_SIZE : (kv_head + 1) * head_groups * HEAD_SIZE]
            head_rows = head_rows.reshape(group_rows, head_groups, HEAD_SIZE)
            head_keys = flattened_cache[:, kv_head * HEAD_SIZE : (kv_head + 1) * HEAD_SIZE]
            head_values = flattened_cache[
                :, (KEY_VALUE_HEADS + kv_head) * HEAD_SIZE : (KEY_VALUE_HEADS + kv_head + 1) * HEAD_SIZE
            ]
            scores = jnp.einsum(
                "rgd,ld->rgl", head_rows, head_keys, preferred_element_type=jnp.float32
            ) * HEAD_SIZE ** (-0.5)
            top = jnp.max(jnp.where(score_mask, scores, -1e30), axis=-1)
            soft = jnp.where(score_mask, jnp.exp(scores - top[..., None]), 0.0)
            total = jnp.sum(soft, axis=-1)
            weighted_part = jnp.einsum(
                "rgl,ld->rgd",
                soft.astype(jnp.bfloat16),
                head_values,
                preferred_element_type=jnp.float32,
            )
            outs.append((top, total, weighted_part))
        part_max = jnp.stack([o[0] for o in outs], axis=1)
        part_sum = jnp.stack([o[1] for o in outs], axis=1)
        part_weighted = jnp.stack([o[2] for o in outs], axis=1)
        return (part_max, part_sum, part_weighted)

    row_max, row_sum, weighted = lax.map(one_group, jnp.arange(local_groups, dtype=jnp.int32))
    row_max = row_max.reshape(count_of_rows, KEY_VALUE_HEADS, head_groups)
    row_sum = row_sum.reshape(count_of_rows, KEY_VALUE_HEADS, head_groups)
    weighted = weighted.reshape(count_of_rows, KEY_VALUE_HEADS, head_groups, HEAD_SIZE)
    row_max, row_sum, weighted = merged((row_max, row_sum, weighted), "tp", merge_parts)
    attended = (
        (weighted / row_sum[..., None])
        .reshape(count_of_rows, QUERY_HEADS * HEAD_SIZE)
        .astype(jnp.bfloat16)
    )
    resid = tokens.astype(jnp.float32) + jnp.dot(
        attended, out_weight, preferred_element_type=jnp.float32
    )
    mid_squares = tp_sum(jnp.sum(resid * resid, axis=1))
    normed = (resid * lax.rsqrt(mid_squares / full_width + EPSILON)[:, None] * norm_gain).astype(
        jnp.bfloat16
    )
    top_count = route_ids.shape[1]
    half_count = lax.axis_size("el")
    experts = half_count
    capacity = count_of_rows * top_count * 2 // experts
    buffer_len = experts * capacity
    flat_ids = route_ids.reshape(-1)
    expert_onehot = (flat_ids[:, None] == jnp.arange(experts, dtype=jnp.int32)[None, :]).astype(
        jnp.int32
    )
    assign_iota = jnp.arange(flat_ids.shape[0], dtype=jnp.int32)
    earlier = (assign_iota[None, :] < assign_iota[:, None]).astype(jnp.bfloat16)
    before = jnp.dot(
        earlier, expert_onehot.astype(jnp.bfloat16), preferred_element_type=jnp.float32
    ).astype(jnp.int32)
    expert_rank = jnp.sum(before * expert_onehot, axis=1)
    my_half = lax.axis_index("el")
    target = (relative(flat_ids, my_half, half_count) * capacity + expert_rank).reshape(
        count_of_rows, top_count
    )
    slot_iota = jnp.arange(buffer_len, dtype=jnp.int32)
    hits = target[None, :, :] == slot_iota[:, None, None]
    dispatch = jnp.any(hits, axis=2).astype(jnp.bfloat16)
    outgoing = jnp.dot(dispatch, normed, preferred_element_type=jnp.float32).astype(jnp.bfloat16)
    arrived = exchange(outgoing.reshape(experts, capacity, feat_part), half_count)
    flat_rows = lax.optimization_barrier(arrived.reshape(buffer_len, feat_part))
    group_count = 4 if buffer_len % 4 == 0 else 1
    group_rows = buffer_len // group_count
    summed = jnp.concatenate(
        [
            expert_block(
                flat_rows[start : start + group_rows], gate_w[0], up_w[0], down_w[0]
            )
            for start in range(0, buffer_len, group_rows)
        ],
        axis=0,
    )
    returned = exchange(summed.reshape(experts, capacity, feat_part), half_count).reshape(
        buffer_len, feat_part
    )
    combine = jnp.sum(
        jnp.where(
            target[:, :, None] == slot_iota[None, None, :],
            route_weights[:, :, None],
            0.0,
        ),
        axis=1,
    )
    branch = jnp.dot(
        combine,
        returned.astype(jnp.float32),
        precision=lax.Precision.HIGHEST,
        preferred_element_type=jnp.float32,
    )
    mixed_rows = resid + branch
    out_squares = tp_sum(jnp.sum(mixed_rows * mixed_rows, axis=1))
    return (
        mixed_rows * lax.rsqrt(out_squares / full_width + EPSILON)[:, None] * final_gain
    ).astype(jnp.bfloat16)


def solution(mesh):
    ep_count, tp_count = mesh.devices.shape
    halves = Mesh(mesh.devices.reshape(2, ep_count // 2, tp_count), ("eh", "el", "tp"))
    ep = ("eh", "el")
    placed = (
        P(ep, "tp"),
        P(ep, None),
        P(ep, "tp", None, None, None),
        P(ep, None),
        P(ep, None),
        P(ep, None),
        P(None, "tp"),
        P("tp"),
        P(ep, None),
        P(ep, None),
        P(ep, None, "tp"),
        P(ep, None, "tp"),
        P(ep, "tp", None),
        P("tp"),
    )
    inner = jax.shard_map(
        shards, mesh=halves, in_specs=placed, out_specs=P(ep, "tp"), check_vma=False
    )
    result_sharding = NamedSharding(mesh, P("ep", "tp"))

    def run(*args):
        return lax.with_sharding_constraint(inner(*args), result_sharding)

    return run
```

```python
import jax
import jax.numpy as jnp
from jax import lax
from jax.sharding import Mesh, NamedSharding, PartitionSpec as P

QUERY_HEADS = 12
KEY_VALUE_HEADS = 2
HEAD_SIZE = 128
PAGE_POSITIONS = 16


EPSILON = 1e-06


def merged(shard, axis, join):
    if lax.axis_size(axis) == 2:
        rounded = jax.tree.map(lambda a: a.astype(jnp.bfloat16), shard)
        other = jax.tree.map(lambda a: lax.ppermute(a, axis, perm=[(0, 1), (1, 0)]), rounded)
        widen = lambda tree: jax.tree.map(lambda a, own: a.astype(own.dtype), tree, shard)
        return join(widen(rounded), widen(other))
    gathered = jax.tree.map(
        lambda a, kind: lax.all_gather(a.astype(kind), axis),
        shard,
        (jnp.bfloat16, jnp.bfloat16, jnp.bfloat16),
    )

    def take(source):
        return jax.tree.map(
            lambda a, own: lax.dynamic_index_in_dim(a, source, 0, False).astype(own.dtype),
            gathered,
            shard,
        )

    return lax.fori_loop(
        1, lax.axis_size(axis), lambda source, state: join(state, take(source)), take(0)
    )


def relative(expert, me, count):
    if count & (count - 1) == 0:
        return jnp.bitwise_xor(expert, me)
    return (expert - me) % count


def exchange(chunks, count):
    pieces = {0: chunks[0]}
    steps = list(range(1, count))
    if count & (count - 1) == 0:
        steps.sort(key=lambda step: (bin(step).count("1"), step))
    for step in steps:
        if count & (count - 1) == 0:
            pairs = [(i, i ^ step) for i in range(count)]
        else:
            pairs = [(i, (i + step) % count) for i in range(count)]
        pieces[step] = lax.ppermute(chunks[step], "el", perm=pairs)
    return jnp.stack([pieces[step] for step in range(count)])


def expert_block(rows, gate_w, up_w, down_w):
    feat_part = rows.shape[1]
    if lax.axis_size("tp") != 2:
        inputs = lax.all_gather(rows, "tp", axis=1, tiled=True)
        gate_value = jnp.dot(inputs, gate_w, preferred_element_type=jnp.float32)
        up_value = jnp.dot(inputs, up_w, preferred_element_type=jnp.float32)
        hidden = (jnp.maximum(gate_value, 0.0) * up_value).astype(jnp.bfloat16)
        partial_value = jnp.dot(hidden, down_w, preferred_element_type=jnp.float32)
        return lax.psum_scatter(
            partial_value.astype(jnp.bfloat16), "tp", scatter_dimension=1, tiled=True
        )
    swap = [(0, 1), (1, 0)]
    mine = lax.axis_index("tp")
    other = 1 - mine
    rows_other = lax.ppermute(rows, "tp", perm=swap)
    gate_parts = gate_w.reshape(2, feat_part, gate_w.shape[1])
    up_parts = up_w.reshape(2, feat_part, up_w.shape[1])

    def half_product(parts, x, which):
        weight = lax.dynamic_index_in_dim(parts, which, 0, keepdims=False)
        return jnp.dot(x, weight, preferred_element_type=jnp.float32)

    gate_value = half_product(gate_parts, rows, mine) + half_product(gate_parts, rows_other, other)
    up_value = half_product(up_parts, rows, mine) + half_product(up_parts, rows_other, other)
    hidden = (jnp.maximum(gate_value, 0.0) * up_value).astype(jnp.bfloat16)

    def down_product(which):
        weight = lax.dynamic_slice_in_dim(down_w, which * feat_part, feat_part, axis=1)
        return jnp.dot(hidden, weight, preferred_element_type=jnp.float32).astype(jnp.bfloat16)

    sent = lax.ppermute(down_product(other), "tp", perm=swap)
    kept = lax.optimization_barrier(down_product(mine))
    return (kept.astype(jnp.float32) + sent.astype(jnp.float32)).astype(jnp.bfloat16)


def tp_sum(value):
    if lax.axis_size("tp") != 2:
        return lax.psum(value, "tp")
    return value + lax.ppermute(value, "tp", perm=[(0, 1), (1, 0)])


def tp_gather(part, axis):
    if lax.axis_size("tp") != 2:
        return lax.all_gather(part, "tp", axis=axis, tiled=True)
    other = lax.ppermute(part, "tp", perm=[(0, 1), (1, 0)])
    first = lax.axis_index("tp") == 0
    low = jnp.where(first, part, other)
    high = jnp.where(first, other, part)
    return jnp.concatenate([low, high], axis=axis)


def tp_scatter_sum(full, axis):
    if lax.axis_size("tp") != 2:
        return lax.psum_scatter(full, "tp", scatter_dimension=axis, tiled=True)
    low, high = jnp.split(full, 2, axis=axis)
    first = lax.axis_index("tp") == 0
    keep = jnp.where(first, low, high)
    send = jnp.where(first, high, low)
    other = lax.ppermute(send, "tp", perm=[(0, 1), (1, 0)])
    return (keep.astype(jnp.float32) + other.astype(jnp.float32)).astype(full.dtype)


def merge_parts(first, second):
    joint_max = jnp.maximum(first[0], second[0])
    scale_first = jnp.exp(first[0] - joint_max)
    scale_second = jnp.exp(second[0] - joint_max)
    return (
        joint_max,
        first[1] * scale_first + second[1] * scale_second,
        first[2] * scale_first[..., None] + second[2] * scale_second[..., None],
    )


def shards(
    tokens,
    queries,
    kv_cache,
    page_table,
    query_lens,
    past_lens,
    out_weight,
    norm_gain,
    route_ids,
    route_weights,
    gate_w,
    up_w,
    down_w,
    final_gain,
):
    tp_index = lax.axis_index("tp")
    tp_count = lax.axis_size("tp")
    count_of_rows, feat_part = tokens.shape
    full_width = feat_part * tp_count
    local_groups = query_lens.shape[0]
    req_count = query_lens.shape[1]
    group_rows = count_of_rows // local_groups
    head_groups = QUERY_HEADS // KEY_VALUE_HEADS
    per_device = page_table.shape[1] // tp_count

    def one_group(local):
        query_count = lax.dynamic_index_in_dim(query_lens, local, 0, keepdims=False)
        past_count = lax.dynamic_index_in_dim(past_lens, local, 0, keepdims=False)
        row_ends = jnp.cumsum(query_count)
        row_starts = row_ends - query_count
        row_iota = jnp.arange(group_rows, dtype=jnp.int32)
        row_req = jnp.sum((row_iota[:, None] >= row_ends[None, :]).astype(jnp.int32), axis=1)
        req_onehot = (row_req[:, None] == jnp.arange(req_count, dtype=jnp.int32)[None, :]).astype(
            jnp.int32
        )
        row_pos = row_iota + jnp.sum(req_onehot * (past_count - row_starts)[None, :], axis=1)
        local_table = lax.dynamic_index_in_dim(
            page_table.reshape(req_count, per_device, tp_count), tp_index, axis=2, keepdims=False
        )
        group_pages = lax.dynamic_index_in_dim(kv_cache, local, 0, keepdims=False)[0]
        page_row_block = group_pages[local_table.reshape(-1)]
        key_count_total = page_row_block.shape[0] * PAGE_POSITIONS
        flattened_cache = page_row_block.reshape(key_count_total, 2 * KEY_VALUE_HEADS * HEAD_SIZE)
        gathered_keys = flattened_cache[:, : KEY_VALUE_HEADS * HEAD_SIZE].reshape(
            key_count_total, KEY_VALUE_HEADS, HEAD_SIZE
        )
        gathered_values = flattened_cache[:, KEY_VALUE_HEADS * HEAD_SIZE :].reshape(
            key_count_total, KEY_VALUE_HEADS, HEAD_SIZE
        )
        key_iota = jnp.arange(key_count_total, dtype=jnp.int32)
        key_req = key_iota // (per_device * PAGE_POSITIONS)
        within = key_iota % (per_device * PAGE_POSITIONS)
        key_pos = (
            within // PAGE_POSITIONS * tp_count + tp_index
        ) * PAGE_POSITIONS + within % PAGE_POSITIONS
        allowed = (row_req[:, None] == key_req[None, :]) & (key_pos[None, :] <= row_pos[:, None])
        score_mask = allowed[:, None, :]
        outs = []
        for kv_head in range(KEY_VALUE_HEADS):
            head_rows = queries[:, kv_head * head_groups * HEAD_SIZE : (kv_head + 1) * head_groups * HEAD_SIZE]
            head_rows = head_rows.reshape(group_rows, head_groups, HEAD_SIZE)
            head_keys = flattened_cache[:, kv_head * HEAD_SIZE : (kv_head + 1) * HEAD_SIZE]
            head_values = flattened_cache[
                :, (KEY_VALUE_HEADS + kv_head) * HEAD_SIZE : (KEY_VALUE_HEADS + kv_head + 1) * HEAD_SIZE
            ]
            scores = jnp.einsum(
                "rgd,ld->rgl", head_rows, head_keys, preferred_element_type=jnp.float32
            ) * HEAD_SIZE ** (-0.5)
            top = jnp.max(jnp.where(score_mask, scores, -1e30), axis=-1)
            soft = jnp.where(score_mask, jnp.exp(scores - top[..., None]), 0.0)
            total = jnp.sum(soft, axis=-1)
            weighted_part = jnp.einsum(
                "rgl,ld->rgd",
                soft.astype(jnp.bfloat16),
                head_values,
                preferred_element_type=jnp.float32,
            )
            outs.append((top, total, weighted_part))
        part_max = jnp.stack([o[0] for o in outs], axis=1)
        part_sum = jnp.stack([o[1] for o in outs], axis=1)
        part_weighted = jnp.stack([o[2] for o in outs], axis=1)
        return (part_max, part_sum, part_weighted)

    row_max, row_sum, weighted = lax.map(one_group, jnp.arange(local_groups, dtype=jnp.int32))
    row_max = row_max.reshape(count_of_rows, KEY_VALUE_HEADS, head_groups)
    row_sum = row_sum.reshape(count_of_rows, KEY_VALUE_HEADS, head_groups)
    weighted = weighted.reshape(count_of_rows, KEY_VALUE_HEADS, head_groups, HEAD_SIZE)
    row_max, row_sum, weighted = merged((row_max, row_sum, weighted), "tp", merge_parts)
    attended = (
        (weighted / row_sum[..., None])
        .reshape(count_of_rows, QUERY_HEADS * HEAD_SIZE)
        .astype(jnp.bfloat16)
    )
    resid = tokens.astype(jnp.float32) + jnp.dot(
        attended, out_weight, preferred_element_type=jnp.float32
    )
    mid_squares = tp_sum(jnp.sum(resid * resid, axis=1))
    normed = (resid * lax.rsqrt(mid_squares / full_width + EPSILON)[:, None] * norm_gain).astype(
        jnp.bfloat16
    )
    top_count = route_ids.shape[1]
    half_count = lax.axis_size("el")
    experts = half_count
    capacity = count_of_rows * top_count * 2 // experts
    buffer_len = experts * capacity
    flat_ids = route_ids.reshape(-1)
    expert_onehot = (flat_ids[:, None] == jnp.arange(experts, dtype=jnp.int32)[None, :]).astype(
        jnp.int32
    )
    assign_iota = jnp.arange(flat_ids.shape[0], dtype=jnp.int32)
    earlier = (assign_iota[None, :] < assign_iota[:, None]).astype(jnp.bfloat16)
    before = jnp.dot(
        earlier, expert_onehot.astype(jnp.bfloat16), preferred_element_type=jnp.float32
    ).astype(jnp.int32)
    expert_rank = jnp.sum(before * expert_onehot, axis=1)
    my_half = lax.axis_index("el")
    target = (relative(flat_ids, my_half, half_count) * capacity + expert_rank).reshape(
        count_of_rows, top_count
    )
    slot_iota = jnp.arange(buffer_len, dtype=jnp.int32)
    hits = target[None, :, :] == slot_iota[:, None, None]
    dispatch = jnp.any(hits, axis=2).astype(jnp.bfloat16)
    outgoing = jnp.dot(dispatch, normed, preferred_element_type=jnp.float32).astype(jnp.bfloat16)
    arrived = exchange(outgoing.reshape(experts, capacity, feat_part), half_count)
    flat_rows = lax.optimization_barrier(arrived.reshape(buffer_len, feat_part))
    group_rows = buffer_len // 2
    summed = jnp.concatenate(
        [
            expert_block(
                flat_rows[start : start + group_rows], gate_w[0], up_w[0], down_w[0]
            )
            for start in (0, group_rows)
        ],
        axis=0,
    )
    returned = exchange(summed.reshape(experts, capacity, feat_part), half_count).reshape(
        buffer_len, feat_part
    )
    combine = jnp.sum(
        jnp.where(
            target[:, :, None] == slot_iota[None, None, :],
            route_weights[:, :, None],
            0.0,
        ),
        axis=1,
    )
    branch = jnp.dot(
        combine,
        returned.astype(jnp.float32),
        precision=lax.Precision.HIGHEST,
        preferred_element_type=jnp.float32,
    )
    mixed_rows = resid + branch
    out_squares = tp_sum(jnp.sum(mixed_rows * mixed_rows, axis=1))
    return (
        mixed_rows * lax.rsqrt(out_squares / full_width + EPSILON)[:, None] * final_gain
    ).astype(jnp.bfloat16)


def solution(mesh):
    ep_count, tp_count = mesh.devices.shape
    halves = Mesh(mesh.devices.reshape(2, ep_count // 2, tp_count), ("eh", "el", "tp"))
    ep = ("eh", "el")
    placed = (
        P(ep, "tp"),
        P(ep, None),
        P(ep, "tp", None, None, None),
        P(ep, None),
        P(ep, None),
        P(ep, None),
        P(None, "tp"),
        P("tp"),
        P(ep, None),
        P(ep, None),
        P(ep, None, "tp"),
        P(ep, None, "tp"),
        P(ep, "tp", None),
        P("tp"),
    )
    inner = jax.shard_map(
        shards, mesh=halves, in_specs=placed, out_specs=P(ep, "tp"), check_vma=False
    )
    result_sharding = NamedSharding(mesh, P("ep", "tp"))

    def run(*args):
        return lax.with_sharding_constraint(inner(*args), result_sharding)

    return run
```

```python
import jax
import jax.numpy as jnp
from jax import lax
from jax.sharding import Mesh, NamedSharding, PartitionSpec as P

QUERY_HEADS = 12
KEY_VALUE_HEADS = 2
HEAD_SIZE = 128
PAGE_POSITIONS = 16


EPSILON = 1e-06


def merged(shard, axis, join):
    if lax.axis_size(axis) == 2:
        rounded = jax.tree.map(lambda a: a.astype(jnp.bfloat16), shard)
        other = jax.tree.map(lambda a: lax.ppermute(a, axis, perm=[(0, 1), (1, 0)]), rounded)
        widen = lambda tree: jax.tree.map(lambda a, own: a.astype(own.dtype), tree, shard)
        return join(widen(rounded), widen(other))
    gathered = jax.tree.map(
        lambda a, kind: lax.all_gather(a.astype(kind), axis),
        shard,
        (jnp.bfloat16, jnp.bfloat16, jnp.bfloat16),
    )

    def take(source):
        return jax.tree.map(
            lambda a, own: lax.dynamic_index_in_dim(a, source, 0, False).astype(own.dtype),
            gathered,
            shard,
        )

    return lax.fori_loop(
        1, lax.axis_size(axis), lambda source, state: join(state, take(source)), take(0)
    )


def relative(expert, me, count):
    if count & (count - 1) == 0:
        return jnp.bitwise_xor(expert, me)
    return (expert - me) % count


def exchange(chunks, count):
    pieces = [chunks[0]]
    for step in range(1, count):
        if count & (count - 1) == 0:
            pairs = [(i, i ^ step) for i in range(count)]
        else:
            pairs = [(i, (i + step) % count) for i in range(count)]
        pieces.append(lax.ppermute(chunks[step], "el", perm=pairs))
    return jnp.stack(pieces)


def expert_block(rows, gate_w, up_w, down_w):
    feat_part = rows.shape[1]
    if lax.axis_size("tp") != 2:
        inputs = lax.all_gather(rows, "tp", axis=1, tiled=True)
        gate_value = jnp.dot(inputs, gate_w, preferred_element_type=jnp.float32)
        up_value = jnp.dot(inputs, up_w, preferred_element_type=jnp.float32)
        hidden = (jnp.maximum(gate_value, 0.0) * up_value).astype(jnp.bfloat16)
        partial_value = jnp.dot(hidden, down_w, preferred_element_type=jnp.float32)
        return lax.psum_scatter(
            partial_value.astype(jnp.bfloat16), "tp", scatter_dimension=1, tiled=True
        )
    swap = [(0, 1), (1, 0)]
    mine = lax.axis_index("tp")
    other = 1 - mine
    rows_other = lax.ppermute(rows, "tp", perm=swap)
    gate_parts = gate_w.reshape(2, feat_part, gate_w.shape[1])
    up_parts = up_w.reshape(2, feat_part, up_w.shape[1])

    def half_product(parts, x, which):
        weight = lax.dynamic_index_in_dim(parts, which, 0, keepdims=False)
        return jnp.dot(x, weight, preferred_element_type=jnp.float32)

    gate_value = half_product(gate_parts, rows, mine) + half_product(gate_parts, rows_other, other)
    up_value = half_product(up_parts, rows, mine) + half_product(up_parts, rows_other, other)
    hidden = (jnp.maximum(gate_value, 0.0) * up_value).astype(jnp.bfloat16)

    def down_product(which):
        weight = lax.dynamic_slice_in_dim(down_w, which * feat_part, feat_part, axis=1)
        return jnp.dot(hidden, weight, preferred_element_type=jnp.float32).astype(jnp.bfloat16)

    sent = lax.ppermute(down_product(other), "tp", perm=swap)
    kept = lax.optimization_barrier(down_product(mine))
    return (kept.astype(jnp.float32) + sent.astype(jnp.float32)).astype(jnp.bfloat16)


def tp_sum(value):
    if lax.axis_size("tp") != 2:
        return lax.psum(value, "tp")
    return value + lax.ppermute(value, "tp", perm=[(0, 1), (1, 0)])


def tp_gather(part, axis):
    if lax.axis_size("tp") != 2:
        return lax.all_gather(part, "tp", axis=axis, tiled=True)
    other = lax.ppermute(part, "tp", perm=[(0, 1), (1, 0)])
    first = lax.axis_index("tp") == 0
    low = jnp.where(first, part, other)
    high = jnp.where(first, other, part)
    return jnp.concatenate([low, high], axis=axis)


def tp_scatter_sum(full, axis):
    if lax.axis_size("tp") != 2:
        return lax.psum_scatter(full, "tp", scatter_dimension=axis, tiled=True)
    low, high = jnp.split(full, 2, axis=axis)
    first = lax.axis_index("tp") == 0
    keep = jnp.where(first, low, high)
    send = jnp.where(first, high, low)
    other = lax.ppermute(send, "tp", perm=[(0, 1), (1, 0)])
    return (keep.astype(jnp.float32) + other.astype(jnp.float32)).astype(full.dtype)


def merge_parts(first, second):
    joint_max = jnp.maximum(first[0], second[0])
    scale_first = jnp.exp(first[0] - joint_max)
    scale_second = jnp.exp(second[0] - joint_max)
    return (
        joint_max,
        first[1] * scale_first + second[1] * scale_second,
        first[2] * scale_first[..., None] + second[2] * scale_second[..., None],
    )


def shards(
    tokens,
    queries,
    kv_cache,
    page_table,
    query_lens,
    past_lens,
    out_weight,
    norm_gain,
    route_ids,
    route_weights,
    gate_w,
    up_w,
    down_w,
    final_gain,
):
    tp_index = lax.axis_index("tp")
    tp_count = lax.axis_size("tp")
    count_of_rows, feat_part = tokens.shape
    full_width = feat_part * tp_count
    local_groups = query_lens.shape[0]
    req_count = query_lens.shape[1]
    group_rows = count_of_rows // local_groups
    head_groups = QUERY_HEADS // KEY_VALUE_HEADS
    per_device = page_table.shape[1] // tp_count

    def one_group(local):
        query_count = lax.dynamic_index_in_dim(query_lens, local, 0, keepdims=False)
        past_count = lax.dynamic_index_in_dim(past_lens, local, 0, keepdims=False)
        row_ends = jnp.cumsum(query_count)
        row_starts = row_ends - query_count
        row_iota = jnp.arange(group_rows, dtype=jnp.int32)
        row_req = jnp.sum((row_iota[:, None] >= row_ends[None, :]).astype(jnp.int32), axis=1)
        req_onehot = (row_req[:, None] == jnp.arange(req_count, dtype=jnp.int32)[None, :]).astype(
            jnp.int32
        )
        row_pos = row_iota + jnp.sum(req_onehot * (past_count - row_starts)[None, :], axis=1)
        local_table = lax.dynamic_index_in_dim(
            page_table.reshape(req_count, per_device, tp_count), tp_index, axis=2, keepdims=False
        )
        group_pages = lax.dynamic_index_in_dim(kv_cache, local, 0, keepdims=False)[0]
        page_row_block = group_pages[local_table.reshape(-1)]
        key_count_total = page_row_block.shape[0] * PAGE_POSITIONS
        flattened_cache = page_row_block.reshape(key_count_total, 2 * KEY_VALUE_HEADS * HEAD_SIZE)
        gathered_keys = flattened_cache[:, : KEY_VALUE_HEADS * HEAD_SIZE].reshape(
            key_count_total, KEY_VALUE_HEADS, HEAD_SIZE
        )
        gathered_values = flattened_cache[:, KEY_VALUE_HEADS * HEAD_SIZE :].reshape(
            key_count_total, KEY_VALUE_HEADS, HEAD_SIZE
        )
        key_iota = jnp.arange(key_count_total, dtype=jnp.int32)
        key_req = key_iota // (per_device * PAGE_POSITIONS)
        within = key_iota % (per_device * PAGE_POSITIONS)
        key_pos = (
            within // PAGE_POSITIONS * tp_count + tp_index
        ) * PAGE_POSITIONS + within % PAGE_POSITIONS
        allowed = (row_req[:, None] == key_req[None, :]) & (key_pos[None, :] <= row_pos[:, None])
        score_mask = allowed[:, None, :]
        outs = []
        for kv_head in range(KEY_VALUE_HEADS):
            head_rows = queries[:, kv_head * head_groups * HEAD_SIZE : (kv_head + 1) * head_groups * HEAD_SIZE]
            head_rows = head_rows.reshape(group_rows, head_groups, HEAD_SIZE)
            head_keys = flattened_cache[:, kv_head * HEAD_SIZE : (kv_head + 1) * HEAD_SIZE]
            head_values = flattened_cache[
                :, (KEY_VALUE_HEADS + kv_head) * HEAD_SIZE : (KEY_VALUE_HEADS + kv_head + 1) * HEAD_SIZE
            ]
            scores = jnp.einsum(
                "rgd,ld->rgl", head_rows, head_keys, preferred_element_type=jnp.float32
            ) * HEAD_SIZE ** (-0.5)
            top = jnp.max(jnp.where(score_mask, scores, -1e30), axis=-1)
            soft = jnp.where(score_mask, jnp.exp(scores - top[..., None]), 0.0)
            total = jnp.sum(soft, axis=-1)
            weighted_part = jnp.einsum(
                "rgl,ld->rgd",
                soft.astype(jnp.bfloat16),
                head_values,
                preferred_element_type=jnp.float32,
            )
            outs.append((top, total, weighted_part))
        part_max = jnp.stack([o[0] for o in outs], axis=1)
        part_sum = jnp.stack([o[1] for o in outs], axis=1)
        part_weighted = jnp.stack([o[2] for o in outs], axis=1)
        return (part_max, part_sum, part_weighted)

    row_max, row_sum, weighted = lax.map(one_group, jnp.arange(local_groups, dtype=jnp.int32))
    row_max = row_max.reshape(count_of_rows, KEY_VALUE_HEADS, head_groups)
    row_sum = row_sum.reshape(count_of_rows, KEY_VALUE_HEADS, head_groups)
    weighted = weighted.reshape(count_of_rows, KEY_VALUE_HEADS, head_groups, HEAD_SIZE)
    row_max, row_sum, weighted = merged((row_max, row_sum, weighted), "tp", merge_parts)
    attended = (
        (weighted / row_sum[..., None])
        .reshape(count_of_rows, QUERY_HEADS * HEAD_SIZE)
        .astype(jnp.bfloat16)
    )
    resid = tokens.astype(jnp.float32) + jnp.dot(
        attended, out_weight, preferred_element_type=jnp.float32
    )
    mid_squares = tp_sum(jnp.sum(resid * resid, axis=1))
    normed = (resid * lax.rsqrt(mid_squares / full_width + EPSILON)[:, None] * norm_gain).astype(
        jnp.bfloat16
    )
    top_count = route_ids.shape[1]
    half_count = lax.axis_size("el")
    experts = half_count
    capacity = count_of_rows * top_count * 2 // experts
    buffer_len = experts * capacity
    flat_ids = route_ids.reshape(-1)
    expert_onehot = (flat_ids[:, None] == jnp.arange(experts, dtype=jnp.int32)[None, :]).astype(
        jnp.int32
    )
    assign_iota = jnp.arange(flat_ids.shape[0], dtype=jnp.int32)
    earlier = (assign_iota[None, :] < assign_iota[:, None]).astype(jnp.bfloat16)
    before = jnp.dot(
        earlier, expert_onehot.astype(jnp.bfloat16), preferred_element_type=jnp.float32
    ).astype(jnp.int32)
    expert_rank = jnp.sum(before * expert_onehot, axis=1)
    my_half = lax.axis_index("el")
    target = (relative(flat_ids, my_half, half_count) * capacity + expert_rank).reshape(
        count_of_rows, top_count
    )
    slot_iota = jnp.arange(buffer_len, dtype=jnp.int32)
    hits = target[None, :, :] == slot_iota[:, None, None]
    dispatch = jnp.any(hits, axis=2).astype(jnp.bfloat16)
    outgoing = jnp.dot(dispatch, normed, preferred_element_type=jnp.float32).astype(jnp.bfloat16)
    arrived = exchange(outgoing.reshape(experts, capacity, feat_part), half_count)
    flat_rows = lax.optimization_barrier(arrived.reshape(buffer_len, feat_part))
    group_rows = buffer_len // 2
    summed = jnp.concatenate(
        [
            expert_block(
                flat_rows[start : start + group_rows], gate_w[0], up_w[0], down_w[0]
            )
            for start in (0, group_rows)
        ],
        axis=0,
    )
    returned = exchange(summed.reshape(experts, capacity, feat_part), half_count).reshape(
        buffer_len, feat_part
    )
    branch = jnp.zeros(resid.shape, jnp.float32)
    for pick in range(top_count):
        choose = (target[:, pick][:, None] == slot_iota[None, :]).astype(jnp.bfloat16)
        picked = jnp.dot(choose, returned, preferred_element_type=jnp.float32)
        branch = branch + route_weights[:, pick][:, None] * picked
    mixed_rows = resid + branch
    out_squares = tp_sum(jnp.sum(mixed_rows * mixed_rows, axis=1))
    return (
        mixed_rows * lax.rsqrt(out_squares / full_width + EPSILON)[:, None] * final_gain
    ).astype(jnp.bfloat16)


def solution(mesh):
    ep_count, tp_count = mesh.devices.shape
    halves = Mesh(mesh.devices.reshape(2, ep_count // 2, tp_count), ("eh", "el", "tp"))
    ep = ("eh", "el")
    placed = (
        P(ep, "tp"),
        P(ep, None),
        P(ep, "tp", None, None, None),
        P(ep, None),
        P(ep, None),
        P(ep, None),
        P(None, "tp"),
        P("tp"),
        P(ep, None),
        P(ep, None),
        P(ep, None, "tp"),
        P(ep, None, "tp"),
        P(ep, "tp", None),
        P("tp"),
    )
    inner = jax.shard_map(
        shards, mesh=halves, in_specs=placed, out_specs=P(ep, "tp"), check_vma=False
    )
    result_sharding = NamedSharding(mesh, P("ep", "tp"))

    def run(*args):
        return lax.with_sharding_constraint(inner(*args), result_sharding)

    return run
```

```python
import jax
import jax.numpy as jnp
from jax import lax
from jax.sharding import Mesh, NamedSharding, PartitionSpec as P

QUERY_HEADS = 12
KEY_VALUE_HEADS = 2
HEAD_SIZE = 128
PAGE_POSITIONS = 16


EPSILON = 1e-06


def merged(shard, axis, join):
    if lax.axis_size(axis) == 2:
        rounded = jax.tree.map(lambda a: a.astype(jnp.bfloat16), shard)
        other = jax.tree.map(lambda a: lax.ppermute(a, axis, perm=[(0, 1), (1, 0)]), rounded)
        widen = lambda tree: jax.tree.map(lambda a, own: a.astype(own.dtype), tree, shard)
        return join(widen(rounded), widen(other))
    gathered = jax.tree.map(
        lambda a, kind: lax.all_gather(a.astype(kind), axis),
        shard,
        (jnp.bfloat16, jnp.bfloat16, jnp.bfloat16),
    )

    def take(source):
        return jax.tree.map(
            lambda a, own: lax.dynamic_index_in_dim(a, source, 0, False).astype(own.dtype),
            gathered,
            shard,
        )

    return lax.fori_loop(
        1, lax.axis_size(axis), lambda source, state: join(state, take(source)), take(0)
    )


def relative(expert, me, count):
    if count & (count - 1) == 0:
        return jnp.bitwise_xor(expert, me)
    return (expert - me) % count


def exchange(chunks, count):
    pieces = [chunks[0]]
    for step in range(1, count):
        if count & (count - 1) == 0:
            pairs = [(i, i ^ step) for i in range(count)]
        else:
            pairs = [(i, (i + step) % count) for i in range(count)]
        pieces.append(lax.ppermute(chunks[step], "el", perm=pairs))
    return jnp.stack(pieces)


def expert_block(rows, gate_w, up_w, down_w):
    feat_part = rows.shape[1]
    if lax.axis_size("tp") != 2:
        inputs = lax.all_gather(rows, "tp", axis=1, tiled=True)
        gate_value = jnp.dot(inputs, gate_w, preferred_element_type=jnp.float32)
        up_value = jnp.dot(inputs, up_w, preferred_element_type=jnp.float32)
        hidden = (jnp.maximum(gate_value, 0.0) * up_value).astype(jnp.bfloat16)
        partial_value = jnp.dot(hidden, down_w, preferred_element_type=jnp.float32)
        return lax.psum_scatter(
            partial_value.astype(jnp.bfloat16), "tp", scatter_dimension=1, tiled=True
        )
    swap = [(0, 1), (1, 0)]
    mine = lax.axis_index("tp")
    other = 1 - mine
    rows_other = lax.ppermute(rows, "tp", perm=swap)
    gate_parts = gate_w.reshape(2, feat_part, gate_w.shape[1])
    up_parts = up_w.reshape(2, feat_part, up_w.shape[1])

    def half_product(parts, x, which):
        weight = lax.dynamic_index_in_dim(parts, which, 0, keepdims=False)
        return jnp.dot(x, weight, preferred_element_type=jnp.float32)

    gate_value = half_product(gate_parts, rows, mine) + half_product(gate_parts, rows_other, other)
    up_value = half_product(up_parts, rows, mine) + half_product(up_parts, rows_other, other)
    hidden = (jnp.maximum(gate_value, 0.0) * up_value).astype(jnp.bfloat16)

    def down_product(which):
        weight = lax.dynamic_slice_in_dim(down_w, which * feat_part, feat_part, axis=1)
        return jnp.dot(hidden, weight, preferred_element_type=jnp.float32).astype(jnp.bfloat16)

    sent = lax.ppermute(down_product(other), "tp", perm=swap)
    kept = down_product(mine)
    return (kept.astype(jnp.float32) + sent.astype(jnp.float32)).astype(jnp.bfloat16)


def tp_sum(value):
    if lax.axis_size("tp") != 2:
        return lax.psum(value, "tp")
    return value + lax.ppermute(value, "tp", perm=[(0, 1), (1, 0)])


def tp_gather(part, axis):
    if lax.axis_size("tp") != 2:
        return lax.all_gather(part, "tp", axis=axis, tiled=True)
    other = lax.ppermute(part, "tp", perm=[(0, 1), (1, 0)])
    first = lax.axis_index("tp") == 0
    low = jnp.where(first, part, other)
    high = jnp.where(first, other, part)
    return jnp.concatenate([low, high], axis=axis)


def tp_scatter_sum(full, axis):
    if lax.axis_size("tp") != 2:
        return lax.psum_scatter(full, "tp", scatter_dimension=axis, tiled=True)
    low, high = jnp.split(full, 2, axis=axis)
    first = lax.axis_index("tp") == 0
    keep = jnp.where(first, low, high)
    send = jnp.where(first, high, low)
    other = lax.ppermute(send, "tp", perm=[(0, 1), (1, 0)])
    return (keep.astype(jnp.float32) + other.astype(jnp.float32)).astype(full.dtype)


def merge_parts(first, second):
    joint_max = jnp.maximum(first[0], second[0])
    scale_first = jnp.exp(first[0] - joint_max)
    scale_second = jnp.exp(second[0] - joint_max)
    return (
        joint_max,
        first[1] * scale_first + second[1] * scale_second,
        first[2] * scale_first[..., None] + second[2] * scale_second[..., None],
    )


def shards(
    tokens,
    queries,
    kv_cache,
    page_table,
    query_lens,
    past_lens,
    out_weight,
    norm_gain,
    route_ids,
    route_weights,
    gate_w,
    up_w,
    down_w,
    final_gain,
):
    tp_index = lax.axis_index("tp")
    tp_count = lax.axis_size("tp")
    count_of_rows, feat_part = tokens.shape
    full_width = feat_part * tp_count
    local_groups = query_lens.shape[0]
    req_count = query_lens.shape[1]
    group_rows = count_of_rows // local_groups
    head_groups = QUERY_HEADS // KEY_VALUE_HEADS
    per_device = page_table.shape[1] // tp_count

    def one_group(local):
        query_count = lax.dynamic_index_in_dim(query_lens, local, 0, keepdims=False)
        past_count = lax.dynamic_index_in_dim(past_lens, local, 0, keepdims=False)
        row_ends = jnp.cumsum(query_count)
        row_starts = row_ends - query_count
        row_iota = jnp.arange(group_rows, dtype=jnp.int32)
        row_req = jnp.sum((row_iota[:, None] >= row_ends[None, :]).astype(jnp.int32), axis=1)
        req_onehot = (row_req[:, None] == jnp.arange(req_count, dtype=jnp.int32)[None, :]).astype(
            jnp.int32
        )
        row_pos = row_iota + jnp.sum(req_onehot * (past_count - row_starts)[None, :], axis=1)
        local_table = lax.dynamic_index_in_dim(
            page_table.reshape(req_count, per_device, tp_count), tp_index, axis=2, keepdims=False
        )
        group_pages = lax.dynamic_index_in_dim(kv_cache, local, 0, keepdims=False)[0]
        page_row_block = group_pages[local_table.reshape(-1)]
        key_count_total = page_row_block.shape[0] * PAGE_POSITIONS
        flattened_cache = page_row_block.reshape(key_count_total, 2 * KEY_VALUE_HEADS * HEAD_SIZE)
        gathered_keys = flattened_cache[:, : KEY_VALUE_HEADS * HEAD_SIZE].reshape(
            key_count_total, KEY_VALUE_HEADS, HEAD_SIZE
        )
        gathered_values = flattened_cache[:, KEY_VALUE_HEADS * HEAD_SIZE :].reshape(
            key_count_total, KEY_VALUE_HEADS, HEAD_SIZE
        )
        key_iota = jnp.arange(key_count_total, dtype=jnp.int32)
        key_req = key_iota // (per_device * PAGE_POSITIONS)
        within = key_iota % (per_device * PAGE_POSITIONS)
        key_pos = (
            within // PAGE_POSITIONS * tp_count + tp_index
        ) * PAGE_POSITIONS + within % PAGE_POSITIONS
        allowed = (row_req[:, None] == key_req[None, :]) & (key_pos[None, :] <= row_pos[:, None])
        score_mask = allowed[:, None, :]
        outs = []
        for kv_head in range(KEY_VALUE_HEADS):
            head_rows = queries[:, kv_head * head_groups * HEAD_SIZE : (kv_head + 1) * head_groups * HEAD_SIZE]
            head_rows = head_rows.reshape(group_rows, head_groups, HEAD_SIZE)
            head_keys = flattened_cache[:, kv_head * HEAD_SIZE : (kv_head + 1) * HEAD_SIZE]
            head_values = flattened_cache[
                :, (KEY_VALUE_HEADS + kv_head) * HEAD_SIZE : (KEY_VALUE_HEADS + kv_head + 1) * HEAD_SIZE
            ]
            scores = jnp.einsum(
                "rgd,ld->rgl", head_rows, head_keys, preferred_element_type=jnp.float32
            ) * HEAD_SIZE ** (-0.5)
            top = jnp.max(jnp.where(score_mask, scores, -1e30), axis=-1)
            soft = jnp.where(score_mask, jnp.exp(scores - top[..., None]), 0.0)
            total = jnp.sum(soft, axis=-1)
            weighted_part = jnp.einsum(
                "rgl,ld->rgd",
                soft.astype(jnp.bfloat16),
                head_values,
                preferred_element_type=jnp.float32,
            )
            outs.append((top, total, weighted_part))
        part_max = jnp.stack([o[0] for o in outs], axis=1)
        part_sum = jnp.stack([o[1] for o in outs], axis=1)
        part_weighted = jnp.stack([o[2] for o in outs], axis=1)
        return (part_max, part_sum, part_weighted)

    row_max, row_sum, weighted = lax.map(one_group, jnp.arange(local_groups, dtype=jnp.int32))
    row_max = row_max.reshape(count_of_rows, KEY_VALUE_HEADS, head_groups)
    row_sum = row_sum.reshape(count_of_rows, KEY_VALUE_HEADS, head_groups)
    weighted = weighted.reshape(count_of_rows, KEY_VALUE_HEADS, head_groups, HEAD_SIZE)
    row_max, row_sum, weighted = merged((row_max, row_sum, weighted), "tp", merge_parts)
    attended = (
        (weighted / row_sum[..., None])
        .reshape(count_of_rows, QUERY_HEADS * HEAD_SIZE)
        .astype(jnp.bfloat16)
    )
    resid = tokens.astype(jnp.float32) + jnp.dot(
        attended, out_weight, preferred_element_type=jnp.float32
    )
    mid_squares = tp_sum(jnp.sum(resid * resid, axis=1))
    normed = (resid * lax.rsqrt(mid_squares / full_width + EPSILON)[:, None] * norm_gain).astype(
        jnp.bfloat16
    )
    top_count = route_ids.shape[1]
    half_count = lax.axis_size("el")
    experts = half_count
    capacity = count_of_rows * top_count * 2 // experts
    buffer_len = experts * capacity
    flat_ids = route_ids.reshape(-1)
    expert_onehot = (flat_ids[:, None] == jnp.arange(experts, dtype=jnp.int32)[None, :]).astype(
        jnp.int32
    )
    assign_iota = jnp.arange(flat_ids.shape[0], dtype=jnp.int32)
    earlier = (assign_iota[None, :] < assign_iota[:, None]).astype(jnp.bfloat16)
    before = jnp.dot(
        earlier, expert_onehot.astype(jnp.bfloat16), preferred_element_type=jnp.float32
    ).astype(jnp.int32)
    expert_rank = jnp.sum(before * expert_onehot, axis=1)
    my_half = lax.axis_index("el")
    target = (relative(flat_ids, my_half, half_count) * capacity + expert_rank).reshape(
        count_of_rows, top_count
    )
    slot_iota = jnp.arange(buffer_len, dtype=jnp.int32)
    hits = target[None, :, :] == slot_iota[:, None, None]
    dispatch = jnp.any(hits, axis=2).astype(jnp.bfloat16)
    outgoing = jnp.dot(dispatch, normed, preferred_element_type=jnp.float32).astype(jnp.bfloat16)
    arrived = exchange(outgoing.reshape(experts, capacity, feat_part), half_count)
    flat_rows = lax.optimization_barrier(arrived.reshape(buffer_len, feat_part))
    group_rows = buffer_len // 2
    summed = jnp.concatenate(
        [
            expert_block(
                flat_rows[start : start + group_rows], gate_w[0], up_w[0], down_w[0]
            )
            for start in (0, group_rows)
        ],
        axis=0,
    )
    returned = exchange(summed.reshape(experts, capacity, feat_part), half_count).reshape(
        buffer_len, feat_part
    )
    combine = jnp.sum(
        jnp.where(
            target[:, :, None] == slot_iota[None, None, :],
            route_weights[:, :, None],
            0.0,
        ),
        axis=1,
    )
    branch = jnp.dot(
        combine,
        returned.astype(jnp.float32),
        precision=lax.Precision.HIGHEST,
        preferred_element_type=jnp.float32,
    )
    mixed_rows = resid + branch
    out_squares = tp_sum(jnp.sum(mixed_rows * mixed_rows, axis=1))
    return (
        mixed_rows * lax.rsqrt(out_squares / full_width + EPSILON)[:, None] * final_gain
    ).astype(jnp.bfloat16)


def solution(mesh):
    ep_count, tp_count = mesh.devices.shape
    halves = Mesh(mesh.devices.reshape(2, ep_count // 2, tp_count), ("eh", "el", "tp"))
    ep = ("eh", "el")
    placed = (
        P(ep, "tp"),
        P(ep, None),
        P(ep, "tp", None, None, None),
        P(ep, None),
        P(ep, None),
        P(ep, None),
        P(None, "tp"),
        P("tp"),
        P(ep, None),
        P(ep, None),
        P(ep, None, "tp"),
        P(ep, None, "tp"),
        P(ep, "tp", None),
        P("tp"),
    )
    inner = jax.shard_map(
        shards, mesh=halves, in_specs=placed, out_specs=P(ep, "tp"), check_vma=False
    )
    result_sharding = NamedSharding(mesh, P("ep", "tp"))

    def run(*args):
        return lax.with_sharding_constraint(inner(*args), result_sharding)

    return run
```

```python
import jax
import jax.numpy as jnp
from jax import lax
from jax.sharding import Mesh, NamedSharding, PartitionSpec as P

QUERY_HEADS = 12
KEY_VALUE_HEADS = 2
HEAD_SIZE = 128
PAGE_POSITIONS = 16


EPSILON = 1e-06


def merged(shard, axis, join):
    if lax.axis_size(axis) == 2:
        rounded = jax.tree.map(lambda a: a.astype(jnp.bfloat16), shard)
        other = jax.tree.map(lambda a: lax.ppermute(a, axis, perm=[(0, 1), (1, 0)]), rounded)
        widen = lambda tree: jax.tree.map(lambda a, own: a.astype(own.dtype), tree, shard)
        return join(widen(rounded), widen(other))
    gathered = jax.tree.map(
        lambda a, kind: lax.all_gather(a.astype(kind), axis),
        shard,
        (jnp.bfloat16, jnp.bfloat16, jnp.bfloat16),
    )

    def take(source):
        return jax.tree.map(
            lambda a, own: lax.dynamic_index_in_dim(a, source, 0, False).astype(own.dtype),
            gathered,
            shard,
        )

    return lax.fori_loop(
        1, lax.axis_size(axis), lambda source, state: join(state, take(source)), take(0)
    )


def relative(expert, me, count):
    if count & (count - 1) == 0:
        return jnp.bitwise_xor(expert, me)
    return (expert - me) % count


def exchange(chunks, count):
    pieces = [chunks[0]]
    for step in range(1, count):
        if count & (count - 1) == 0:
            pairs = [(i, i ^ step) for i in range(count)]
        else:
            pairs = [(i, (i + step) % count) for i in range(count)]
        pieces.append(lax.ppermute(chunks[step], "el", perm=pairs))
    return jnp.stack(pieces)


def expert_block(rows, gate_w, up_w, down_w):
    feat_part = rows.shape[1]
    if lax.axis_size("tp") != 2:
        inputs = lax.all_gather(rows, "tp", axis=1, tiled=True)
        gate_value = jnp.dot(inputs, gate_w, preferred_element_type=jnp.float32)
        up_value = jnp.dot(inputs, up_w, preferred_element_type=jnp.float32)
        hidden = (jnp.maximum(gate_value, 0.0) * up_value).astype(jnp.bfloat16)
        partial_value = jnp.dot(hidden, down_w, preferred_element_type=jnp.float32)
        return lax.psum_scatter(
            partial_value.astype(jnp.bfloat16), "tp", scatter_dimension=1, tiled=True
        )
    swap = [(0, 1), (1, 0)]
    mine = lax.axis_index("tp")
    other = 1 - mine
    rows_other = lax.ppermute(rows, "tp", perm=swap)
    gate_parts = gate_w.reshape(2, feat_part, gate_w.shape[1])
    up_parts = up_w.reshape(2, feat_part, up_w.shape[1])

    def half_product(parts, x, which):
        weight = lax.dynamic_index_in_dim(parts, which, 0, keepdims=False)
        return jnp.dot(x, weight, preferred_element_type=jnp.float32)

    gate_value = half_product(gate_parts, rows, mine) + half_product(gate_parts, rows_other, other)
    up_value = half_product(up_parts, rows, mine) + half_product(up_parts, rows_other, other)
    hidden = (jnp.maximum(gate_value, 0.0) * up_value).astype(jnp.bfloat16)

    def down_product(which):
        weight = lax.dynamic_slice_in_dim(down_w, which * feat_part, feat_part, axis=1)
        return jnp.dot(hidden, weight, preferred_element_type=jnp.float32).astype(jnp.bfloat16)

    sent = lax.ppermute(down_product(other), "tp", perm=swap)
    kept = lax.optimization_barrier(down_product(mine))
    return (kept.astype(jnp.float32) + sent.astype(jnp.float32)).astype(jnp.bfloat16)


def tp_sum(value):
    if lax.axis_size("tp") != 2:
        return lax.psum(value, "tp")
    return value + lax.ppermute(value, "tp", perm=[(0, 1), (1, 0)])


def tp_gather(part, axis):
    if lax.axis_size("tp") != 2:
        return lax.all_gather(part, "tp", axis=axis, tiled=True)
    other = lax.ppermute(part, "tp", perm=[(0, 1), (1, 0)])
    first = lax.axis_index("tp") == 0
    low = jnp.where(first, part, other)
    high = jnp.where(first, other, part)
    return jnp.concatenate([low, high], axis=axis)


def tp_scatter_sum(full, axis):
    if lax.axis_size("tp") != 2:
        return lax.psum_scatter(full, "tp", scatter_dimension=axis, tiled=True)
    low, high = jnp.split(full, 2, axis=axis)
    first = lax.axis_index("tp") == 0
    keep = jnp.where(first, low, high)
    send = jnp.where(first, high, low)
    other = lax.ppermute(send, "tp", perm=[(0, 1), (1, 0)])
    return (keep.astype(jnp.float32) + other.astype(jnp.float32)).astype(full.dtype)


def merge_parts(first, second):
    joint_max = jnp.maximum(first[0], second[0])
    scale_first = jnp.exp(first[0] - joint_max)
    scale_second = jnp.exp(second[0] - joint_max)
    return (
        joint_max,
        first[1] * scale_first + second[1] * scale_second,
        first[2] * scale_first[..., None] + second[2] * scale_second[..., None],
    )


def shards(
    tokens,
    queries,
    kv_cache,
    page_table,
    query_lens,
    past_lens,
    out_weight,
    norm_gain,
    route_ids,
    route_weights,
    gate_w,
    up_w,
    down_w,
    final_gain,
):
    tp_index = lax.axis_index("tp")
    tp_count = lax.axis_size("tp")
    count_of_rows, feat_part = tokens.shape
    full_width = feat_part * tp_count
    local_groups = query_lens.shape[0]
    req_count = query_lens.shape[1]
    group_rows = count_of_rows // local_groups
    head_groups = QUERY_HEADS // KEY_VALUE_HEADS
    per_device = page_table.shape[1] // tp_count

    def one_group(local):
        query_count = lax.dynamic_index_in_dim(query_lens, local, 0, keepdims=False)
        past_count = lax.dynamic_index_in_dim(past_lens, local, 0, keepdims=False)
        row_ends = jnp.cumsum(query_count)
        row_starts = row_ends - query_count
        row_iota = jnp.arange(group_rows, dtype=jnp.int32)
        row_req = jnp.sum((row_iota[:, None] >= row_ends[None, :]).astype(jnp.int32), axis=1)
        req_onehot = (row_req[:, None] == jnp.arange(req_count, dtype=jnp.int32)[None, :]).astype(
            jnp.int32
        )
        row_pos = row_iota + jnp.sum(req_onehot * (past_count - row_starts)[None, :], axis=1)
        local_table = lax.dynamic_index_in_dim(
            page_table.reshape(req_count, per_device, tp_count), tp_index, axis=2, keepdims=False
        )
        group_pages = lax.dynamic_index_in_dim(kv_cache, local, 0, keepdims=False)[0]
        page_row_block = group_pages[local_table.reshape(-1)]
        key_count_total = page_row_block.shape[0] * PAGE_POSITIONS
        flattened_cache = page_row_block.reshape(key_count_total, 2 * KEY_VALUE_HEADS * HEAD_SIZE)
        gathered_keys = flattened_cache[:, : KEY_VALUE_HEADS * HEAD_SIZE].reshape(
            key_count_total, KEY_VALUE_HEADS, HEAD_SIZE
        )
        gathered_values = flattened_cache[:, KEY_VALUE_HEADS * HEAD_SIZE :].reshape(
            key_count_total, KEY_VALUE_HEADS, HEAD_SIZE
        )
        key_iota = jnp.arange(key_count_total, dtype=jnp.int32)
        key_req = key_iota // (per_device * PAGE_POSITIONS)
        within = key_iota % (per_device * PAGE_POSITIONS)
        key_pos = (
            within // PAGE_POSITIONS * tp_count + tp_index
        ) * PAGE_POSITIONS + within % PAGE_POSITIONS
        allowed = (row_req[:, None] == key_req[None, :]) & (key_pos[None, :] <= row_pos[:, None])
        score_mask = allowed[:, None, :]
        outs = []
        for kv_head in range(KEY_VALUE_HEADS):
            head_rows = queries[:, kv_head * head_groups * HEAD_SIZE : (kv_head + 1) * head_groups * HEAD_SIZE]
            head_rows = head_rows.reshape(group_rows, head_groups, HEAD_SIZE)
            head_keys = flattened_cache[:, kv_head * HEAD_SIZE : (kv_head + 1) * HEAD_SIZE]
            head_values = flattened_cache[
                :, (KEY_VALUE_HEADS + kv_head) * HEAD_SIZE : (KEY_VALUE_HEADS + kv_head + 1) * HEAD_SIZE
            ]
            scores = jnp.einsum(
                "rgd,ld->rgl", head_rows, head_keys, preferred_element_type=jnp.float32
            ) * HEAD_SIZE ** (-0.5)
            masked = jnp.where(score_mask, scores, -1e30)
            top = jnp.max(masked, axis=-1)
            shift = jnp.where(top > -1e29, top, 0.0)
            soft = jnp.exp(masked - shift[..., None])
            total = jnp.sum(soft, axis=-1)
            weighted_part = jnp.einsum(
                "rgl,ld->rgd",
                soft.astype(jnp.bfloat16),
                head_values,
                preferred_element_type=jnp.float32,
            )
            outs.append((top, total, weighted_part))
        part_max = jnp.stack([o[0] for o in outs], axis=1)
        part_sum = jnp.stack([o[1] for o in outs], axis=1)
        part_weighted = jnp.stack([o[2] for o in outs], axis=1)
        return (part_max, part_sum, part_weighted)

    row_max, row_sum, weighted = lax.map(one_group, jnp.arange(local_groups, dtype=jnp.int32))
    row_max = row_max.reshape(count_of_rows, KEY_VALUE_HEADS, head_groups)
    row_sum = row_sum.reshape(count_of_rows, KEY_VALUE_HEADS, head_groups)
    weighted = weighted.reshape(count_of_rows, KEY_VALUE_HEADS, head_groups, HEAD_SIZE)
    row_max, row_sum, weighted = merged((row_max, row_sum, weighted), "tp", merge_parts)
    attended = (
        (weighted / row_sum[..., None])
        .reshape(count_of_rows, QUERY_HEADS * HEAD_SIZE)
        .astype(jnp.bfloat16)
    )
    resid = tokens.astype(jnp.float32) + jnp.dot(
        attended, out_weight, preferred_element_type=jnp.float32
    )
    mid_squares = tp_sum(jnp.sum(resid * resid, axis=1))
    normed = (resid * lax.rsqrt(mid_squares / full_width + EPSILON)[:, None] * norm_gain).astype(
        jnp.bfloat16
    )
    top_count = route_ids.shape[1]
    half_count = lax.axis_size("el")
    experts = half_count
    capacity = count_of_rows * top_count * 2 // experts
    buffer_len = experts * capacity
    flat_ids = route_ids.reshape(-1)
    expert_onehot = (flat_ids[:, None] == jnp.arange(experts, dtype=jnp.int32)[None, :]).astype(
        jnp.int32
    )
    assign_iota = jnp.arange(flat_ids.shape[0], dtype=jnp.int32)
    earlier = (assign_iota[None, :] < assign_iota[:, None]).astype(jnp.bfloat16)
    before = jnp.dot(
        earlier, expert_onehot.astype(jnp.bfloat16), preferred_element_type=jnp.float32
    ).astype(jnp.int32)
    expert_rank = jnp.sum(before * expert_onehot, axis=1)
    my_half = lax.axis_index("el")
    target = (relative(flat_ids, my_half, half_count) * capacity + expert_rank).reshape(
        count_of_rows, top_count
    )
    slot_iota = jnp.arange(buffer_len, dtype=jnp.int32)
    hits = target[None, :, :] == slot_iota[:, None, None]
    dispatch = jnp.any(hits, axis=2).astype(jnp.bfloat16)
    outgoing = jnp.dot(dispatch, normed, preferred_element_type=jnp.float32).astype(jnp.bfloat16)
    arrived = exchange(outgoing.reshape(experts, capacity, feat_part), half_count)
    flat_rows = lax.optimization_barrier(arrived.reshape(buffer_len, feat_part))
    group_rows = buffer_len // 2
    summed = jnp.concatenate(
        [
            expert_block(
                flat_rows[start : start + group_rows], gate_w[0], up_w[0], down_w[0]
            )
            for start in (0, group_rows)
        ],
        axis=0,
    )
    returned = exchange(summed.reshape(experts, capacity, feat_part), half_count).reshape(
        buffer_len, feat_part
    )
    combine = jnp.sum(
        jnp.where(
            target[:, :, None] == slot_iota[None, None, :],
            route_weights[:, :, None],
            0.0,
        ),
        axis=1,
    )
    branch = jnp.dot(
        combine,
        returned.astype(jnp.float32),
        precision=lax.Precision.HIGHEST,
        preferred_element_type=jnp.float32,
    )
    mixed_rows = resid + branch
    out_squares = tp_sum(jnp.sum(mixed_rows * mixed_rows, axis=1))
    return (
        mixed_rows * lax.rsqrt(out_squares / full_width + EPSILON)[:, None] * final_gain
    ).astype(jnp.bfloat16)


def solution(mesh):
    ep_count, tp_count = mesh.devices.shape
    halves = Mesh(mesh.devices.reshape(2, ep_count // 2, tp_count), ("eh", "el", "tp"))
    ep = ("eh", "el")
    placed = (
        P(ep, "tp"),
        P(ep, None),
        P(ep, "tp", None, None, None),
        P(ep, None),
        P(ep, None),
        P(ep, None),
        P(None, "tp"),
        P("tp"),
        P(ep, None),
        P(ep, None),
        P(ep, None, "tp"),
        P(ep, None, "tp"),
        P(ep, "tp", None),
        P("tp"),
    )
    inner = jax.shard_map(
        shards, mesh=halves, in_specs=placed, out_specs=P(ep, "tp"), check_vma=False
    )
    result_sharding = NamedSharding(mesh, P("ep", "tp"))

    def run(*args):
        return lax.with_sharding_constraint(inner(*args), result_sharding)

    return run
```

```python
import jax
import jax.numpy as jnp
from jax import lax
from jax.sharding import Mesh, NamedSharding, PartitionSpec as P

QUERY_HEADS = 12
KEY_VALUE_HEADS = 2
HEAD_SIZE = 128
PAGE_POSITIONS = 16


EPSILON = 1e-06


def merged(shard, axis, join):
    if lax.axis_size(axis) == 2:
        rounded = jax.tree.map(lambda a: a.astype(jnp.bfloat16), shard)
        swap = [(0, 1), (1, 0)]
        stats = lax.ppermute(jnp.stack(rounded[:2]), axis, perm=swap)
        other = (stats[0], stats[1], lax.ppermute(rounded[2], axis, perm=swap))
        widen = lambda tree: jax.tree.map(lambda a, own: a.astype(own.dtype), tree, shard)
        return join(widen(rounded), widen(other))
    gathered = jax.tree.map(
        lambda a, kind: lax.all_gather(a.astype(kind), axis),
        shard,
        (jnp.bfloat16, jnp.bfloat16, jnp.bfloat16),
    )

    def take(source):
        return jax.tree.map(
            lambda a, own: lax.dynamic_index_in_dim(a, source, 0, False).astype(own.dtype),
            gathered,
            shard,
        )

    return lax.fori_loop(
        1, lax.axis_size(axis), lambda source, state: join(state, take(source)), take(0)
    )


def relative(expert, me, count):
    if count & (count - 1) == 0:
        return jnp.bitwise_xor(expert, me)
    return (expert - me) % count


def exchange(chunks, count):
    pieces = [chunks[0]]
    for step in range(1, count):
        if count & (count - 1) == 0:
            pairs = [(i, i ^ step) for i in range(count)]
        else:
            pairs = [(i, (i + step) % count) for i in range(count)]
        pieces.append(lax.ppermute(chunks[step], "el", perm=pairs))
    return jnp.stack(pieces)


def expert_block(rows, gate_w, up_w, down_w):
    feat_part = rows.shape[1]
    if lax.axis_size("tp") != 2:
        inputs = lax.all_gather(rows, "tp", axis=1, tiled=True)
        gate_value = jnp.dot(inputs, gate_w, preferred_element_type=jnp.float32)
        up_value = jnp.dot(inputs, up_w, preferred_element_type=jnp.float32)
        hidden = (jnp.maximum(gate_value, 0.0) * up_value).astype(jnp.bfloat16)
        partial_value = jnp.dot(hidden, down_w, preferred_element_type=jnp.float32)
        return lax.psum_scatter(
            partial_value.astype(jnp.bfloat16), "tp", scatter_dimension=1, tiled=True
        )
    swap = [(0, 1), (1, 0)]
    mine = lax.axis_index("tp")
    other = 1 - mine
    rows_other = lax.ppermute(rows, "tp", perm=swap)
    gate_parts = gate_w.reshape(2, feat_part, gate_w.shape[1])
    up_parts = up_w.reshape(2, feat_part, up_w.shape[1])

    def half_product(parts, x, which):
        weight = lax.dynamic_index_in_dim(parts, which, 0, keepdims=False)
        return jnp.dot(x, weight, preferred_element_type=jnp.float32)

    gate_value = half_product(gate_parts, rows, mine) + half_product(gate_parts, rows_other, other)
    up_value = half_product(up_parts, rows, mine) + half_product(up_parts, rows_other, other)
    hidden = (jnp.maximum(gate_value, 0.0) * up_value).astype(jnp.bfloat16)

    def down_product(which):
        weight = lax.dynamic_slice_in_dim(down_w, which * feat_part, feat_part, axis=1)
        return jnp.dot(hidden, weight, preferred_element_type=jnp.float32).astype(jnp.bfloat16)

    sent = lax.ppermute(down_product(other), "tp", perm=swap)
    kept = lax.optimization_barrier(down_product(mine))
    return (kept.astype(jnp.float32) + sent.astype(jnp.float32)).astype(jnp.bfloat16)


def tp_sum(value):
    if lax.axis_size("tp") != 2:
        return lax.psum(value, "tp")
    return value + lax.ppermute(value, "tp", perm=[(0, 1), (1, 0)])


def tp_gather(part, axis):
    if lax.axis_size("tp") != 2:
        return lax.all_gather(part, "tp", axis=axis, tiled=True)
    other = lax.ppermute(part, "tp", perm=[(0, 1), (1, 0)])
    first = lax.axis_index("tp") == 0
    low = jnp.where(first, part, other)
    high = jnp.where(first, other, part)
    return jnp.concatenate([low, high], axis=axis)


def tp_scatter_sum(full, axis):
    if lax.axis_size("tp") != 2:
        return lax.psum_scatter(full, "tp", scatter_dimension=axis, tiled=True)
    low, high = jnp.split(full, 2, axis=axis)
    first = lax.axis_index("tp") == 0
    keep = jnp.where(first, low, high)
    send = jnp.where(first, high, low)
    other = lax.ppermute(send, "tp", perm=[(0, 1), (1, 0)])
    return (keep.astype(jnp.float32) + other.astype(jnp.float32)).astype(full.dtype)


def merge_parts(first, second):
    joint_max = jnp.maximum(first[0], second[0])
    scale_first = jnp.exp(first[0] - joint_max)
    scale_second = jnp.exp(second[0] - joint_max)
    return (
        joint_max,
        first[1] * scale_first + second[1] * scale_second,
        first[2] * scale_first[..., None] + second[2] * scale_second[..., None],
    )


def shards(
    tokens,
    queries,
    kv_cache,
    page_table,
    query_lens,
    past_lens,
    out_weight,
    norm_gain,
    route_ids,
    route_weights,
    gate_w,
    up_w,
    down_w,
    final_gain,
):
    tp_index = lax.axis_index("tp")
    tp_count = lax.axis_size("tp")
    count_of_rows, feat_part = tokens.shape
    full_width = feat_part * tp_count
    local_groups = query_lens.shape[0]
    req_count = query_lens.shape[1]
    group_rows = count_of_rows // local_groups
    head_groups = QUERY_HEADS // KEY_VALUE_HEADS
    per_device = page_table.shape[1] // tp_count

    def one_group(local):
        query_count = lax.dynamic_index_in_dim(query_lens, local, 0, keepdims=False)
        past_count = lax.dynamic_index_in_dim(past_lens, local, 0, keepdims=False)
        row_ends = jnp.cumsum(query_count)
        row_starts = row_ends - query_count
        row_iota = jnp.arange(group_rows, dtype=jnp.int32)
        row_req = jnp.sum((row_iota[:, None] >= row_ends[None, :]).astype(jnp.int32), axis=1)
        req_onehot = (row_req[:, None] == jnp.arange(req_count, dtype=jnp.int32)[None, :]).astype(
            jnp.int32
        )
        row_pos = row_iota + jnp.sum(req_onehot * (past_count - row_starts)[None, :], axis=1)
        local_table = lax.dynamic_index_in_dim(
            page_table.reshape(req_count, per_device, tp_count), tp_index, axis=2, keepdims=False
        )
        group_pages = lax.dynamic_index_in_dim(kv_cache, local, 0, keepdims=False)[0]
        page_row_block = group_pages[local_table.reshape(-1)]
        key_count_total = page_row_block.shape[0] * PAGE_POSITIONS
        flattened_cache = page_row_block.reshape(key_count_total, 2 * KEY_VALUE_HEADS * HEAD_SIZE)
        gathered_keys = flattened_cache[:, : KEY_VALUE_HEADS * HEAD_SIZE].reshape(
            key_count_total, KEY_VALUE_HEADS, HEAD_SIZE
        )
        gathered_values = flattened_cache[:, KEY_VALUE_HEADS * HEAD_SIZE :].reshape(
            key_count_total, KEY_VALUE_HEADS, HEAD_SIZE
        )
        key_iota = jnp.arange(key_count_total, dtype=jnp.int32)
        key_req = key_iota // (per_device * PAGE_POSITIONS)
        within = key_iota % (per_device * PAGE_POSITIONS)
        key_pos = (
            within // PAGE_POSITIONS * tp_count + tp_index
        ) * PAGE_POSITIONS + within % PAGE_POSITIONS
        allowed = (row_req[:, None] == key_req[None, :]) & (key_pos[None, :] <= row_pos[:, None])
        score_mask = allowed[:, None, :]
        outs = []
        for kv_head in range(KEY_VALUE_HEADS):
            head_rows = queries[:, kv_head * head_groups * HEAD_SIZE : (kv_head + 1) * head_groups * HEAD_SIZE]
            head_rows = head_rows.reshape(group_rows, head_groups, HEAD_SIZE)
            head_keys = flattened_cache[:, kv_head * HEAD_SIZE : (kv_head + 1) * HEAD_SIZE]
            head_values = flattened_cache[
                :, (KEY_VALUE_HEADS + kv_head) * HEAD_SIZE : (KEY_VALUE_HEADS + kv_head + 1) * HEAD_SIZE
            ]
            scores = jnp.einsum(
                "rgd,ld->rgl", head_rows, head_keys, preferred_element_type=jnp.float32
            ) * HEAD_SIZE ** (-0.5)
            top = jnp.max(jnp.where(score_mask, scores, -1e30), axis=-1)
            soft = jnp.where(score_mask, jnp.exp(scores - top[..., None]), 0.0)
            total = jnp.sum(soft, axis=-1)
            weighted_part = jnp.einsum(
                "rgl,ld->rgd",
                soft.astype(jnp.bfloat16),
                head_values,
                preferred_element_type=jnp.float32,
            )
            outs.append((top, total, weighted_part))
        part_max = jnp.stack([o[0] for o in outs], axis=1)
        part_sum = jnp.stack([o[1] for o in outs], axis=1)
        part_weighted = jnp.stack([o[2] for o in outs], axis=1)
        return (part_max, part_sum, part_weighted)

    row_max, row_sum, weighted = lax.map(one_group, jnp.arange(local_groups, dtype=jnp.int32))
    row_max = row_max.reshape(count_of_rows, KEY_VALUE_HEADS, head_groups)
    row_sum = row_sum.reshape(count_of_rows, KEY_VALUE_HEADS, head_groups)
    weighted = weighted.reshape(count_of_rows, KEY_VALUE_HEADS, head_groups, HEAD_SIZE)
    row_max, row_sum, weighted = merged((row_max, row_sum, weighted), "tp", merge_parts)
    attended = (
        (weighted / row_sum[..., None])
        .reshape(count_of_rows, QUERY_HEADS * HEAD_SIZE)
        .astype(jnp.bfloat16)
    )
    resid = tokens.astype(jnp.float32) + jnp.dot(
        attended, out_weight, preferred_element_type=jnp.float32
    )
    mid_squares = tp_sum(jnp.sum(resid * resid, axis=1))
    normed = (resid * lax.rsqrt(mid_squares / full_width + EPSILON)[:, None] * norm_gain).astype(
        jnp.bfloat16
    )
    top_count = route_ids.shape[1]
    half_count = lax.axis_size("el")
    experts = half_count
    capacity = count_of_rows * top_count * 2 // experts
    buffer_len = experts * capacity
    flat_ids = route_ids.reshape(-1)
    expert_onehot = (flat_ids[:, None] == jnp.arange(experts, dtype=jnp.int32)[None, :]).astype(
        jnp.int32
    )
    assign_iota = jnp.arange(flat_ids.shape[0], dtype=jnp.int32)
    earlier = (assign_iota[None, :] < assign_iota[:, None]).astype(jnp.bfloat16)
    before = jnp.dot(
        earlier, expert_onehot.astype(jnp.bfloat16), preferred_element_type=jnp.float32
    ).astype(jnp.int32)
    expert_rank = jnp.sum(before * expert_onehot, axis=1)
    my_half = lax.axis_index("el")
    target = (relative(flat_ids, my_half, half_count) * capacity + expert_rank).reshape(
        count_of_rows, top_count
    )
    slot_iota = jnp.arange(buffer_len, dtype=jnp.int32)
    hits = target[None, :, :] == slot_iota[:, None, None]
    dispatch = jnp.any(hits, axis=2).astype(jnp.bfloat16)
    outgoing = jnp.dot(dispatch, normed, preferred_element_type=jnp.float32).astype(jnp.bfloat16)
    arrived = exchange(outgoing.reshape(experts, capacity, feat_part), half_count)
    flat_rows = lax.optimization_barrier(arrived.reshape(buffer_len, feat_part))
    group_rows = buffer_len // 2
    summed = jnp.concatenate(
        [
            expert_block(
                flat_rows[start : start + group_rows], gate_w[0], up_w[0], down_w[0]
            )
            for start in (0, group_rows)
        ],
        axis=0,
    )
    returned = exchange(summed.reshape(experts, capacity, feat_part), half_count).reshape(
        buffer_len, feat_part
    )
    combine = jnp.sum(
        jnp.where(
            target[:, :, None] == slot_iota[None, None, :],
            route_weights[:, :, None],
            0.0,
        ),
        axis=1,
    )
    branch = jnp.dot(
        combine,
        returned.astype(jnp.float32),
        precision=lax.Precision.HIGHEST,
        preferred_element_type=jnp.float32,
    )
    mixed_rows = resid + branch
    out_squares = tp_sum(jnp.sum(mixed_rows * mixed_rows, axis=1))
    return (
        mixed_rows * lax.rsqrt(out_squares / full_width + EPSILON)[:, None] * final_gain
    ).astype(jnp.bfloat16)


def solution(mesh):
    ep_count, tp_count = mesh.devices.shape
    halves = Mesh(mesh.devices.reshape(2, ep_count // 2, tp_count), ("eh", "el", "tp"))
    ep = ("eh", "el")
    placed = (
        P(ep, "tp"),
        P(ep, None),
        P(ep, "tp", None, None, None),
        P(ep, None),
        P(ep, None),
        P(ep, None),
        P(None, "tp"),
        P("tp"),
        P(ep, None),
        P(ep, None),
        P(ep, None, "tp"),
        P(ep, None, "tp"),
        P(ep, "tp", None),
        P("tp"),
    )
    inner = jax.shard_map(
        shards, mesh=halves, in_specs=placed, out_specs=P(ep, "tp"), check_vma=False
    )
    result_sharding = NamedSharding(mesh, P("ep", "tp"))

    def run(*args):
        return lax.with_sharding_constraint(inner(*args), result_sharding)

    return run
```

```python
import jax
import jax.numpy as jnp
from jax import lax
from jax.sharding import Mesh, NamedSharding, PartitionSpec as P

QUERY_HEADS = 12
KEY_VALUE_HEADS = 2
HEAD_SIZE = 128
PAGE_POSITIONS = 16


EPSILON = 1e-06


def merged(shard, axis, join):
    if lax.axis_size(axis) == 2:
        rounded = jax.tree.map(lambda a: a.astype(jnp.bfloat16), shard)
        other = jax.tree.map(lambda a: lax.ppermute(a, axis, perm=[(0, 1), (1, 0)]), rounded)
        widen = lambda tree: jax.tree.map(lambda a, own: a.astype(own.dtype), tree, shard)
        return join(widen(rounded), widen(other))
    gathered = jax.tree.map(
        lambda a, kind: lax.all_gather(a.astype(kind), axis),
        shard,
        (jnp.bfloat16, jnp.bfloat16, jnp.bfloat16),
    )

    def take(source):
        return jax.tree.map(
            lambda a, own: lax.dynamic_index_in_dim(a, source, 0, False).astype(own.dtype),
            gathered,
            shard,
        )

    return lax.fori_loop(
        1, lax.axis_size(axis), lambda source, state: join(state, take(source)), take(0)
    )


def relative(expert, me, count):
    if count & (count - 1) == 0:
        return jnp.bitwise_xor(expert, me)
    return (expert - me) % count


def exchange(chunks, count):
    pieces = [chunks[0]]
    for step in range(1, count):
        if count & (count - 1) == 0:
            pairs = [(i, i ^ step) for i in range(count)]
        else:
            pairs = [(i, (i + step) % count) for i in range(count)]
        pieces.append(lax.ppermute(chunks[step], "el", perm=pairs))
    return jnp.stack(pieces)


def expert_block(rows, gate_w, up_w, down_w):
    feat_part = rows.shape[1]
    if lax.axis_size("tp") != 2:
        inputs = lax.all_gather(rows, "tp", axis=1, tiled=True)
        gate_value = jnp.dot(inputs, gate_w, preferred_element_type=jnp.float32)
        up_value = jnp.dot(inputs, up_w, preferred_element_type=jnp.float32)
        hidden = (jnp.maximum(gate_value, 0.0) * up_value).astype(jnp.bfloat16)
        partial_value = jnp.dot(hidden, down_w, preferred_element_type=jnp.float32)
        return lax.psum_scatter(
            partial_value.astype(jnp.bfloat16), "tp", scatter_dimension=1, tiled=True
        )
    swap = [(0, 1), (1, 0)]
    mine = lax.axis_index("tp")
    other = 1 - mine
    rows_other = lax.ppermute(rows, "tp", perm=swap)
    gate_parts = gate_w.reshape(2, feat_part, gate_w.shape[1])
    up_parts = up_w.reshape(2, feat_part, up_w.shape[1])

    def half_product(parts, x, which):
        weight = lax.dynamic_index_in_dim(parts, which, 0, keepdims=False)
        return jnp.dot(x, weight, preferred_element_type=jnp.float32)

    gate_value = half_product(gate_parts, rows, mine) + half_product(gate_parts, rows_other, other)
    up_value = half_product(up_parts, rows, mine) + half_product(up_parts, rows_other, other)
    hidden = (jnp.maximum(gate_value, 0.0) * up_value).astype(jnp.bfloat16)

    def down_product(which):
        weight = lax.dynamic_slice_in_dim(down_w, which * feat_part, feat_part, axis=1)
        return jnp.dot(hidden, weight, preferred_element_type=jnp.float32).astype(jnp.bfloat16)

    sent = lax.ppermute(down_product(other), "tp", perm=swap)
    kept = lax.optimization_barrier(down_product(mine))
    return (kept.astype(jnp.float32) + sent.astype(jnp.float32)).astype(jnp.bfloat16)


def tp_sum(value):
    if lax.axis_size("tp") != 2:
        return lax.psum(value, "tp")
    return value + lax.ppermute(value, "tp", perm=[(0, 1), (1, 0)])


def tp_gather(part, axis):
    if lax.axis_size("tp") != 2:
        return lax.all_gather(part, "tp", axis=axis, tiled=True)
    other = lax.ppermute(part, "tp", perm=[(0, 1), (1, 0)])
    first = lax.axis_index("tp") == 0
    low = jnp.where(first, part, other)
    high = jnp.where(first, other, part)
    return jnp.concatenate([low, high], axis=axis)


def tp_scatter_sum(full, axis):
    if lax.axis_size("tp") != 2:
        return lax.psum_scatter(full, "tp", scatter_dimension=axis, tiled=True)
    low, high = jnp.split(full, 2, axis=axis)
    first = lax.axis_index("tp") == 0
    keep = jnp.where(first, low, high)
    send = jnp.where(first, high, low)
    other = lax.ppermute(send, "tp", perm=[(0, 1), (1, 0)])
    return (keep.astype(jnp.float32) + other.astype(jnp.float32)).astype(full.dtype)


def merge_parts(first, second):
    joint_max = jnp.maximum(first[0], second[0])
    scale_first = jnp.exp(first[0] - joint_max)
    scale_second = jnp.exp(second[0] - joint_max)
    return (
        joint_max,
        first[1] * scale_first + second[1] * scale_second,
        first[2] * scale_first[..., None] + second[2] * scale_second[..., None],
    )


def shards(
    tokens,
    queries,
    kv_cache,
    page_table,
    query_lens,
    past_lens,
    out_weight,
    norm_gain,
    route_ids,
    route_weights,
    gate_w,
    up_w,
    down_w,
    final_gain,
):
    tp_index = lax.axis_index("tp")
    tp_count = lax.axis_size("tp")
    count_of_rows, feat_part = tokens.shape
    full_width = feat_part * tp_count
    local_groups = query_lens.shape[0]
    req_count = query_lens.shape[1]
    group_rows = count_of_rows // local_groups
    head_groups = QUERY_HEADS // KEY_VALUE_HEADS
    per_device = page_table.shape[1] // tp_count

    def one_group(local):
        query_count = lax.dynamic_index_in_dim(query_lens, local, 0, keepdims=False)
        past_count = lax.dynamic_index_in_dim(past_lens, local, 0, keepdims=False)
        row_ends = jnp.cumsum(query_count)
        row_starts = row_ends - query_count
        row_iota = jnp.arange(group_rows, dtype=jnp.int32)
        row_req = jnp.sum((row_iota[:, None] >= row_ends[None, :]).astype(jnp.int32), axis=1)
        req_onehot = (row_req[:, None] == jnp.arange(req_count, dtype=jnp.int32)[None, :]).astype(
            jnp.int32
        )
        row_pos = row_iota + jnp.sum(req_onehot * (past_count - row_starts)[None, :], axis=1)
        local_table = lax.dynamic_index_in_dim(
            page_table.reshape(req_count, per_device, tp_count), tp_index, axis=2, keepdims=False
        )
        group_pages = lax.dynamic_index_in_dim(kv_cache, local, 0, keepdims=False)[0]
        page_row_block = group_pages[local_table.reshape(-1)]
        key_count_total = page_row_block.shape[0] * PAGE_POSITIONS
        flattened_cache = page_row_block.reshape(key_count_total, 2 * KEY_VALUE_HEADS * HEAD_SIZE)
        gathered_keys = flattened_cache[:, : KEY_VALUE_HEADS * HEAD_SIZE].reshape(
            key_count_total, KEY_VALUE_HEADS, HEAD_SIZE
        )
        gathered_values = flattened_cache[:, KEY_VALUE_HEADS * HEAD_SIZE :].reshape(
            key_count_total, KEY_VALUE_HEADS, HEAD_SIZE
        )
        key_iota = jnp.arange(key_count_total, dtype=jnp.int32)
        key_req = key_iota // (per_device * PAGE_POSITIONS)
        within = key_iota % (per_device * PAGE_POSITIONS)
        key_pos = (
            within // PAGE_POSITIONS * tp_count + tp_index
        ) * PAGE_POSITIONS + within % PAGE_POSITIONS
        allowed = (row_req[:, None] == key_req[None, :]) & (key_pos[None, :] <= row_pos[:, None])
        score_mask = allowed[:, None, :]
        outs = []
        for kv_head in range(KEY_VALUE_HEADS):
            head_rows = queries.reshape(group_rows, QUERY_HEADS, HEAD_SIZE)[
                :, kv_head * head_groups : (kv_head + 1) * head_groups, :
            ]
            head_keys = flattened_cache[:, kv_head * HEAD_SIZE : (kv_head + 1) * HEAD_SIZE]
            head_values = flattened_cache[
                :, (KEY_VALUE_HEADS + kv_head) * HEAD_SIZE : (KEY_VALUE_HEADS + kv_head + 1) * HEAD_SIZE
            ]
            scores = jnp.einsum(
                "rgd,ld->rgl", head_rows, head_keys, preferred_element_type=jnp.float32
            ) * HEAD_SIZE ** (-0.5)
            top = jnp.max(jnp.where(score_mask, scores, -1e30), axis=-1)
            soft = jnp.where(score_mask, jnp.exp(scores - top[..., None]), 0.0)
            total = jnp.sum(soft, axis=-1)
            weighted_part = jnp.einsum(
                "rgl,ld->rgd",
                soft.astype(jnp.bfloat16),
                head_values,
                preferred_element_type=jnp.float32,
            )
            outs.append((top, total, weighted_part))
        part_max = jnp.stack([o[0] for o in outs], axis=1)
        part_sum = jnp.stack([o[1] for o in outs], axis=1)
        part_weighted = jnp.stack([o[2] for o in outs], axis=1)
        return (part_max, part_sum, part_weighted)

    row_max, row_sum, weighted = lax.map(one_group, jnp.arange(local_groups, dtype=jnp.int32))
    row_max = row_max.reshape(count_of_rows, KEY_VALUE_HEADS, head_groups)
    row_sum = row_sum.reshape(count_of_rows, KEY_VALUE_HEADS, head_groups)
    weighted = weighted.reshape(count_of_rows, KEY_VALUE_HEADS, head_groups, HEAD_SIZE)
    row_max, row_sum, weighted = merged((row_max, row_sum, weighted), "tp", merge_parts)
    attended = (
        (weighted / row_sum[..., None])
        .reshape(count_of_rows, QUERY_HEADS * HEAD_SIZE)
        .astype(jnp.bfloat16)
    )
    resid = tokens.astype(jnp.float32) + jnp.dot(
        attended, out_weight, preferred_element_type=jnp.float32
    )
    mid_squares = tp_sum(jnp.sum(resid * resid, axis=1))
    normed = (resid * lax.rsqrt(mid_squares / full_width + EPSILON)[:, None] * norm_gain).astype(
        jnp.bfloat16
    )
    top_count = route_ids.shape[1]
    half_count = lax.axis_size("el")
    experts = half_count
    capacity = count_of_rows * top_count * 2 // experts
    buffer_len = experts * capacity
    flat_ids = route_ids.reshape(-1)
    expert_onehot = (flat_ids[:, None] == jnp.arange(experts, dtype=jnp.int32)[None, :]).astype(
        jnp.int32
    )
    assign_iota = jnp.arange(flat_ids.shape[0], dtype=jnp.int32)
    earlier = (assign_iota[None, :] < assign_iota[:, None]).astype(jnp.bfloat16)
    before = jnp.dot(
        earlier, expert_onehot.astype(jnp.bfloat16), preferred_element_type=jnp.float32
    ).astype(jnp.int32)
    expert_rank = jnp.sum(before * expert_onehot, axis=1)
    my_half = lax.axis_index("el")
    target = (relative(flat_ids, my_half, half_count) * capacity + expert_rank).reshape(
        count_of_rows, top_count
    )
    slot_iota = jnp.arange(buffer_len, dtype=jnp.int32)
    hits = target[None, :, :] == slot_iota[:, None, None]
    dispatch = jnp.any(hits, axis=2).astype(jnp.bfloat16)
    outgoing = jnp.dot(dispatch, normed, preferred_element_type=jnp.float32).astype(jnp.bfloat16)
    arrived = exchange(outgoing.reshape(experts, capacity, feat_part), half_count)
    flat_rows = lax.optimization_barrier(arrived.reshape(buffer_len, feat_part))
    group_rows = buffer_len // 2
    summed = jnp.concatenate(
        [
            expert_block(
                flat_rows[start : start + group_rows], gate_w[0], up_w[0], down_w[0]
            )
            for start in (0, group_rows)
        ],
        axis=0,
    )
    returned = exchange(summed.reshape(experts, capacity, feat_part), half_count).reshape(
        buffer_len, feat_part
    )
    combine = jnp.sum(
        jnp.where(
            target[:, :, None] == slot_iota[None, None, :],
            route_weights[:, :, None],
            0.0,
        ),
        axis=1,
    )
    branch = jnp.dot(
        combine,
        returned.astype(jnp.float32),
        precision=lax.Precision.HIGHEST,
        preferred_element_type=jnp.float32,
    )
    mixed_rows = resid + branch
    out_squares = tp_sum(jnp.sum(mixed_rows * mixed_rows, axis=1))
    return (
        mixed_rows * lax.rsqrt(out_squares / full_width + EPSILON)[:, None] * final_gain
    ).astype(jnp.bfloat16)


def solution(mesh):
    ep_count, tp_count = mesh.devices.shape
    halves = Mesh(mesh.devices.reshape(2, ep_count // 2, tp_count), ("eh", "el", "tp"))
    ep = ("eh", "el")
    placed = (
        P(ep, "tp"),
        P(ep, None),
        P(ep, "tp", None, None, None),
        P(ep, None),
        P(ep, None),
        P(ep, None),
        P(None, "tp"),
        P("tp"),
        P(ep, None),
        P(ep, None),
        P(ep, None, "tp"),
        P(ep, None, "tp"),
        P(ep, "tp", None),
        P("tp"),
    )
    inner = jax.shard_map(
        shards, mesh=halves, in_specs=placed, out_specs=P(ep, "tp"), check_vma=False
    )
    result_sharding = NamedSharding(mesh, P("ep", "tp"))

    def run(*args):
        return lax.with_sharding_constraint(inner(*args), result_sharding)

    return run
```

```python
import jax
import jax.numpy as jnp
from jax import lax
from jax.sharding import Mesh, NamedSharding, PartitionSpec as P

QUERY_HEADS = 12
KEY_VALUE_HEADS = 2
HEAD_SIZE = 128
PAGE_POSITIONS = 16


EPSILON = 1e-06


def merged(shard, axis, join):
    if lax.axis_size(axis) == 2:
        rounded = jax.tree.map(lambda a: a.astype(jnp.bfloat16), shard)
        swap = [(0, 1), (1, 0)]
        stats = lax.ppermute(jnp.stack(rounded[:2]), axis, perm=swap)
        other = (stats[0], stats[1], lax.ppermute(rounded[2], axis, perm=swap))
        widen = lambda tree: jax.tree.map(lambda a, own: a.astype(own.dtype), tree, shard)
        return join(widen(rounded), widen(other))
    gathered = jax.tree.map(
        lambda a, kind: lax.all_gather(a.astype(kind), axis),
        shard,
        (jnp.bfloat16, jnp.bfloat16, jnp.bfloat16),
    )

    def take(source):
        return jax.tree.map(
            lambda a, own: lax.dynamic_index_in_dim(a, source, 0, False).astype(own.dtype),
            gathered,
            shard,
        )

    return lax.fori_loop(
        1, lax.axis_size(axis), lambda source, state: join(state, take(source)), take(0)
    )


def relative(expert, me, count):
    if count & (count - 1) == 0:
        return jnp.bitwise_xor(expert, me)
    return (expert - me) % count


def exchange(chunks, count):
    pieces = [chunks[0]]
    for step in range(1, count):
        if count & (count - 1) == 0:
            pairs = [(i, i ^ step) for i in range(count)]
        else:
            pairs = [(i, (i + step) % count) for i in range(count)]
        pieces.append(lax.ppermute(chunks[step], "el", perm=pairs))
    return jnp.stack(pieces)


def expert_block(rows, gate_w, up_w, down_w):
    feat_part = rows.shape[1]
    if lax.axis_size("tp") != 2:
        inputs = lax.all_gather(rows, "tp", axis=1, tiled=True)
        gate_value = jnp.dot(inputs, gate_w, preferred_element_type=jnp.float32)
        up_value = jnp.dot(inputs, up_w, preferred_element_type=jnp.float32)
        hidden = (jnp.maximum(gate_value, 0.0) * up_value).astype(jnp.bfloat16)
        partial_value = jnp.dot(hidden, down_w, preferred_element_type=jnp.float32)
        return lax.psum_scatter(
            partial_value.astype(jnp.bfloat16), "tp", scatter_dimension=1, tiled=True
        )
    swap = [(0, 1), (1, 0)]
    mine = lax.axis_index("tp")
    other = 1 - mine
    rows_other = lax.ppermute(rows, "tp", perm=swap)
    gate_parts = gate_w.reshape(2, feat_part, gate_w.shape[1])
    up_parts = up_w.reshape(2, feat_part, up_w.shape[1])

    def half_product(parts, x, which):
        weight = lax.dynamic_index_in_dim(parts, which, 0, keepdims=False)
        return jnp.dot(x, weight, preferred_element_type=jnp.float32)

    gate_value = half_product(gate_parts, rows, mine) + half_product(gate_parts, rows_other, other)
    up_value = half_product(up_parts, rows, mine) + half_product(up_parts, rows_other, other)
    hidden = (jnp.maximum(gate_value, 0.0) * up_value).astype(jnp.bfloat16)

    def down_product(which):
        weight = lax.dynamic_slice_in_dim(down_w, which * feat_part, feat_part, axis=1)
        return jnp.dot(hidden, weight, preferred_element_type=jnp.float32).astype(jnp.bfloat16)

    sent = lax.ppermute(down_product(other), "tp", perm=swap)
    kept = lax.optimization_barrier(down_product(mine))
    return (kept.astype(jnp.float32) + sent.astype(jnp.float32)).astype(jnp.bfloat16)


def tp_sum(value):
    if lax.axis_size("tp") != 2:
        return lax.psum(value, "tp")
    return value + lax.ppermute(value, "tp", perm=[(0, 1), (1, 0)])


def tp_gather(part, axis):
    if lax.axis_size("tp") != 2:
        return lax.all_gather(part, "tp", axis=axis, tiled=True)
    other = lax.ppermute(part, "tp", perm=[(0, 1), (1, 0)])
    first = lax.axis_index("tp") == 0
    low = jnp.where(first, part, other)
    high = jnp.where(first, other, part)
    return jnp.concatenate([low, high], axis=axis)


def tp_scatter_sum(full, axis):
    if lax.axis_size("tp") != 2:
        return lax.psum_scatter(full, "tp", scatter_dimension=axis, tiled=True)
    low, high = jnp.split(full, 2, axis=axis)
    first = lax.axis_index("tp") == 0
    keep = jnp.where(first, low, high)
    send = jnp.where(first, high, low)
    other = lax.ppermute(send, "tp", perm=[(0, 1), (1, 0)])
    return (keep.astype(jnp.float32) + other.astype(jnp.float32)).astype(full.dtype)


def merge_parts(first, second):
    joint_max = jnp.maximum(first[0], second[0])
    scale_first = jnp.exp(first[0] - joint_max)
    scale_second = jnp.exp(second[0] - joint_max)
    return (
        joint_max,
        first[1] * scale_first + second[1] * scale_second,
        first[2] * scale_first[..., None] + second[2] * scale_second[..., None],
    )


def shards(
    tokens,
    queries,
    kv_cache,
    page_table,
    query_lens,
    past_lens,
    out_weight,
    norm_gain,
    route_ids,
    route_weights,
    gate_w,
    up_w,
    down_w,
    final_gain,
):
    tp_index = lax.axis_index("tp")
    tp_count = lax.axis_size("tp")
    count_of_rows, feat_part = tokens.shape
    full_width = feat_part * tp_count
    local_groups = query_lens.shape[0]
    req_count = query_lens.shape[1]
    group_rows = count_of_rows // local_groups
    head_groups = QUERY_HEADS // KEY_VALUE_HEADS
    per_device = page_table.shape[1] // tp_count

    def one_group(local):
        query_count = lax.dynamic_index_in_dim(query_lens, local, 0, keepdims=False)
        past_count = lax.dynamic_index_in_dim(past_lens, local, 0, keepdims=False)
        req_iota = jnp.arange(req_count, dtype=jnp.int32)
        row_ends = jnp.sum(
            jnp.where(req_iota[None, :] <= req_iota[:, None], query_count[None, :], 0), axis=1
        )
        row_starts = row_ends - query_count
        row_iota = jnp.arange(group_rows, dtype=jnp.int32)
        row_req = jnp.sum((row_iota[:, None] >= row_ends[None, :]).astype(jnp.int32), axis=1)
        req_onehot = (row_req[:, None] == jnp.arange(req_count, dtype=jnp.int32)[None, :]).astype(
            jnp.int32
        )
        row_pos = row_iota + jnp.sum(req_onehot * (past_count - row_starts)[None, :], axis=1)
        local_table = page_table[:, 0::tp_count]
        for other in range(1, tp_count):
            local_table = jnp.where(tp_index == other, page_table[:, other::tp_count], local_table)
        group_pages = lax.dynamic_index_in_dim(kv_cache, local, 0, keepdims=False)[0]
        page_row_block = group_pages[local_table.reshape(-1)]
        key_count_total = page_row_block.shape[0] * PAGE_POSITIONS
        flattened_cache = page_row_block.reshape(key_count_total, 2 * KEY_VALUE_HEADS * HEAD_SIZE)
        gathered_keys = flattened_cache[:, : KEY_VALUE_HEADS * HEAD_SIZE].reshape(
            key_count_total, KEY_VALUE_HEADS, HEAD_SIZE
        )
        gathered_values = flattened_cache[:, KEY_VALUE_HEADS * HEAD_SIZE :].reshape(
            key_count_total, KEY_VALUE_HEADS, HEAD_SIZE
        )
        key_iota = jnp.arange(key_count_total, dtype=jnp.int32)
        key_req = key_iota // (per_device * PAGE_POSITIONS)
        within = key_iota % (per_device * PAGE_POSITIONS)
        key_pos = (
            within // PAGE_POSITIONS * tp_count + tp_index
        ) * PAGE_POSITIONS + within % PAGE_POSITIONS
        allowed = (row_req[:, None] == key_req[None, :]) & (key_pos[None, :] <= row_pos[:, None])
        score_mask = allowed[:, None, :]
        outs = []
        for kv_head in range(KEY_VALUE_HEADS):
            head_rows = queries[:, kv_head * head_groups * HEAD_SIZE : (kv_head + 1) * head_groups * HEAD_SIZE]
            head_rows = head_rows.reshape(group_rows, head_groups, HEAD_SIZE)
            head_keys = flattened_cache[:, kv_head * HEAD_SIZE : (kv_head + 1) * HEAD_SIZE]
            head_values = flattened_cache[
                :, (KEY_VALUE_HEADS + kv_head) * HEAD_SIZE : (KEY_VALUE_HEADS + kv_head + 1) * HEAD_SIZE
            ]
            scores = jnp.einsum(
                "rgd,ld->rgl", head_rows, head_keys, preferred_element_type=jnp.float32
            ) * HEAD_SIZE ** (-0.5)
            top = jnp.max(jnp.where(score_mask, scores, -1e30), axis=-1)
            soft = jnp.where(score_mask, jnp.exp(scores - top[..., None]), 0.0)
            total = jnp.sum(soft, axis=-1)
            weighted_part = jnp.einsum(
                "rgl,ld->rgd",
                soft.astype(jnp.bfloat16),
                head_values,
                preferred_element_type=jnp.float32,
            )
            outs.append((top, total, weighted_part))
        part_max = jnp.stack([o[0] for o in outs], axis=1)
        part_sum = jnp.stack([o[1] for o in outs], axis=1)
        part_weighted = jnp.stack([o[2] for o in outs], axis=1)
        return (part_max, part_sum, part_weighted)

    row_max, row_sum, weighted = lax.map(one_group, jnp.arange(local_groups, dtype=jnp.int32))
    row_max = row_max.reshape(count_of_rows, KEY_VALUE_HEADS, head_groups)
    row_sum = row_sum.reshape(count_of_rows, KEY_VALUE_HEADS, head_groups)
    weighted = weighted.reshape(count_of_rows, KEY_VALUE_HEADS, head_groups, HEAD_SIZE)
    row_max, row_sum, weighted = merged((row_max, row_sum, weighted), "tp", merge_parts)
    attended = (
        (weighted / row_sum[..., None])
        .reshape(count_of_rows, QUERY_HEADS * HEAD_SIZE)
        .astype(jnp.bfloat16)
    )
    resid = tokens.astype(jnp.float32) + jnp.dot(
        attended, out_weight, preferred_element_type=jnp.float32
    )
    mid_squares = tp_sum(jnp.sum(resid * resid, axis=1))
    normed = (resid * lax.rsqrt(mid_squares / full_width + EPSILON)[:, None] * norm_gain).astype(
        jnp.bfloat16
    )
    top_count = route_ids.shape[1]
    half_count = lax.axis_size("el")
    experts = half_count
    capacity = count_of_rows * top_count * 2 // experts
    buffer_len = experts * capacity
    flat_ids = route_ids.reshape(-1)
    expert_onehot = (flat_ids[:, None] == jnp.arange(experts, dtype=jnp.int32)[None, :]).astype(
        jnp.int32
    )
    assign_iota = jnp.arange(flat_ids.shape[0], dtype=jnp.int32)
    earlier = (assign_iota[None, :] < assign_iota[:, None]).astype(jnp.bfloat16)
    before = jnp.dot(
        earlier, expert_onehot.astype(jnp.bfloat16), preferred_element_type=jnp.float32
    ).astype(jnp.int32)
    expert_rank = jnp.sum(before * expert_onehot, axis=1)
    my_half = lax.axis_index("el")
    target = (relative(flat_ids, my_half, half_count) * capacity + expert_rank).reshape(
        count_of_rows, top_count
    )
    slot_iota = jnp.arange(buffer_len, dtype=jnp.int32)
    hits = target[None, :, :] == slot_iota[:, None, None]
    dispatch = jnp.any(hits, axis=2).astype(jnp.bfloat16)
    outgoing = jnp.dot(dispatch, normed, preferred_element_type=jnp.float32).astype(jnp.bfloat16)
    arrived = exchange(outgoing.reshape(experts, capacity, feat_part), half_count)
    flat_rows = lax.optimization_barrier(arrived.reshape(buffer_len, feat_part))
    group_rows = buffer_len // 2
    summed = jnp.concatenate(
        [
            expert_block(
                flat_rows[start : start + group_rows], gate_w[0], up_w[0], down_w[0]
            )
            for start in (0, group_rows)
        ],
        axis=0,
    )
    returned = exchange(summed.reshape(experts, capacity, feat_part), half_count).reshape(
        buffer_len, feat_part
    )
    combine = jnp.sum(
        jnp.where(
            target[:, :, None] == slot_iota[None, None, :],
            route_weights[:, :, None],
            0.0,
        ),
        axis=1,
    )
    branch = jnp.dot(
        combine,
        returned.astype(jnp.float32),
        precision=lax.Precision.HIGHEST,
        preferred_element_type=jnp.float32,
    )
    mixed_rows = resid + branch
    out_squares = tp_sum(jnp.sum(mixed_rows * mixed_rows, axis=1))
    return (
        mixed_rows * lax.rsqrt(out_squares / full_width + EPSILON)[:, None] * final_gain
    ).astype(jnp.bfloat16)


def solution(mesh):
    ep_count, tp_count = mesh.devices.shape
    halves = Mesh(mesh.devices.reshape(2, ep_count // 2, tp_count), ("eh", "el", "tp"))
    ep = ("eh", "el")
    placed = (
        P(ep, "tp"),
        P(ep, None),
        P(ep, "tp", None, None, None),
        P(ep, None),
        P(ep, None),
        P(ep, None),
        P(None, "tp"),
        P("tp"),
        P(ep, None),
        P(ep, None),
        P(ep, None, "tp"),
        P(ep, None, "tp"),
        P(ep, "tp", None),
        P("tp"),
    )
    inner = jax.shard_map(
        shards, mesh=halves, in_specs=placed, out_specs=P(ep, "tp"), check_vma=False
    )
    result_sharding = NamedSharding(mesh, P("ep", "tp"))

    def run(*args):
        return lax.with_sharding_constraint(inner(*args), result_sharding)

    return run
```

```python
import jax
import jax.numpy as jnp
from jax import lax
from jax.sharding import Mesh, NamedSharding, PartitionSpec as P

QUERY_HEADS = 12
KEY_VALUE_HEADS = 2
HEAD_SIZE = 128
PAGE_POSITIONS = 16


EPSILON = 1e-06


def merged(shard, axis, join):
    if lax.axis_size(axis) == 2:
        rounded = jax.tree.map(lambda a: a.astype(jnp.bfloat16), shard)
        swap = [(0, 1), (1, 0)]
        stats = lax.ppermute(jnp.stack(rounded[:2]), axis, perm=swap)
        other = (stats[0], stats[1], lax.ppermute(rounded[2], axis, perm=swap))
        widen = lambda tree: jax.tree.map(lambda a, own: a.astype(own.dtype), tree, shard)
        return join(widen(rounded), widen(other))
    gathered = jax.tree.map(
        lambda a, kind: lax.all_gather(a.astype(kind), axis),
        shard,
        (jnp.bfloat16, jnp.bfloat16, jnp.bfloat16),
    )

    def take(source):
        return jax.tree.map(
            lambda a, own: lax.dynamic_index_in_dim(a, source, 0, False).astype(own.dtype),
            gathered,
            shard,
        )

    return lax.fori_loop(
        1, lax.axis_size(axis), lambda source, state: join(state, take(source)), take(0)
    )


def relative(expert, me, count):
    if count & (count - 1) == 0:
        return jnp.bitwise_xor(expert, me)
    return (expert - me) % count


def exchange(chunks, count):
    pieces = [chunks[0]]
    for step in range(1, count):
        if count & (count - 1) == 0:
            pairs = [(i, i ^ step) for i in range(count)]
        else:
            pairs = [(i, (i + step) % count) for i in range(count)]
        pieces.append(lax.ppermute(chunks[step], "el", perm=pairs))
    return jnp.stack(pieces)


def expert_block(rows, gate_w, up_w, down_w):
    feat_part = rows.shape[1]
    if lax.axis_size("tp") != 2:
        inputs = lax.all_gather(rows, "tp", axis=1, tiled=True)
        gate_value = jnp.dot(inputs, gate_w, preferred_element_type=jnp.float32)
        up_value = jnp.dot(inputs, up_w, preferred_element_type=jnp.float32)
        hidden = (jnp.maximum(gate_value, 0.0) * up_value).astype(jnp.bfloat16)
        partial_value = jnp.dot(hidden, down_w, preferred_element_type=jnp.float32)
        return lax.psum_scatter(
            partial_value.astype(jnp.bfloat16), "tp", scatter_dimension=1, tiled=True
        )
    swap = [(0, 1), (1, 0)]
    mine = lax.axis_index("tp")
    other = 1 - mine
    rows_other = lax.ppermute(rows, "tp", perm=swap)
    gate_parts = gate_w.reshape(2, feat_part, gate_w.shape[1])
    up_parts = up_w.reshape(2, feat_part, up_w.shape[1])

    def half_product(parts, x, which):
        weight = lax.dynamic_index_in_dim(parts, which, 0, keepdims=False)
        return jnp.dot(x, weight, preferred_element_type=jnp.float32)

    gate_value = half_product(gate_parts, rows, mine) + half_product(gate_parts, rows_other, other)
    up_value = half_product(up_parts, rows, mine) + half_product(up_parts, rows_other, other)
    hidden = (jnp.maximum(gate_value, 0.0) * up_value).astype(jnp.bfloat16)

    def down_product(which):
        weight = lax.dynamic_slice_in_dim(down_w, which * feat_part, feat_part, axis=1)
        return jnp.dot(hidden, weight, preferred_element_type=jnp.float32).astype(jnp.bfloat16)

    sent = lax.ppermute(down_product(other), "tp", perm=swap)
    kept = lax.optimization_barrier(down_product(mine))
    return (kept.astype(jnp.float32) + sent.astype(jnp.float32)).astype(jnp.bfloat16)


def tp_sum(value):
    if lax.axis_size("tp") != 2:
        return lax.psum(value, "tp")
    return value + lax.ppermute(value, "tp", perm=[(0, 1), (1, 0)])


def tp_gather(part, axis):
    if lax.axis_size("tp") != 2:
        return lax.all_gather(part, "tp", axis=axis, tiled=True)
    other = lax.ppermute(part, "tp", perm=[(0, 1), (1, 0)])
    first = lax.axis_index("tp") == 0
    low = jnp.where(first, part, other)
    high = jnp.where(first, other, part)
    return jnp.concatenate([low, high], axis=axis)


def tp_scatter_sum(full, axis):
    if lax.axis_size("tp") != 2:
        return lax.psum_scatter(full, "tp", scatter_dimension=axis, tiled=True)
    low, high = jnp.split(full, 2, axis=axis)
    first = lax.axis_index("tp") == 0
    keep = jnp.where(first, low, high)
    send = jnp.where(first, high, low)
    other = lax.ppermute(send, "tp", perm=[(0, 1), (1, 0)])
    return (keep.astype(jnp.float32) + other.astype(jnp.float32)).astype(full.dtype)


def merge_parts(first, second):
    joint_max = jnp.maximum(first[0], second[0])
    scale_first = jnp.exp(first[0] - joint_max)
    scale_second = jnp.exp(second[0] - joint_max)
    return (
        joint_max,
        first[1] * scale_first + second[1] * scale_second,
        first[2] * scale_first[..., None] + second[2] * scale_second[..., None],
    )


def shards(
    tokens,
    queries,
    kv_cache,
    page_table,
    query_lens,
    past_lens,
    out_weight,
    norm_gain,
    route_ids,
    route_weights,
    gate_w,
    up_w,
    down_w,
    final_gain,
):
    tp_index = lax.axis_index("tp")
    tp_count = lax.axis_size("tp")
    count_of_rows, feat_part = tokens.shape
    full_width = feat_part * tp_count
    local_groups = query_lens.shape[0]
    req_count = query_lens.shape[1]
    group_rows = count_of_rows // local_groups
    head_groups = QUERY_HEADS // KEY_VALUE_HEADS
    per_device = page_table.shape[1] // tp_count

    def one_group(local):
        query_count = lax.dynamic_index_in_dim(query_lens, local, 0, keepdims=False)
        past_count = lax.dynamic_index_in_dim(past_lens, local, 0, keepdims=False)
        row_ends = jnp.cumsum(query_count)
        row_starts = row_ends - query_count
        row_iota = jnp.arange(group_rows, dtype=jnp.int32)
        row_req = jnp.sum((row_iota[:, None] >= row_ends[None, :]).astype(jnp.int32), axis=1)
        req_onehot = (row_req[:, None] == jnp.arange(req_count, dtype=jnp.int32)[None, :]).astype(
            jnp.int32
        )
        row_pos = row_iota + jnp.sum(req_onehot * (past_count - row_starts)[None, :], axis=1)
        local_table = lax.dynamic_index_in_dim(
            page_table.reshape(req_count, per_device, tp_count), tp_index, axis=2, keepdims=False
        )
        group_pages = lax.dynamic_index_in_dim(kv_cache, local, 0, keepdims=False)[0]
        page_row_block = group_pages[local_table.reshape(-1)]
        key_count_total = page_row_block.shape[0] * PAGE_POSITIONS
        flattened_cache = page_row_block.reshape(key_count_total, 2 * KEY_VALUE_HEADS * HEAD_SIZE)
        gathered_keys = flattened_cache[:, : KEY_VALUE_HEADS * HEAD_SIZE].reshape(
            key_count_total, KEY_VALUE_HEADS, HEAD_SIZE
        )
        gathered_values = flattened_cache[:, KEY_VALUE_HEADS * HEAD_SIZE :].reshape(
            key_count_total, KEY_VALUE_HEADS, HEAD_SIZE
        )
        key_iota = jnp.arange(key_count_total, dtype=jnp.int32)
        key_req = key_iota // (per_device * PAGE_POSITIONS)
        within = key_iota % (per_device * PAGE_POSITIONS)
        key_pos = (
            within // PAGE_POSITIONS * tp_count + tp_index
        ) * PAGE_POSITIONS + within % PAGE_POSITIONS
        allowed = (row_req[:, None] == key_req[None, :]) & (key_pos[None, :] <= row_pos[:, None])
        score_mask = allowed[:, None, :]
        outs = []
        for kv_head in range(KEY_VALUE_HEADS):
            head_rows = queries.reshape(group_rows, QUERY_HEADS, HEAD_SIZE)[
                :, kv_head * head_groups : (kv_head + 1) * head_groups, :
            ]
            head_keys = flattened_cache[:, kv_head * HEAD_SIZE : (kv_head + 1) * HEAD_SIZE]
            head_values = flattened_cache[
                :, (KEY_VALUE_HEADS + kv_head) * HEAD_SIZE : (KEY_VALUE_HEADS + kv_head + 1) * HEAD_SIZE
            ]
            scores = jnp.einsum(
                "rgd,ld->rgl", head_rows, head_keys, preferred_element_type=jnp.float32
            ) * HEAD_SIZE ** (-0.5)
            top = jnp.max(jnp.where(score_mask, scores, -1e30), axis=-1)
            soft = jnp.where(score_mask, jnp.exp(scores - top[..., None]), 0.0)
            total = jnp.sum(soft, axis=-1)
            weighted_part = jnp.einsum(
                "rgl,ld->rgd",
                soft.astype(jnp.bfloat16),
                head_values,
                preferred_element_type=jnp.float32,
            )
            outs.append((top, total, weighted_part))
        part_max = jnp.stack([o[0] for o in outs], axis=1)
        part_sum = jnp.stack([o[1] for o in outs], axis=1)
        part_weighted = jnp.stack([o[2] for o in outs], axis=1)
        return (part_max, part_sum, part_weighted)

    row_max, row_sum, weighted = lax.map(one_group, jnp.arange(local_groups, dtype=jnp.int32))
    row_max = row_max.reshape(count_of_rows, KEY_VALUE_HEADS, head_groups)
    row_sum = row_sum.reshape(count_of_rows, KEY_VALUE_HEADS, head_groups)
    weighted = weighted.reshape(count_of_rows, KEY_VALUE_HEADS, head_groups, HEAD_SIZE)
    row_max, row_sum, weighted = merged((row_max, row_sum, weighted), "tp", merge_parts)
    attended = (
        (weighted / row_sum[..., None])
        .reshape(count_of_rows, QUERY_HEADS * HEAD_SIZE)
        .astype(jnp.bfloat16)
    )
    resid = tokens.astype(jnp.float32) + jnp.dot(
        attended, out_weight, preferred_element_type=jnp.float32
    )
    mid_squares = tp_sum(jnp.sum(resid * resid, axis=1))
    normed = (resid * lax.rsqrt(mid_squares / full_width + EPSILON)[:, None] * norm_gain).astype(
        jnp.bfloat16
    )
    top_count = route_ids.shape[1]
    half_count = lax.axis_size("el")
    experts = half_count
    capacity = count_of_rows * top_count * 2 // experts
    buffer_len = experts * capacity
    flat_ids = route_ids.reshape(-1)
    expert_onehot = (flat_ids[:, None] == jnp.arange(experts, dtype=jnp.int32)[None, :]).astype(
        jnp.int32
    )
    assign_iota = jnp.arange(flat_ids.shape[0], dtype=jnp.int32)
    earlier = (assign_iota[None, :] < assign_iota[:, None]).astype(jnp.bfloat16)
    before = jnp.dot(
        earlier, expert_onehot.astype(jnp.bfloat16), preferred_element_type=jnp.float32
    ).astype(jnp.int32)
    expert_rank = jnp.sum(before * expert_onehot, axis=1)
    my_half = lax.axis_index("el")
    target = (relative(flat_ids, my_half, half_count) * capacity + expert_rank).reshape(
        count_of_rows, top_count
    )
    slot_iota = jnp.arange(buffer_len, dtype=jnp.int32)
    hits = target[None, :, :] == slot_iota[:, None, None]
    dispatch = jnp.any(hits, axis=2).astype(jnp.bfloat16)
    outgoing = jnp.dot(dispatch, normed, preferred_element_type=jnp.float32).astype(jnp.bfloat16)
    arrived = exchange(outgoing.reshape(experts, capacity, feat_part), half_count)
    flat_rows = lax.optimization_barrier(arrived.reshape(buffer_len, feat_part))
    group_rows = buffer_len // 2
    summed = jnp.concatenate(
        [
            expert_block(
                flat_rows[start : start + group_rows], gate_w[0], up_w[0], down_w[0]
            )
            for start in (0, group_rows)
        ],
        axis=0,
    )
    returned = exchange(summed.reshape(experts, capacity, feat_part), half_count).reshape(
        buffer_len, feat_part
    )
    combine = jnp.sum(
        jnp.where(
            target[:, :, None] == slot_iota[None, None, :],
            route_weights[:, :, None],
            0.0,
        ),
        axis=1,
    )
    branch = jnp.dot(
        combine,
        returned.astype(jnp.float32),
        precision=lax.Precision.HIGHEST,
        preferred_element_type=jnp.float32,
    )
    mixed_rows = resid + branch
    out_squares = tp_sum(jnp.sum(mixed_rows * mixed_rows, axis=1))
    return (
        mixed_rows * lax.rsqrt(out_squares / full_width + EPSILON)[:, None] * final_gain
    ).astype(jnp.bfloat16)


def solution(mesh):
    ep_count, tp_count = mesh.devices.shape
    halves = Mesh(mesh.devices.reshape(2, ep_count // 2, tp_count), ("eh", "el", "tp"))
    ep = ("eh", "el")
    placed = (
        P(ep, "tp"),
        P(ep, None),
        P(ep, "tp", None, None, None),
        P(ep, None),
        P(ep, None),
        P(ep, None),
        P(None, "tp"),
        P("tp"),
        P(ep, None),
        P(ep, None),
        P(ep, None, "tp"),
        P(ep, None, "tp"),
        P(ep, "tp", None),
        P("tp"),
    )
    inner = jax.shard_map(
        shards, mesh=halves, in_specs=placed, out_specs=P(ep, "tp"), check_vma=False
    )
    result_sharding = NamedSharding(mesh, P("ep", "tp"))

    def run(*args):
        return lax.with_sharding_constraint(inner(*args), result_sharding)

    return run
```
